256 devices in a mesh: dp: 16 (over y_lo, z), tm: 16 (over x, y_hi, core).
Axes of the slice: x: 4, y: 4 (y_hi: 2, y_lo: 2; y = y_hi * 2 + y_lo), z: 8, core: 2. Of those that a mesh axis runs over, the one named last changes fastest.
Arguments:
- frames: bfloat16 [16, 2048, 1024], P('dp', 'tm'), may hold values from -6 to 6
- cotangent: bfloat16 [16, 2048, 1024], P('dp', 'tm'), may hold values from -6 to 6
- lengths: int32 [16], P('dp'), may hold values from 512 to 2048, as said below
- w_proj: bfloat16 [1024, 2048], replicated
- gain_attn: float32 [1024], replicated, may hold values from 0.25 to 1.75
- gain_conv: float32 [1024], replicated, may hold values from 0.25 to 1.75
- w_conv: bfloat16 [31, 1024], replicated, may hold values from -1 to 1
Outputs:
- grad_frames: bfloat16 [16, 2048, 1024], P('dp', 'tm')
- grad_proj: float32 [1024, 2048], P(('dp', 'tm'))
- grad_conv: float32 [31, 1024], replicated
- grad_gains: float32 [2, 1024], replicated
The draws below stay inside these ranges and needn't reach their ends.
Inputs may be any that keep to these rules, and one draw needn't show every extreme that they name: lengths[r] counts the valid frames of recording r; later frames are padding. Some recording has exactly 2048 and some exactly 512.
All inputs are finite; a program needn't handle non-finite values.
Results may differ from the reference program's by a relative error of at most 0.035.
Values may be sent and summed in bfloat16 or wider, within the bound.
No kernel may reach another device: no remote copies, remote signals or barrier semaphores. Data moves between devices by JAX's collectives and lax.ppermute only.
A program may use at most 128 MiB of HBM per device.

```python
import math
import jax
import jax.numpy as jnp
from jax import lax

D = 1024
HEADS = 8
HDIM = 64
KER = 31
HD = 512
LEN = 2048
RECS = 16


def draw_frames(key, part):
    base = jax.random.normal(key, (RECS, LEN, D), jnp.float32)
    return jnp.clip(base, -6.0, 6.0).astype(jnp.bfloat16)


def draw_w_proj(key, part):
    width = HEADS * HDIM
    base = jnp.clip(jax.random.normal(key, (D, 4 * width), jnp.float32), -6.0, 6.0)
    column = jnp.arange(4 * width)
    factor = jnp.where(column < 3 * width, D ** (-0.5), width ** (-0.5)).astype(jnp.float32)
    return (base * factor[None, :]).astype(jnp.bfloat16)


def draw_lengths(key, part):
    lowest = LEN // 4
    picks = jax.random.randint(key, (RECS,), lowest, LEN + 1)
    order = jax.random.permutation(jax.random.fold_in(key, 1), RECS)
    picks = jnp.where(order == 0, LEN, picks)
    picks = jnp.where(order == 1, lowest, picks)
    return picks.astype(jnp.int32)


def raised(drawn, rng, source, target, parts, factor):
    def block_of(position):
        return (jnp.arange(drawn.shape[position]) // (drawn.shape[position] // parts)).reshape((-1,) + (1,) * (drawn.ndim - 1 - position))

    first = jax.random.permutation(rng, parts)[block_of(target)]
    second = (block_of(target) + parts // 2) % parts
    return jnp.where((block_of(source) == first) | (block_of(source) == second), factor * drawn, drawn)


def block_scale(key, extent, shards, least, largest):
    level = 1.0
    for position, blocks in shards:
        steps = jax.random.uniform(jax.random.fold_in(jax.random.fold_in(key, 6), position), (blocks,), jnp.float32, least / len(shards), largest / len(shards))
        level = level * jnp.repeat(jnp.exp(steps), extent[position] // blocks).reshape((-1,) + (1,) * (len(extent) - 1 - position))
    return level


def normal_values(key, extent, scale, most, cuts=(), kind=jnp.bfloat16):
    loudness = block_scale(key, extent, cuts, -0.22, 0.18) if cuts else 1.0
    array = jax.random.normal(key, extent, jnp.float32) * scale * loudness
    return jnp.minimum(jnp.maximum(array, -most), most).astype(kind)


def noise_with(own_key, shape, scale, limit, cuts, heavy, held_as=jnp.bfloat16):
    result = scale * jax.random.normal(own_key, shape, jnp.float32)
    if cuts:
        result = result * block_scale(own_key, shape, cuts, -0.22, 0.18)
    return jnp.clip(raised(result, jax.random.fold_in(own_key, 3), *heavy), -limit, limit).astype(held_as)


def setup_inputs(seed: int = 0) -> dict:
    key_list = jax.random.split(jax.random.key(seed), 8)
    frames = draw_frames(jax.random.fold_in(key_list[7], 71), 0)
    cotangent = noise_with(key_list[1], (RECS, LEN, D), 1.0, 6.0, ((0, 16), (1, 16)), (1, 2, 16, 2.0))
    lengths = draw_lengths(jax.random.fold_in(key_list[7], 71), 0)
    w_proj = draw_w_proj(jax.random.fold_in(key_list[7], 71), 0)
    gain_attn = jnp.clip(1.0 + 0.15 * jax.random.normal(key_list[4], (D,), jnp.float32), 0.25, 1.75)
    gain_conv = jnp.clip(1.0 + 0.15 * jax.random.normal(key_list[5], (D,), jnp.float32), 0.25, 1.75)
    w_conv = normal_values(key_list[6], (KER, D), KER ** -0.5, 1.0)
    return dict(frames=frames, cotangent=cotangent, lengths=lengths, w_proj=w_proj, gain_attn=gain_attn, gain_conv=gain_conv, w_conv=w_conv)


epsilon = 1e-05
negative = -1e+30

def normalize(inputs, gain):
    centre = inputs - lax.optimization_barrier(jnp.mean(inputs, axis=-1, keepdims=True))
    spread = lax.optimization_barrier(jnp.mean(centre * centre, axis=-1, keepdims=True))
    return centre * lax.rsqrt(spread + epsilon) * gain

def stored(values):
    return lax.optimization_barrier(values.astype(jnp.bfloat16))

def split_heads(matrix):
    return matrix.reshape(matrix.shape[0], HEADS, HDIM).astype(jnp.float32)

def attention(queries, key_rows, value_rows, length):
    block = math.gcd(LEN, 512)
    scaling = 1.0 / math.sqrt(HDIM)
    key_heads = split_heads(key_rows)
    value_heads = split_heads(value_rows)
    living = (jnp.arange(LEN, dtype=jnp.int32) < length)[None, None, :]

    def one_block(query_block):
        query_heads = split_heads(query_block)
        scores = jnp.where(living, jnp.einsum('bhd,lhd->hbl', query_heads, key_heads) * scaling, negative)
        top = lax.optimization_barrier(jnp.max(scores, axis=-1))
        weights = jnp.where(living, jnp.exp(scores - top[:, :, None]), 0.0)
        total = lax.optimization_barrier(jnp.sum(weights, axis=-1))
        output = jnp.einsum('hbl,lhd->bhd', stored(weights).astype(jnp.float32), value_heads) / total.T[:, :, None]
        return (stored(output.reshape(block, HD)), (top + jnp.log(total)).T)
    attended, logsum = lax.map(one_block, queries.reshape(LEN // block, block, HD))
    return (attended.reshape(LEN, HD), logsum.reshape(LEN, HEADS))

def attention_back(queries, key_rows, value_rows, attended, logsum, grad_attended, length):
    block = math.gcd(LEN, 512)
    scaling = 1.0 / math.sqrt(HDIM)
    key_heads = split_heads(key_rows)
    value_heads = split_heads(value_rows)
    living = (jnp.arange(LEN, dtype=jnp.int32) < length)[None, None, :]
    delta = lax.optimization_barrier(jnp.sum(split_heads(grad_attended) * split_heads(attended), axis=-1))

    def one_block(carried, members):
        query_block, grad_block, logsum_block, delta_block = members
        query_heads = split_heads(query_block)
        grad_heads = split_heads(grad_block)
        scores = jnp.where(living, jnp.einsum('bhd,lhd->hbl', query_heads, key_heads) * scaling, negative)
        probs = jnp.where(living, jnp.exp(scores - logsum_block.T[:, :, None]), 0.0)
        dprobs = jnp.einsum('bhd,lhd->hbl', grad_heads, value_heads)
        grad_scores = stored(probs * (dprobs - delta_block.T[:, :, None])).astype(jnp.float32)
        probs_low = stored(probs).astype(jnp.float32)
        grad_query = jnp.einsum('hbl,lhd->bhd', grad_scores, key_heads) * scaling
        grad_key = carried[0] + jnp.einsum('hbl,bhd->lhd', grad_scores, query_heads) * scaling
        grad_value = carried[1] + jnp.einsum('hbl,bhd->lhd', probs_low, grad_heads)
        return ((grad_key, grad_value), stored(grad_query.reshape(block, HD)))
    zero_heads = jnp.zeros((LEN, HEADS, HDIM), jnp.float32)
    members = (queries.reshape(LEN // block, block, HD), grad_attended.reshape(LEN // block, block, HD), logsum.reshape(LEN // block, block, HEADS), delta.reshape(LEN // block, block, HEADS))
    (grad_key, grad_value), grad_query = lax.scan(one_block, (zero_heads, zero_heads), members)
    return (grad_query.reshape(LEN, HD), stored(grad_key.reshape(LEN, HD)), stored(grad_value.reshape(LEN, HD)))

def recording(frames, cotangent, length, w_proj, gain_attn, gain_conv, w_conv):
    inputs = frames.astype(jnp.float32)
    normed_attn = stored(normalize(inputs, gain_attn))
    projected = stored(jnp.dot(normed_attn, w_proj[:, :3 * HD], preferred_element_type=jnp.float32))
    queries = projected[:, :HD]
    key_rows = projected[:, HD:2 * HD]
    value_rows = projected[:, 2 * HD:]
    attended, logsum = attention(queries, key_rows, value_rows, length)
    w_out = w_proj[:, 3 * HD:]
    resid = stored(inputs + jnp.dot(attended, w_out.T, preferred_element_type=jnp.float32))
    resid_f = resid.astype(jnp.float32)
    valid = (jnp.arange(LEN, dtype=jnp.int32) < length)[:, None]
    normed_conv = stored(jnp.where(valid, normalize(resid_f, gain_conv), 0.0))
    reach = KER // 2
    padded = jnp.pad(normed_conv.astype(jnp.float32), ((reach, reach), (0, 0)))
    kernel = w_conv.astype(jnp.float32)
    conv = jnp.zeros((LEN, D), jnp.float32)
    for shift_index in range(KER):
        conv = conv + kernel[shift_index] * padded[shift_index:shift_index + LEN]
    upstream = cotangent.astype(jnp.float32)
    gate = jax.nn.sigmoid(conv)
    grad_conv_in = upstream * gate * (1.0 + conv * (1.0 - gate))
    conv_term = jnp.stack([lax.optimization_barrier(jnp.sum(grad_conv_in * padded[shift_index:shift_index + LEN], axis=0)) for shift_index in range(KER)])
    grad_padded = jnp.pad(grad_conv_in, ((reach, reach), (0, 0)))
    grad_normed = jnp.zeros((LEN, D), jnp.float32)
    for shift_index in range(KER):
        begin = 2 * reach - shift_index
        grad_normed = grad_normed + kernel[shift_index] * grad_padded[begin:begin + LEN]
    grad_normed = jnp.where(valid, grad_normed, 0.0)
    unused_conv, pull_conv = jax.vjp(normalize, resid_f, gain_conv)
    back_resid, gain_conv_term = pull_conv(grad_normed)
    grad_resid = upstream + back_resid
    grad_resid_low = stored(grad_resid)
    grad_attended = stored(jnp.dot(grad_resid_low, w_out, preferred_element_type=jnp.float32))
    grad_query, grad_key, grad_value = attention_back(queries, key_rows, value_rows, attended, logsum, grad_attended, length)
    grad_qkv = jnp.concatenate([grad_query, grad_key, grad_value], axis=1)
    back_normed = jnp.dot(grad_qkv, w_proj[:, :3 * HD].T, preferred_element_type=jnp.float32)
    unused_attn, pull_attn = jax.vjp(normalize, inputs, gain_attn)
    back_inputs, gain_attn_term = pull_attn(back_normed)
    grad_frames = (grad_resid + back_inputs).astype(jnp.bfloat16)
    proj_term = jnp.concatenate([jnp.dot(normed_attn.T, grad_qkv, preferred_element_type=jnp.float32), jnp.dot(grad_resid_low.T, attended, preferred_element_type=jnp.float32)], axis=1)
    return (grad_frames, proj_term, conv_term, jnp.stack([gain_attn_term, gain_conv_term]))

def reference(frames, cotangent, lengths, w_proj, gain_attn, gain_conv, w_conv):

    def advance(totals, members):
        grad_frames, proj_term, conv_term, gains_term = recording(members[0], members[1], members[2], w_proj, gain_attn, gain_conv, w_conv)
        return ((totals[0] + proj_term, totals[1] + conv_term, totals[2] + gains_term), grad_frames)
    start = (jnp.zeros((D, 4 * HD), jnp.float32), jnp.zeros((KER, D), jnp.float32), jnp.zeros((2, D), jnp.float32))
    totals, grad_frames = lax.scan(advance, start, (frames, cotangent, lengths))
    grad_scale = 1.0 / math.sqrt(RECS * LEN)
    return (grad_frames, totals[0] * grad_scale, totals[1] * grad_scale, totals[2] * grad_scale)
```

```python
import math

import jax
import jax.numpy as jnp
from jax import lax
from jax.sharding import PartitionSpec as P

HEADS = 8
HDIM = 64
KER = 31


epsilon = 1e-05
negative = -1e30


def padded_2(value, sides, width):
    for axis, dim in sides:
        size, length = (lax.axis_size(axis), value.shape[dim])
        up = [(i, (i + 1) % size) for i in range(size - 1)]
        down = [(j, i) for i, j in up]
        last = lax.slice_in_dim(value, length - width, length, axis=dim)
        first = lax.slice_in_dim(value, 0, width, axis=dim)
        before = lax.ppermute(last, axis, up)
        after = lax.ppermute(first, axis, down)
        value = jnp.concatenate([before, value, after], axis=dim)
    return value


def normalize(inputs, gain):
    centre = inputs - jnp.mean(inputs, axis=-1, keepdims=True)
    spread = jnp.mean(centre * centre, axis=-1, keepdims=True)
    return centre * lax.rsqrt(spread + epsilon) * gain


def split_heads(matrix):
    return matrix.reshape(matrix.shape[0], HEADS, HDIM)


def over_blocks(advance, carried, members):
    total_rows = members[0].shape[0]
    stride = math.gcd(total_rows, 1024)

    def one_block(block_index, inner_state):
        offset = block_index * stride
        sliced = tuple((lax.dynamic_slice_in_dim(member, offset, stride, 0) for member in members))
        return advance(inner_state, sliced, offset)

    return lax.fori_loop(0, total_rows // stride, one_block, carried)


def forward_step(query_heads, length, scaling):

    def advance(carried, sliced, first_row):
        key_heads = split_heads(sliced[0])
        value_heads = split_heads(sliced[1])
        positions = first_row + jnp.arange(key_heads.shape[0], dtype=jnp.int32)
        living = (positions < length)[None, None, :]
        scores = (
            jnp.einsum("bhd,lhd->hbl", query_heads, key_heads, preferred_element_type=jnp.float32)
            * scaling
        )
        scores = jnp.where(living, scores, negative)
        top_old, total_old, accumulated = carried
        top_new = jnp.maximum(top_old, jnp.max(scores, axis=-1))
        weights = jnp.where(living, jnp.exp(scores - top_new[:, :, None]), 0.0)
        fading = jnp.exp(top_old - top_new)
        total_new = total_old * fading + jnp.sum(weights, axis=-1)
        update = jnp.einsum(
            "hbl,lhd->bhd",
            weights.astype(jnp.bfloat16),
            value_heads,
            preferred_element_type=jnp.float32,
        )
        return (top_new, total_new, accumulated * fading.T[:, :, None] + update)

    return advance


def query_side(query_heads, grad_heads, logsum, delta, length, scaling):

    def advance(carried, sliced, first_row):
        key_heads = split_heads(sliced[0])
        value_heads = split_heads(sliced[1])
        count_here = key_heads.shape[0]
        positions = first_row + jnp.arange(count_here, dtype=jnp.int32)
        living = (positions < length)[None, None, :]
        scores = (
            jnp.einsum("bhd,lhd->hbl", query_heads, key_heads, preferred_element_type=jnp.float32)
            * scaling
        )
        scores = jnp.where(living, scores, negative)
        probs = jnp.where(living, jnp.exp(scores - logsum.T[:, :, None]), 0.0)
        dprobs = jnp.einsum(
            "bhd,lhd->hbl", grad_heads, value_heads, preferred_element_type=jnp.float32
        )
        grad_scores = (probs * (dprobs - delta.T[:, :, None])).astype(jnp.bfloat16)
        grad_query = (
            carried[0]
            + jnp.einsum("hbl,lhd->bhd", grad_scores, key_heads, preferred_element_type=jnp.float32)
            * scaling
        )
        return (grad_query,)

    return advance


def key_side(key_heads, value_heads, own_living, scaling):

    def advance(carried, sliced, first_row):
        query_heads = split_heads(sliced[0].astype(jnp.bfloat16))
        grad_heads = split_heads(sliced[1].astype(jnp.bfloat16))
        logsum_block = sliced[2]
        delta_block = sliced[3]
        scores = (
            jnp.einsum("bhd,lhd->hbl", query_heads, key_heads, preferred_element_type=jnp.float32)
            * scaling
        )
        scores = jnp.where(own_living, scores, negative)
        probs = jnp.where(own_living, jnp.exp(scores - logsum_block.T[:, :, None]), 0.0)
        dprobs = jnp.einsum(
            "bhd,lhd->hbl", grad_heads, value_heads, preferred_element_type=jnp.float32
        )
        grad_scores = (probs * (dprobs - delta_block.T[:, :, None])).astype(jnp.bfloat16)
        grad_key = (
            carried[0]
            + jnp.einsum(
                "hbl,bhd->lhd", grad_scores, query_heads, preferred_element_type=jnp.float32
            )
            * scaling
        )
        grad_value = carried[1] + jnp.einsum(
            "hbl,bhd->lhd",
            probs.astype(jnp.bfloat16),
            grad_heads,
            preferred_element_type=jnp.float32,
        )
        return (grad_key, grad_value)

    return advance


def per_device(frames, cotangent, lengths, w_proj, gain_attn, gain_conv, w_conv):
    frame_count = frames.shape[1]
    width = HEADS * HDIM
    cycle_size = lax.axis_size("tm")
    own_start = lax.axis_index("tm") * frame_count
    length = lengths[0]
    scaling = 1.0 / math.sqrt(HDIM)
    total_frames = lax.axis_size("dp") * frames.shape[0] * frame_count * cycle_size
    grad_scale = 1.0 / math.sqrt(total_frames)
    contract_last = (((1,), (1,)), ((), ()))
    contract_first = (((0,), (0,)), ((), ()))
    inputs = frames[0].astype(jnp.float32)
    normed_attn = normalize(inputs, gain_attn).astype(jnp.bfloat16)
    projected = jnp.dot(
        normed_attn, w_proj[:, : 3 * width], preferred_element_type=jnp.float32
    ).astype(jnp.bfloat16)
    queries = projected[:, :width]
    key_rows = projected[:, width : 2 * width]
    value_rows = projected[:, 2 * width :]
    query_heads = split_heads(queries)
    start_state = (
        jnp.full((HEADS, frame_count), negative, jnp.float32),
        jnp.zeros((HEADS, frame_count), jnp.float32),
        jnp.zeros((frame_count, HEADS, HDIM), jnp.float32),
    )
    advance_forward = forward_step(query_heads, length, scaling)
    key_value_all = lax.all_gather(projected[:, width:], "tm", axis=0, tiled=True)
    keys_all = key_value_all[:, :width]
    values_all = key_value_all[:, width:]
    top_all, total_all, accumulated = over_blocks(
        advance_forward,
        start_state,
        (keys_all, values_all),
    )
    attended = (
        (accumulated / total_all.T[:, :, None]).reshape(frame_count, width).astype(jnp.bfloat16)
    )
    logsum = (top_all + jnp.log(total_all)).T
    w_out = w_proj[:, 3 * width :]
    mixed = inputs + lax.dot_general(
        attended, w_out, contract_last, preferred_element_type=jnp.float32
    )
    resid_f = mixed.astype(jnp.bfloat16).astype(jnp.float32)
    positions = own_start + jnp.arange(frame_count, dtype=jnp.int32)
    valid = (positions < length)[:, None]
    normed_conv = jnp.where(valid, normalize(resid_f, gain_conv), 0.0).astype(jnp.bfloat16)
    reach = KER // 2
    padded = padded_2(normed_conv, (("tm", 0),), reach).astype(jnp.float32)
    kernel = w_conv.astype(jnp.float32)
    conv = jnp.zeros((frame_count, padded.shape[1]), jnp.float32)
    for shift_index in range(KER):
        conv = conv + kernel[shift_index] * padded[shift_index : shift_index + frame_count]
    upstream = cotangent[0].astype(jnp.float32)
    gate = jax.nn.sigmoid(conv)
    grad_conv_in = upstream * gate * (1.0 + conv * (1.0 - gate))
    conv_term = jnp.stack(
        [
            jnp.sum(grad_conv_in * padded[shift_index : shift_index + frame_count], axis=0)
            for shift_index in range(KER)
        ]
    )
    grad_padded = padded_2(grad_conv_in.astype(jnp.bfloat16), (("tm", 0),), reach).astype(
        grad_conv_in.dtype
    )
    grad_normed = jnp.zeros_like(grad_conv_in)
    for shift_index in range(KER):
        begin = 2 * reach - shift_index
        grad_normed = grad_normed + kernel[shift_index] * grad_padded[begin : begin + frame_count]
    grad_normed = jnp.where(valid, grad_normed, 0.0)
    unused_conv, pull_conv = jax.vjp(normalize, resid_f, gain_conv)
    back_resid, gain_conv_term = pull_conv(grad_normed)
    grad_resid = upstream + back_resid
    grad_resid_low = grad_resid.astype(jnp.bfloat16)
    grad_attended = jnp.dot(grad_resid_low, w_out, preferred_element_type=jnp.float32).astype(
        jnp.bfloat16
    )
    grad_heads = split_heads(grad_attended)
    delta = jnp.sum(
        grad_heads.astype(jnp.float32) * split_heads(attended).astype(jnp.float32), axis=-1
    )
    zero_heads = jnp.zeros((frame_count, HEADS, HDIM), jnp.float32)
    back_start = (zero_heads,)
    advance_back = query_side(query_heads, grad_heads, logsum, delta, length, scaling)
    back_state = over_blocks(
        advance_back,
        back_start,
        (keys_all, values_all),
    )
    own_living = valid[:, 0][None, None, :]
    advance_keys = key_side(split_heads(key_rows), split_heads(value_rows), own_living, scaling)
    rows_all = lax.all_gather(
        jnp.concatenate([queries, grad_attended], axis=1), "tm", axis=0, tiled=True
    )
    stats_all = lax.all_gather(jnp.concatenate([logsum, delta], axis=1), "tm", axis=0, tiled=True)
    grad_keys, grad_values = over_blocks(
        advance_keys,
        (zero_heads, zero_heads),
        (rows_all[:, :width], rows_all[:, width:], stats_all[:, :HEADS], stats_all[:, HEADS:]),
    )
    grad_qkv = jnp.concatenate(
        [
            back_state[0].reshape(frame_count, width).astype(jnp.bfloat16),
            grad_keys.reshape(frame_count, width).astype(jnp.bfloat16),
            grad_values.reshape(frame_count, width).astype(jnp.bfloat16),
        ],
        axis=1,
    )
    back_normed = lax.dot_general(
        grad_qkv, w_proj[:, : 3 * width], contract_last, preferred_element_type=jnp.float32
    )
    unused_attn, pull_attn = jax.vjp(normalize, inputs, gain_attn)
    back_inputs, gain_attn_term = pull_attn(back_normed)
    grad_frames = (grad_resid + back_inputs).astype(jnp.bfloat16)[None]
    inner_part = lax.dot_general(
        normed_attn, grad_qkv, contract_first, preferred_element_type=jnp.float32
    )
    outer_part = lax.dot_general(
        grad_resid_low, attended, contract_first, preferred_element_type=jnp.float32
    )
    axes = ("dp", "tm")
    devices = lax.axis_size(axes)
    rows = inner_part.shape[0]
    small = jnp.concatenate([conv_term, gain_attn_term[None], gain_conv_term[None]], axis=0)
    small_count = small.size
    small_width = -(-small_count // rows)
    small_flat = jnp.pad(small.reshape(-1), (0, small_width * rows - small_count))
    packed = jnp.concatenate(
        [inner_part, outer_part, small_flat.reshape(rows, small_width)], axis=1
    )
    packed = packed.reshape(devices, rows // devices, packed.shape[1]).astype(jnp.bfloat16)
    reduced = lax.all_to_all(packed, axes, 0, 0, tiled=True).astype(jnp.float32).sum(0)
    grad_proj = reduced[:, : 4 * width]
    small_part = reduced[:, 4 * width :].reshape(1, -1)
    small_all = lax.all_to_all(
        jnp.broadcast_to(small_part, (devices, small_part.shape[1])), axes, 0, 0, tiled=True
    )
    small_sum = small_all.reshape(-1)[:small_count]
    conv_sum = small_sum[: conv_term.size].reshape(conv_term.shape)
    gains_sum = small_sum[conv_term.size :].reshape(2, -1)
    return (grad_frames, grad_proj * grad_scale, conv_sum * grad_scale, gains_sum * grad_scale)


def solution(mesh):
    return jax.shard_map(
        per_device,
        mesh=mesh,
        in_specs=(P("dp", "tm", None), P("dp", "tm", None), P("dp"), P(), P(), P(), P()),
        out_specs=(P("dp", "tm", None), P(("dp", "tm"), None), P(), P()),
        check_vma=False,
    )
```

```python
import math

import jax
import jax.numpy as jnp
from jax import lax
from jax.sharding import PartitionSpec as P

HEADS = 8
HDIM = 64
KER = 31


epsilon = 1e-05
negative = -1e30


def padded_2(value, sides, width):
    for axis, dim in sides:
        size, length = (lax.axis_size(axis), value.shape[dim])
        up = [(i, (i + 1) % size) for i in range(size - 1)]
        down = [(j, i) for i, j in up]
        last = lax.slice_in_dim(value, length - width, length, axis=dim)
        first = lax.slice_in_dim(value, 0, width, axis=dim)
        before = lax.ppermute(last, axis, up)
        after = lax.ppermute(first, axis, down)
        value = jnp.concatenate([before, value, after], axis=dim)
    return value


def normalize(inputs, gain):
    centre = inputs - jnp.mean(inputs, axis=-1, keepdims=True)
    spread = jnp.mean(centre * centre, axis=-1, keepdims=True)
    return centre * lax.rsqrt(spread + epsilon) * gain


def split_heads(matrix):
    return matrix.reshape(matrix.shape[0], HEADS, HDIM)


def over_blocks(advance, carried, members):
    total_rows = members[0].shape[0]
    stride = math.gcd(total_rows, 1024)

    def one_block(block_index, inner_state):
        offset = block_index * stride
        sliced = tuple((lax.dynamic_slice_in_dim(member, offset, stride, 0) for member in members))
        return advance(inner_state, sliced, offset)

    return lax.fori_loop(0, total_rows // stride, one_block, carried)


def forward_step(query_heads, length, scaling):

    def advance(carried, sliced, first_row):
        key_heads = split_heads(sliced[0])
        value_heads = split_heads(sliced[1])
        positions = first_row + jnp.arange(key_heads.shape[0], dtype=jnp.int32)
        living = (positions < length)[None, None, :]
        scores = (
            jnp.einsum("bhd,lhd->hbl", query_heads, key_heads, preferred_element_type=jnp.float32)
            * scaling
        )
        scores = jnp.where(living, scores, negative)
        top_old, total_old, accumulated = carried
        top_new = jnp.maximum(top_old, jnp.max(scores, axis=-1))
        weights = jnp.where(living, jnp.exp(scores - top_new[:, :, None]), 0.0)
        fading = jnp.exp(top_old - top_new)
        total_new = total_old * fading + jnp.sum(weights, axis=-1)
        update = jnp.einsum(
            "hbl,lhd->bhd",
            weights.astype(jnp.bfloat16),
            value_heads,
            preferred_element_type=jnp.float32,
        )
        return (top_new, total_new, accumulated * fading.T[:, :, None] + update)

    return advance


def query_side(query_heads, grad_heads, logsum, delta, length, scaling):

    def advance(carried, sliced, first_row):
        key_heads = split_heads(sliced[0])
        value_heads = split_heads(sliced[1])
        count_here = key_heads.shape[0]
        positions = first_row + jnp.arange(count_here, dtype=jnp.int32)
        living = (positions < length)[None, None, :]
        scores = (
            jnp.einsum("bhd,lhd->hbl", query_heads, key_heads, preferred_element_type=jnp.float32)
            * scaling
        )
        scores = jnp.where(living, scores, negative)
        probs = jnp.where(living, jnp.exp(scores - logsum.T[:, :, None]), 0.0)
        dprobs = jnp.einsum(
            "bhd,lhd->hbl", grad_heads, value_heads, preferred_element_type=jnp.float32
        )
        grad_scores = (probs * (dprobs - delta.T[:, :, None])).astype(jnp.bfloat16)
        grad_query = (
            carried[0]
            + jnp.einsum("hbl,lhd->bhd", grad_scores, key_heads, preferred_element_type=jnp.float32)
            * scaling
        )
        return (grad_query,)

    return advance


def key_side(key_heads, value_heads, own_living, scaling):

    def advance(carried, sliced, first_row):
        query_heads = split_heads(sliced[0].astype(jnp.bfloat16))
        grad_heads = split_heads(sliced[1].astype(jnp.bfloat16))
        logsum_block = sliced[2]
        delta_block = sliced[3]
        scores = (
            jnp.einsum("bhd,lhd->hbl", query_heads, key_heads, preferred_element_type=jnp.float32)
            * scaling
        )
        scores = jnp.where(own_living, scores, negative)
        probs = jnp.where(own_living, jnp.exp(scores - logsum_block.T[:, :, None]), 0.0)
        dprobs = jnp.einsum(
            "bhd,lhd->hbl", grad_heads, value_heads, preferred_element_type=jnp.float32
        )
        grad_scores = (probs * (dprobs - delta_block.T[:, :, None])).astype(jnp.bfloat16)
        grad_key = (
            carried[0]
            + jnp.einsum(
                "hbl,bhd->lhd", grad_scores, query_heads, preferred_element_type=jnp.float32
            )
            * scaling
        )
        grad_value = carried[1] + jnp.einsum(
            "hbl,bhd->lhd",
            probs.astype(jnp.bfloat16),
            grad_heads,
            preferred_element_type=jnp.float32,
        )
        return (grad_key, grad_value)

    return advance


def per_device(frames, cotangent, lengths, w_proj, gain_attn, gain_conv, w_conv):
    frame_count = frames.shape[1]
    width = HEADS * HDIM
    cycle_size = lax.axis_size("tm")
    own_start = lax.axis_index("tm") * frame_count
    length = lengths[0]
    scaling = 1.0 / math.sqrt(HDIM)
    total_frames = lax.axis_size("dp") * frames.shape[0] * frame_count * cycle_size
    grad_scale = 1.0 / math.sqrt(total_frames)
    contract_last = (((1,), (1,)), ((), ()))
    contract_first = (((0,), (0,)), ((), ()))
    inputs = frames[0].astype(jnp.float32)
    normed_attn = normalize(inputs, gain_attn).astype(jnp.bfloat16)
    projected = jnp.dot(
        normed_attn, w_proj[:, : 3 * width], preferred_element_type=jnp.float32
    ).astype(jnp.bfloat16)
    tm_count = lax.axis_size("tm")
    halves = tm_count // HEADS
    me = lax.axis_index("tm")
    half = me // HEADS
    span = frame_count * HEADS
    total = frame_count * tm_count
    key_live = (jnp.arange(total, dtype=jnp.int32) < length)[None, :]
    half_live = lax.dynamic_slice_in_dim(key_live, half * span, span, 1)
    mine = (jnp.arange(halves) == half).reshape(halves, 1, 1, 1, 1)
    qkv = projected.reshape(frame_count, 3, HEADS, HDIM).transpose(2, 0, 1, 3)
    got = lax.all_to_all(jnp.tile(qkv, (halves, 1, 1, 1)), "tm", 0, 0, tiled=True)
    got = got.reshape(total, 3, HDIM)
    q_all, k_all, v_all = got[:, 0], got[:, 1], got[:, 2]
    q_half = lax.dynamic_slice_in_dim(q_all, half * span, span, 0)
    scores = lax.dot_general(q_half, k_all, contract_last, preferred_element_type=jnp.float32)
    scores = jnp.where(key_live, scores * scaling, negative)
    top = jnp.max(scores, axis=-1)
    weights = jnp.where(key_live, jnp.exp(scores - top[:, None]), 0.0)
    summed = jnp.sum(weights, axis=-1)
    acc = jnp.dot(weights.astype(jnp.bfloat16), v_all, preferred_element_type=jnp.float32)
    a_half = (acc / summed[:, None]).astype(jnp.bfloat16)
    lse_half = top + jnp.log(summed)

    def to_frames(rows):
        blocks = rows.reshape((1, HEADS, frame_count) + rows.shape[1:])
        placed = jnp.where(mine.reshape((halves,) + (1,) * (blocks.ndim - 1)), blocks, 0)
        placed = placed.reshape((tm_count, frame_count) + rows.shape[1:])
        back = lax.all_to_all(placed, "tm", 0, 0, tiled=True)
        back = back.reshape((halves, HEADS, frame_count) + rows.shape[1:])
        return jnp.sum(back.astype(jnp.float32), axis=0).astype(rows.dtype)

    attended = to_frames(a_half).transpose(1, 0, 2).reshape(frame_count, width)
    w_out = w_proj[:, 3 * width :]
    mixed = inputs + lax.dot_general(
        attended, w_out, contract_last, preferred_element_type=jnp.float32
    )
    resid_f = mixed.astype(jnp.bfloat16).astype(jnp.float32)
    positions = own_start + jnp.arange(frame_count, dtype=jnp.int32)
    valid = (positions < length)[:, None]
    normed_conv = jnp.where(valid, normalize(resid_f, gain_conv), 0.0).astype(jnp.bfloat16)
    reach = KER // 2
    padded = padded_2(normed_conv, (("tm", 0),), reach).astype(jnp.float32)
    kernel = w_conv.astype(jnp.float32)
    conv = jnp.zeros((frame_count, padded.shape[1]), jnp.float32)
    for shift_index in range(KER):
        conv = conv + kernel[shift_index] * padded[shift_index : shift_index + frame_count]
    upstream = cotangent[0].astype(jnp.float32)
    gate = jax.nn.sigmoid(conv)
    grad_conv_in = upstream * gate * (1.0 + conv * (1.0 - gate))
    conv_term = jnp.stack(
        [
            jnp.sum(grad_conv_in * padded[shift_index : shift_index + frame_count], axis=0)
            for shift_index in range(KER)
        ]
    )
    grad_padded = padded_2(grad_conv_in.astype(jnp.bfloat16), (("tm", 0),), reach).astype(
        grad_conv_in.dtype
    )
    grad_normed = jnp.zeros_like(grad_conv_in)
    for shift_index in range(KER):
        begin = 2 * reach - shift_index
        grad_normed = grad_normed + kernel[shift_index] * grad_padded[begin : begin + frame_count]
    grad_normed = jnp.where(valid, grad_normed, 0.0)
    unused_conv, pull_conv = jax.vjp(normalize, resid_f, gain_conv)
    back_resid, gain_conv_term = pull_conv(grad_normed)
    grad_resid = upstream + back_resid
    grad_resid_low = grad_resid.astype(jnp.bfloat16)
    grad_attended = jnp.dot(grad_resid_low, w_out, preferred_element_type=jnp.float32).astype(
        jnp.bfloat16
    )
    send_grad = grad_attended.reshape(frame_count, HEADS, HDIM).transpose(1, 0, 2)
    da_all = lax.all_to_all(jnp.tile(send_grad, (halves, 1, 1)), "tm", 0, 0, tiled=True)
    da_all = da_all.reshape(total, HDIM)
    da_half = lax.dynamic_slice_in_dim(da_all, half * span, span, 0)
    delta_half = jnp.sum(da_half.astype(jnp.float32) * a_half.astype(jnp.float32), axis=-1)
    stats_half = jnp.stack([lse_half, delta_half], axis=0)
    partner = lax.ppermute(
        stats_half, "tm", [(i, (i + HEADS) % tm_count) for i in range(tm_count)]
    )
    stats_all = jnp.where(
        half == 0,
        jnp.concatenate([stats_half, partner], axis=1),
        jnp.concatenate([partner, stats_half], axis=1),
    )
    lse_all = stats_all[0][:, None]
    delta_all = stats_all[1][:, None]
    scores = lax.dot_general(q_half, k_all, contract_last, preferred_element_type=jnp.float32)
    scores = jnp.where(key_live, scores * scaling, negative)
    probs = jnp.where(key_live, jnp.exp(scores - lse_half[:, None]), 0.0)
    dprobs = lax.dot_general(da_half, v_all, contract_last, preferred_element_type=jnp.float32)
    grad_scores = (probs * (dprobs - delta_half[:, None])).astype(jnp.bfloat16)
    grad_q = jnp.dot(grad_scores, k_all, preferred_element_type=jnp.float32) * scaling
    k_half = lax.dynamic_slice_in_dim(k_all, half * span, span, 0)
    v_half = lax.dynamic_slice_in_dim(v_all, half * span, span, 0)
    scores = lax.dot_general(q_all, k_half, contract_last, preferred_element_type=jnp.float32)
    scores = jnp.where(half_live, scores * scaling, negative)
    probs = jnp.where(half_live, jnp.exp(scores - lse_all), 0.0)
    dprobs = lax.dot_general(da_all, v_half, contract_last, preferred_element_type=jnp.float32)
    grad_scores = (probs * (dprobs - delta_all)).astype(jnp.bfloat16)
    grad_k = (
        lax.dot_general(grad_scores, q_all, contract_first, preferred_element_type=jnp.float32)
        * scaling
    )
    grad_v = lax.dot_general(
        probs.astype(jnp.bfloat16), da_all, contract_first, preferred_element_type=jnp.float32
    )
    grad_rows = jnp.stack([grad_q, grad_k, grad_v], axis=1).astype(jnp.bfloat16)
    grad_qkv = to_frames(grad_rows).transpose(1, 2, 0, 3).reshape(frame_count, 3 * width)
    back_normed = lax.dot_general(
        grad_qkv, w_proj[:, : 3 * width], contract_last, preferred_element_type=jnp.float32
    )
    unused_attn, pull_attn = jax.vjp(normalize, inputs, gain_attn)
    back_inputs, gain_attn_term = pull_attn(back_normed)
    grad_frames = (grad_resid + back_inputs).astype(jnp.bfloat16)[None]
    inner_part = lax.dot_general(
        normed_attn, grad_qkv, contract_first, preferred_element_type=jnp.float32
    )
    outer_part = lax.dot_general(
        grad_resid_low, attended, contract_first, preferred_element_type=jnp.float32
    )
    axes = ("dp", "tm")
    devices = lax.axis_size(axes)
    rows = inner_part.shape[0]
    small = jnp.concatenate([conv_term, gain_attn_term[None], gain_conv_term[None]], axis=0)
    small_count = small.size
    small_width = -(-small_count // rows)
    small_flat = jnp.pad(small.reshape(-1), (0, small_width * rows - small_count))
    packed = jnp.concatenate(
        [inner_part, outer_part, small_flat.reshape(rows, small_width)], axis=1
    )
    packed = packed.reshape(devices, rows // devices, packed.shape[1]).astype(jnp.bfloat16)
    reduced = lax.all_to_all(packed, axes, 0, 0, tiled=True).astype(jnp.float32).sum(0)
    grad_proj = reduced[:, : 4 * width]
    small_part = reduced[:, 4 * width :].reshape(1, -1)
    small_all = lax.all_to_all(
        jnp.broadcast_to(small_part, (devices, small_part.shape[1])), axes, 0, 0, tiled=True
    )
    small_sum = small_all.reshape(-1)[:small_count]
    conv_sum = small_sum[: conv_term.size].reshape(conv_term.shape)
    gains_sum = small_sum[conv_term.size :].reshape(2, -1)
    return (grad_frames, grad_proj * grad_scale, conv_sum * grad_scale, gains_sum * grad_scale)


def solution(mesh):
    return jax.shard_map(
        per_device,
        mesh=mesh,
        in_specs=(P("dp", "tm", None), P("dp", "tm", None), P("dp"), P(), P(), P(), P()),
        out_specs=(P("dp", "tm", None), P(("dp", "tm"), None), P(), P()),
        check_vma=False,
    )
```

```python
import math

import jax
import jax.numpy as jnp
from jax import lax
from jax.sharding import PartitionSpec as P

HEADS = 8
HDIM = 64
KER = 31


epsilon = 1e-05
negative = -1e30


def padded_2(value, sides, width):
    for axis, dim in sides:
        size, length = (lax.axis_size(axis), value.shape[dim])
        up = [(i, (i + 1) % size) for i in range(size - 1)]
        down = [(j, i) for i, j in up]
        last = lax.slice_in_dim(value, length - width, length, axis=dim)
        first = lax.slice_in_dim(value, 0, width, axis=dim)
        before = lax.ppermute(last, axis, up)
        after = lax.ppermute(first, axis, down)
        value = jnp.concatenate([before, value, after], axis=dim)
    return value


def normalize(inputs, gain):
    centre = inputs - jnp.mean(inputs, axis=-1, keepdims=True)
    spread = jnp.mean(centre * centre, axis=-1, keepdims=True)
    return centre * lax.rsqrt(spread + epsilon) * gain


def split_heads(matrix):
    return matrix.reshape(matrix.shape[0], HEADS, HDIM)


def over_blocks(advance, carried, members):
    total_rows = members[0].shape[0]
    stride = math.gcd(total_rows, 1024)

    def one_block(block_index, inner_state):
        offset = block_index * stride
        sliced = tuple((lax.dynamic_slice_in_dim(member, offset, stride, 0) for member in members))
        return advance(inner_state, sliced, offset)

    return lax.fori_loop(0, total_rows // stride, one_block, carried)


def forward_step(query_heads, length, scaling):

    def advance(carried, sliced, first_row):
        key_heads = split_heads(sliced[0])
        value_heads = split_heads(sliced[1])
        positions = first_row + jnp.arange(key_heads.shape[0], dtype=jnp.int32)
        living = (positions < length)[None, None, :]
        scores = (
            jnp.einsum("bhd,lhd->hbl", query_heads, key_heads, preferred_element_type=jnp.float32)
            * scaling
        )
        scores = jnp.where(living, scores, negative)
        top_old, total_old, accumulated = carried
        top_new = jnp.maximum(top_old, jnp.max(scores, axis=-1))
        weights = jnp.where(living, jnp.exp(scores - top_new[:, :, None]), 0.0)
        fading = jnp.exp(top_old - top_new)
        total_new = total_old * fading + jnp.sum(weights, axis=-1)
        update = jnp.einsum(
            "hbl,lhd->bhd",
            weights.astype(jnp.bfloat16),
            value_heads,
            preferred_element_type=jnp.float32,
        )
        return (top_new, total_new, accumulated * fading.T[:, :, None] + update)

    return advance


def query_side(query_heads, grad_heads, logsum, delta, length, scaling):

    def advance(carried, sliced, first_row):
        key_heads = split_heads(sliced[0])
        value_heads = split_heads(sliced[1])
        count_here = key_heads.shape[0]
        positions = first_row + jnp.arange(count_here, dtype=jnp.int32)
        living = (positions < length)[None, None, :]
        scores = (
            jnp.einsum("bhd,lhd->hbl", query_heads, key_heads, preferred_element_type=jnp.float32)
            * scaling
        )
        scores = jnp.where(living, scores, negative)
        probs = jnp.where(living, jnp.exp(scores - logsum.T[:, :, None]), 0.0)
        dprobs = jnp.einsum(
            "bhd,lhd->hbl", grad_heads, value_heads, preferred_element_type=jnp.float32
        )
        grad_scores = (probs * (dprobs - delta.T[:, :, None])).astype(jnp.bfloat16)
        grad_query = (
            carried[0]
            + jnp.einsum("hbl,lhd->bhd", grad_scores, key_heads, preferred_element_type=jnp.float32)
            * scaling
        )
        return (grad_query,)

    return advance


def key_side(key_heads, value_heads, own_living, scaling):

    def advance(carried, sliced, first_row):
        query_heads = split_heads(sliced[0].astype(jnp.bfloat16))
        grad_heads = split_heads(sliced[1].astype(jnp.bfloat16))
        logsum_block = sliced[2]
        delta_block = sliced[3]
        scores = (
            jnp.einsum("bhd,lhd->hbl", query_heads, key_heads, preferred_element_type=jnp.float32)
            * scaling
        )
        scores = jnp.where(own_living, scores, negative)
        probs = jnp.where(own_living, jnp.exp(scores - logsum_block.T[:, :, None]), 0.0)
        dprobs = jnp.einsum(
            "bhd,lhd->hbl", grad_heads, value_heads, preferred_element_type=jnp.float32
        )
        grad_scores = (probs * (dprobs - delta_block.T[:, :, None])).astype(jnp.bfloat16)
        grad_key = (
            carried[0]
            + jnp.einsum(
                "hbl,bhd->lhd", grad_scores, query_heads, preferred_element_type=jnp.float32
            )
            * scaling
        )
        grad_value = carried[1] + jnp.einsum(
            "hbl,bhd->lhd",
            probs.astype(jnp.bfloat16),
            grad_heads,
            preferred_element_type=jnp.float32,
        )
        return (grad_key, grad_value)

    return advance


def per_device(frames, cotangent, lengths, w_proj, gain_attn, gain_conv, w_conv):
    frame_count = frames.shape[1]
    width = HEADS * HDIM
    cycle_size = lax.axis_size("tm")
    own_start = lax.axis_index("tm") * frame_count
    length = lengths[0]
    scaling = 1.0 / math.sqrt(HDIM)
    total_frames = lax.axis_size("dp") * frames.shape[0] * frame_count * cycle_size
    grad_scale = 1.0 / math.sqrt(total_frames)
    contract_last = (((1,), (1,)), ((), ()))
    contract_first = (((0,), (0,)), ((), ()))
    inputs = frames[0].astype(jnp.float32)
    normed_attn = normalize(inputs, gain_attn).astype(jnp.bfloat16)
    projected = jnp.dot(
        normed_attn, w_proj[:, : 3 * width], preferred_element_type=jnp.float32
    ).astype(jnp.bfloat16)
    tm_count = lax.axis_size("tm")
    halves = tm_count // HEADS
    me = lax.axis_index("tm")
    half = me // HEADS
    span = frame_count * HEADS
    total = frame_count * tm_count
    key_live = (jnp.arange(total, dtype=jnp.int32) < length)[None, :]
    half_live = lax.dynamic_slice_in_dim(key_live, half * span, span, 1)
    mine = (jnp.arange(halves) == half).reshape(halves, 1, 1, 1, 1)
    qkv = projected.reshape(frame_count, 3, HEADS, HDIM).transpose(2, 0, 1, 3)
    got = lax.all_to_all(jnp.tile(qkv, (halves, 1, 1, 1)), "tm", 0, 0, tiled=True)
    got = got.reshape(total, 3, HDIM)
    q_all, k_all, v_all = got[:, 0], got[:, 1], got[:, 2]
    q_half = lax.dynamic_slice_in_dim(q_all, half * span, span, 0)
    scores = lax.dot_general(q_half, k_all, contract_last, preferred_element_type=jnp.float32)
    scores = jnp.where(key_live, scores * scaling, negative)
    top = jnp.max(scores, axis=-1)
    weights = jnp.where(key_live, jnp.exp(scores - top[:, None]), 0.0)
    summed = jnp.sum(weights, axis=-1)
    acc = jnp.dot(weights.astype(jnp.bfloat16), v_all, preferred_element_type=jnp.float32)
    a_half = (acc / summed[:, None]).astype(jnp.bfloat16)
    lse_half = top + jnp.log(summed)

    def to_frames(rows):
        blocks = rows.reshape((1, HEADS, frame_count) + rows.shape[1:])
        placed = jnp.where(mine.reshape((halves,) + (1,) * (blocks.ndim - 1)), blocks, 0)
        placed = placed.reshape((tm_count, frame_count) + rows.shape[1:])
        back = lax.all_to_all(placed, "tm", 0, 0, tiled=True)
        back = back.reshape((halves, HEADS, frame_count) + rows.shape[1:])
        return jnp.sum(back.astype(jnp.float32), axis=0).astype(rows.dtype)

    attended = to_frames(a_half).transpose(1, 0, 2).reshape(frame_count, width)
    w_out = w_proj[:, 3 * width :]
    mixed = inputs + lax.dot_general(
        attended, w_out, contract_last, preferred_element_type=jnp.float32
    )
    resid_f = mixed.astype(jnp.bfloat16).astype(jnp.float32)
    positions = own_start + jnp.arange(frame_count, dtype=jnp.int32)
    valid = (positions < length)[:, None]
    normed_conv = jnp.where(valid, normalize(resid_f, gain_conv), 0.0).astype(jnp.bfloat16)
    reach = KER // 2
    padded = padded_2(normed_conv, (("tm", 0),), reach).astype(jnp.float32)
    kernel = w_conv.astype(jnp.float32)
    conv = jnp.zeros((frame_count, padded.shape[1]), jnp.float32)
    for shift_index in range(KER):
        conv = conv + kernel[shift_index] * padded[shift_index : shift_index + frame_count]
    upstream = cotangent[0].astype(jnp.float32)
    gate = jax.nn.sigmoid(conv)
    grad_conv_in = upstream * gate * (1.0 + conv * (1.0 - gate))
    conv_term = jnp.stack(
        [
            jnp.sum(grad_conv_in * padded[shift_index : shift_index + frame_count], axis=0)
            for shift_index in range(KER)
        ]
    )
    grad_padded = padded_2(grad_conv_in.astype(jnp.bfloat16), (("tm", 0),), reach).astype(
        grad_conv_in.dtype
    )
    grad_normed = jnp.zeros_like(grad_conv_in)
    for shift_index in range(KER):
        begin = 2 * reach - shift_index
        grad_normed = grad_normed + kernel[shift_index] * grad_padded[begin : begin + frame_count]
    grad_normed = jnp.where(valid, grad_normed, 0.0)
    unused_conv, pull_conv = jax.vjp(normalize, resid_f, gain_conv)
    back_resid, gain_conv_term = pull_conv(grad_normed)
    grad_resid = upstream + back_resid
    grad_resid_low = grad_resid.astype(jnp.bfloat16)
    grad_attended = jnp.dot(grad_resid_low, w_out, preferred_element_type=jnp.float32).astype(
        jnp.bfloat16
    )
    send_grad = grad_attended.reshape(frame_count, HEADS, HDIM).transpose(1, 0, 2)
    da_all = lax.all_to_all(jnp.tile(send_grad, (halves, 1, 1)), "tm", 0, 0, tiled=True)
    da_all = da_all.reshape(total, HDIM)
    da_half = lax.dynamic_slice_in_dim(da_all, half * span, span, 0)
    delta_half = jnp.sum(da_half.astype(jnp.float32) * a_half.astype(jnp.float32), axis=-1)
    stats_half = jnp.stack([lse_half, delta_half], axis=0)
    partner = lax.ppermute(
        stats_half, "tm", [(i, (i + HEADS) % tm_count) for i in range(tm_count)]
    )
    stats_all = jnp.where(
        half == 0,
        jnp.concatenate([stats_half, partner], axis=1),
        jnp.concatenate([partner, stats_half], axis=1),
    )
    lse_all = stats_all[0][:, None]
    delta_all = stats_all[1][:, None]
    scores = lax.dot_general(q_half, k_all, contract_last, preferred_element_type=jnp.float32)
    scores = jnp.where(key_live, scores * scaling, negative)
    probs = jnp.where(key_live, jnp.exp(scores - lse_half[:, None]), 0.0)
    dprobs = lax.dot_general(da_half, v_all, contract_last, preferred_element_type=jnp.float32)
    grad_scores = (probs * (dprobs - delta_half[:, None])).astype(jnp.bfloat16)
    grad_q = jnp.dot(grad_scores, k_all, preferred_element_type=jnp.float32) * scaling
    k_half = lax.dynamic_slice_in_dim(k_all, half * span, span, 0)
    v_half = lax.dynamic_slice_in_dim(v_all, half * span, span, 0)
    scores = lax.dot_general(q_all, k_half, contract_last, preferred_element_type=jnp.float32)
    scores = jnp.where(half_live, scores * scaling, negative)
    probs = jnp.where(half_live, jnp.exp(scores - lse_all), 0.0)
    dprobs = lax.dot_general(da_all, v_half, contract_last, preferred_element_type=jnp.float32)
    grad_scores = (probs * (dprobs - delta_all)).astype(jnp.bfloat16)
    grad_k = (
        lax.dot_general(grad_scores, q_all, contract_first, preferred_element_type=jnp.float32)
        * scaling
    )
    grad_v = lax.dot_general(
        probs.astype(jnp.bfloat16), da_all, contract_first, preferred_element_type=jnp.float32
    )
    grad_rows = jnp.stack([grad_q, grad_k, grad_v], axis=1).astype(jnp.bfloat16)
    grad_qkv = to_frames(grad_rows).transpose(1, 2, 0, 3).reshape(frame_count, 3 * width)
    back_normed = lax.dot_general(
        grad_qkv, w_proj[:, : 3 * width], contract_last, preferred_element_type=jnp.float32
    )
    unused_attn, pull_attn = jax.vjp(normalize, inputs, gain_attn)
    back_inputs, gain_attn_term = pull_attn(back_normed)
    grad_frames = (grad_resid + back_inputs).astype(jnp.bfloat16)[None]
    inner_part = lax.dot_general(
        normed_attn, grad_qkv, contract_first, preferred_element_type=jnp.float32
    )
    outer_part = lax.dot_general(
        grad_resid_low, attended, contract_first, preferred_element_type=jnp.float32
    )
    axes = ("dp", "tm")
    devices = lax.axis_size(axes)
    rows = inner_part.shape[0]
    small = jnp.concatenate([conv_term, gain_attn_term[None], gain_conv_term[None]], axis=0)
    small_count = small.size
    small_width = -(-small_count // rows)
    small_flat = jnp.pad(small.reshape(-1), (0, small_width * rows - small_count))
    packed = jnp.concatenate(
        [inner_part, outer_part, small_flat.reshape(rows, small_width)], axis=1
    )
    outer_count = lax.axis_size("dp")
    packed = packed.reshape(outer_count, tm_count, rows // devices, packed.shape[1])
    packed = packed.transpose(1, 0, 2, 3).astype(jnp.bfloat16)
    reduced = lax.all_to_all(packed, "tm", 0, 0, tiled=True).astype(jnp.float32).sum(0)
    reduced = lax.all_to_all(reduced.astype(jnp.bfloat16), "dp", 0, 0, tiled=True)
    reduced = reduced.astype(jnp.float32).sum(0)
    grad_proj = reduced[:, : 4 * width]
    small_part = reduced[:, 4 * width :].reshape(1, -1)
    small_all = lax.all_to_all(
        jnp.broadcast_to(small_part, (devices, small_part.shape[1])), axes, 0, 0, tiled=True
    )
    small_sum = small_all.reshape(-1)[:small_count]
    conv_sum = small_sum[: conv_term.size].reshape(conv_term.shape)
    gains_sum = small_sum[conv_term.size :].reshape(2, -1)
    return (grad_frames, grad_proj * grad_scale, conv_sum * grad_scale, gains_sum * grad_scale)


def solution(mesh):
    return jax.shard_map(
        per_device,
        mesh=mesh,
        in_specs=(P("dp", "tm", None), P("dp", "tm", None), P("dp"), P(), P(), P(), P()),
        out_specs=(P("dp", "tm", None), P(("dp", "tm"), None), P(), P()),
        check_vma=False,
    )
```

```python
import math

import jax
import jax.numpy as jnp
from jax import lax
from jax.sharding import PartitionSpec as P

HEADS = 8
HDIM = 64
KER = 31


epsilon = 1e-05
negative = -1e30


def padded_2(value, sides, width):
    for axis, dim in sides:
        size, length = (lax.axis_size(axis), value.shape[dim])
        up = [(i, (i + 1) % size) for i in range(size - 1)]
        down = [(j, i) for i, j in up]
        last = lax.slice_in_dim(value, length - width, length, axis=dim)
        first = lax.slice_in_dim(value, 0, width, axis=dim)
        before = lax.ppermute(last, axis, up)
        after = lax.ppermute(first, axis, down)
        value = jnp.concatenate([before, value, after], axis=dim)
    return value


def normalize(inputs, gain):
    centre = inputs - jnp.mean(inputs, axis=-1, keepdims=True)
    spread = jnp.mean(centre * centre, axis=-1, keepdims=True)
    return centre * lax.rsqrt(spread + epsilon) * gain


def split_heads(matrix):
    return matrix.reshape(matrix.shape[0], HEADS, HDIM)


def over_blocks(advance, carried, members):
    total_rows = members[0].shape[0]
    stride = math.gcd(total_rows, 1024)

    def one_block(block_index, inner_state):
        offset = block_index * stride
        sliced = tuple((lax.dynamic_slice_in_dim(member, offset, stride, 0) for member in members))
        return advance(inner_state, sliced, offset)

    return lax.fori_loop(0, total_rows // stride, one_block, carried)


def forward_step(query_heads, length, scaling):

    def advance(carried, sliced, first_row):
        key_heads = split_heads(sliced[0])
        value_heads = split_heads(sliced[1])
        positions = first_row + jnp.arange(key_heads.shape[0], dtype=jnp.int32)
        living = (positions < length)[None, None, :]
        scores = (
            jnp.einsum("bhd,lhd->hbl", query_heads, key_heads, preferred_element_type=jnp.float32)
            * scaling
        )
        scores = jnp.where(living, scores, negative)
        top_old, total_old, accumulated = carried
        top_new = jnp.maximum(top_old, jnp.max(scores, axis=-1))
        weights = jnp.where(living, jnp.exp(scores - top_new[:, :, None]), 0.0)
        fading = jnp.exp(top_old - top_new)
        total_new = total_old * fading + jnp.sum(weights, axis=-1)
        update = jnp.einsum(
            "hbl,lhd->bhd",
            weights.astype(jnp.bfloat16),
            value_heads,
            preferred_element_type=jnp.float32,
        )
        return (top_new, total_new, accumulated * fading.T[:, :, None] + update)

    return advance


def query_side(query_heads, grad_heads, logsum, delta, length, scaling):

    def advance(carried, sliced, first_row):
        key_heads = split_heads(sliced[0])
        value_heads = split_heads(sliced[1])
        count_here = key_heads.shape[0]
        positions = first_row + jnp.arange(count_here, dtype=jnp.int32)
        living = (positions < length)[None, None, :]
        scores = (
            jnp.einsum("bhd,lhd->hbl", query_heads, key_heads, preferred_element_type=jnp.float32)
            * scaling
        )
        scores = jnp.where(living, scores, negative)
        probs = jnp.where(living, jnp.exp(scores - logsum.T[:, :, None]), 0.0)
        dprobs = jnp.einsum(
            "bhd,lhd->hbl", grad_heads, value_heads, preferred_element_type=jnp.float32
        )
        grad_scores = (probs * (dprobs - delta.T[:, :, None])).astype(jnp.bfloat16)
        grad_query = (
            carried[0]
            + jnp.einsum("hbl,lhd->bhd", grad_scores, key_heads, preferred_element_type=jnp.float32)
            * scaling
        )
        return (grad_query,)

    return advance


def key_side(key_heads, value_heads, own_living, scaling):

    def advance(carried, sliced, first_row):
        query_heads = split_heads(sliced[0].astype(jnp.bfloat16))
        grad_heads = split_heads(sliced[1].astype(jnp.bfloat16))
        logsum_block = sliced[2]
        delta_block = sliced[3]
        scores = (
            jnp.einsum("bhd,lhd->hbl", query_heads, key_heads, preferred_element_type=jnp.float32)
            * scaling
        )
        scores = jnp.where(own_living, scores, negative)
        probs = jnp.where(own_living, jnp.exp(scores - logsum_block.T[:, :, None]), 0.0)
        dprobs = jnp.einsum(
            "bhd,lhd->hbl", grad_heads, value_heads, preferred_element_type=jnp.float32
        )
        grad_scores = (probs * (dprobs - delta_block.T[:, :, None])).astype(jnp.bfloat16)
        grad_key = (
            carried[0]
            + jnp.einsum(
                "hbl,bhd->lhd", grad_scores, query_heads, preferred_element_type=jnp.float32
            )
            * scaling
        )
        grad_value = carried[1] + jnp.einsum(
            "hbl,bhd->lhd",
            probs.astype(jnp.bfloat16),
            grad_heads,
            preferred_element_type=jnp.float32,
        )
        return (grad_key, grad_value)

    return advance


def per_device(frames, cotangent, lengths, w_proj, gain_attn, gain_conv, w_conv):
    frame_count = frames.shape[1]
    width = HEADS * HDIM
    cycle_size = lax.axis_size("tm")
    own_start = lax.axis_index("tm") * frame_count
    length = lengths[0]
    scaling = 1.0 / math.sqrt(HDIM)
    total_frames = lax.axis_size("dp") * frames.shape[0] * frame_count * cycle_size
    grad_scale = 1.0 / math.sqrt(total_frames)
    contract_last = (((1,), (1,)), ((), ()))
    contract_first = (((0,), (0,)), ((), ()))
    inputs = frames[0].astype(jnp.float32)
    normed_attn = normalize(inputs, gain_attn).astype(jnp.bfloat16)
    projected = jnp.dot(
        normed_attn, w_proj[:, : 3 * width], preferred_element_type=jnp.float32
    ).astype(jnp.bfloat16)
    tm_count = lax.axis_size("tm")
    halves = tm_count // HEADS
    me = lax.axis_index("tm")
    half = me // HEADS
    span = frame_count * HEADS
    total = frame_count * tm_count
    key_live = (jnp.arange(total, dtype=jnp.int32) < length)[None, :]
    half_live = lax.dynamic_slice_in_dim(key_live, half * span, span, 1)
    mine = (jnp.arange(halves) == half).reshape(halves, 1, 1, 1, 1)
    qkv = projected.reshape(frame_count, 3, HEADS, HDIM).transpose(2, 0, 1, 3)
    got = lax.all_to_all(jnp.tile(qkv, (halves, 1, 1, 1)), "tm", 0, 0, tiled=True)
    got = got.reshape(total, 3, HDIM)
    q_all, k_all, v_all = got[:, 0], got[:, 1], got[:, 2]
    q_half = lax.dynamic_slice_in_dim(q_all, half * span, span, 0)
    scores = lax.dot_general(q_half, k_all, contract_last, preferred_element_type=jnp.float32)
    scores = jnp.where(key_live, scores * scaling, negative)
    top = jnp.max(scores, axis=-1)
    weights = jnp.where(key_live, jnp.exp(scores - top[:, None]), 0.0)
    summed = jnp.sum(weights, axis=-1)
    acc = jnp.dot(weights.astype(jnp.bfloat16), v_all, preferred_element_type=jnp.float32)
    a_half = (acc / summed[:, None]).astype(jnp.bfloat16)
    lse_half = top + jnp.log(summed)

    def to_frames(rows):
        blocks = rows.reshape((1, HEADS, frame_count) + rows.shape[1:])
        placed = jnp.where(mine.reshape((halves,) + (1,) * (blocks.ndim - 1)), blocks, 0)
        placed = placed.reshape((tm_count, frame_count) + rows.shape[1:])
        back = lax.all_to_all(placed, "tm", 0, 0, tiled=True)
        back = back.reshape((halves, HEADS, frame_count) + rows.shape[1:])
        return jnp.sum(back.astype(jnp.float32), axis=0).astype(rows.dtype)

    attended = to_frames(a_half).transpose(1, 0, 2).reshape(frame_count, width)
    w_out = w_proj[:, 3 * width :]
    mixed = inputs + lax.dot_general(
        attended, w_out, contract_last, preferred_element_type=jnp.float32
    )
    resid_f = mixed.astype(jnp.bfloat16).astype(jnp.float32)
    positions = own_start + jnp.arange(frame_count, dtype=jnp.int32)
    valid = (positions < length)[:, None]
    normed_conv = jnp.where(valid, normalize(resid_f, gain_conv), 0.0).astype(jnp.bfloat16)
    reach = KER // 2
    padded = padded_2(normed_conv, (("tm", 0),), reach).astype(jnp.float32)
    kernel = w_conv.astype(jnp.float32)
    conv = jnp.zeros((frame_count, padded.shape[1]), jnp.float32)
    for shift_index in range(KER):
        conv = conv + kernel[shift_index] * padded[shift_index : shift_index + frame_count]
    upstream = cotangent[0].astype(jnp.float32)
    gate = jax.nn.sigmoid(conv)
    grad_conv_in = upstream * gate * (1.0 + conv * (1.0 - gate))
    conv_term = jnp.stack(
        [
            jnp.sum(grad_conv_in * padded[shift_index : shift_index + frame_count], axis=0)
            for shift_index in range(KER)
        ]
    )
    grad_padded = padded_2(grad_conv_in.astype(jnp.bfloat16), (("tm", 0),), reach).astype(
        grad_conv_in.dtype
    )
    grad_normed = jnp.zeros_like(grad_conv_in)
    for shift_index in range(KER):
        begin = 2 * reach - shift_index
        grad_normed = grad_normed + kernel[shift_index] * grad_padded[begin : begin + frame_count]
    grad_normed = jnp.where(valid, grad_normed, 0.0)
    unused_conv, pull_conv = jax.vjp(normalize, resid_f, gain_conv)
    back_resid, gain_conv_term = pull_conv(grad_normed)
    grad_resid = upstream + back_resid
    grad_resid_low = grad_resid.astype(jnp.bfloat16)
    grad_attended = jnp.dot(grad_resid_low, w_out, preferred_element_type=jnp.float32).astype(
        jnp.bfloat16
    )
    send_grad = grad_attended.reshape(frame_count, HEADS, HDIM).transpose(1, 0, 2)
    da_all = lax.all_to_all(jnp.tile(send_grad, (halves, 1, 1)), "tm", 0, 0, tiled=True)
    da_all = da_all.reshape(total, HDIM)
    da_half = lax.dynamic_slice_in_dim(da_all, half * span, span, 0)
    delta_half = jnp.sum(da_half.astype(jnp.float32) * a_half.astype(jnp.float32), axis=-1)
    stats_half = jnp.stack([lse_half, delta_half], axis=0)
    partner = lax.ppermute(
        stats_half, "tm", [(i, (i + HEADS) % tm_count) for i in range(tm_count)]
    )
    stats_all = jnp.where(
        half == 0,
        jnp.concatenate([stats_half, partner], axis=1),
        jnp.concatenate([partner, stats_half], axis=1),
    )
    lse_all = stats_all[0][:, None]
    delta_all = stats_all[1][:, None]
    scores = lax.dot_general(q_half, k_all, contract_last, preferred_element_type=jnp.float32)
    scores = jnp.where(key_live, scores * scaling, negative)
    probs = jnp.where(key_live, jnp.exp(scores - lse_half[:, None]), 0.0)
    dprobs = lax.dot_general(da_half, v_all, contract_last, preferred_element_type=jnp.float32)
    grad_scores = (probs * (dprobs - delta_half[:, None])).astype(jnp.bfloat16)
    grad_q = jnp.dot(grad_scores, k_all, preferred_element_type=jnp.float32) * scaling
    k_half = lax.dynamic_slice_in_dim(k_all, half * span, span, 0)
    v_half = lax.dynamic_slice_in_dim(v_all, half * span, span, 0)
    scores = lax.dot_general(q_all, k_half, contract_last, preferred_element_type=jnp.float32)
    scores = jnp.where(half_live, scores * scaling, negative)
    probs = jnp.where(half_live, jnp.exp(scores - lse_all), 0.0)
    dprobs = lax.dot_general(da_all, v_half, contract_last, preferred_element_type=jnp.float32)
    grad_scores = (probs * (dprobs - delta_all)).astype(jnp.bfloat16)
    grad_k = (
        lax.dot_general(grad_scores, q_all, contract_first, preferred_element_type=jnp.float32)
        * scaling
    )
    grad_v = lax.dot_general(
        probs.astype(jnp.bfloat16), da_all, contract_first, preferred_element_type=jnp.float32
    )
    grad_rows = jnp.stack([grad_q, grad_k, grad_v], axis=1).astype(jnp.bfloat16)
    grad_qkv = to_frames(grad_rows).transpose(1, 2, 0, 3).reshape(frame_count, 3 * width)
    back_normed = lax.dot_general(
        grad_qkv, w_proj[:, : 3 * width], contract_last, preferred_element_type=jnp.float32
    )
    unused_attn, pull_attn = jax.vjp(normalize, inputs, gain_attn)
    back_inputs, gain_attn_term = pull_attn(back_normed)
    grad_frames = (grad_resid + back_inputs).astype(jnp.bfloat16)[None]
    inner_part = lax.dot_general(
        normed_attn, grad_qkv, contract_first, preferred_element_type=jnp.float32
    )
    outer_part = lax.dot_general(
        grad_resid_low, attended, contract_first, preferred_element_type=jnp.float32
    )
    axes = ("dp", "tm")
    devices = lax.axis_size(axes)
    dp_count = lax.axis_size("dp")
    rows = inner_part.shape[0]
    rows_per = rows // devices

    def two_parts(value):
        high = value.astype(jnp.bfloat16)
        low = (value - high.astype(jnp.float32)).astype(jnp.bfloat16)
        return jnp.concatenate([high, low])

    def one_part(pair):
        half_size = pair.shape[0] // 2
        return pair[:half_size] + pair[half_size:]

    def reduce_rows(matrix, extra):
        cols = matrix.shape[1]
        body_size = dp_count * rows_per * cols
        chunks = matrix.reshape(dp_count, tm_count, rows_per, cols).transpose(1, 0, 2, 3)
        chunks = chunks.reshape(tm_count, body_size).astype(jnp.bfloat16)
        if extra is not None:
            chunks = jnp.concatenate(
                [chunks, jnp.broadcast_to(two_parts(extra), (tm_count, 2 * extra.size))], axis=1
            )
        got = lax.all_to_all(chunks, "tm", 0, 0, tiled=True).astype(jnp.float32).sum(0)
        body = got[:body_size].reshape(dp_count, rows_per * cols).astype(jnp.bfloat16)
        if extra is not None:
            partial = one_part(got[body_size:])
            body = jnp.concatenate(
                [body, jnp.broadcast_to(two_parts(partial), (dp_count, 2 * extra.size))], axis=1
            )
        got = lax.all_to_all(body, "dp", 0, 0, tiled=True).astype(jnp.float32).sum(0)
        result = got[: rows_per * cols].reshape(rows_per, cols)
        return result, (one_part(got[rows_per * cols :]) if extra is not None else None)

    small = jnp.concatenate([conv_term, gain_conv_term[None]], axis=0)
    small_count = small.size
    small_width = -(-small_count // rows)
    small_flat = jnp.pad(small.reshape(-1), (0, small_width * rows - small_count))
    early = jnp.concatenate([outer_part, small_flat.reshape(rows, small_width)], axis=1)
    early_sum, unused = reduce_rows(early, None)
    small_part = early_sum[:, width:].reshape(1, -1)
    small_all = lax.all_to_all(
        jnp.broadcast_to(small_part, (devices, small_part.shape[1])), axes, 0, 0, tiled=True
    )
    small_sum = small_all.reshape(-1)[:small_count]
    conv_sum = small_sum[: conv_term.size].reshape(conv_term.shape)
    gain_conv_sum = small_sum[conv_term.size :]
    inner_sum, gain_attn_sum = reduce_rows(inner_part, gain_attn_term)
    grad_proj = jnp.concatenate([inner_sum, early_sum[:, :width]], axis=1)
    gains_sum = jnp.stack([gain_attn_sum, gain_conv_sum])
    return (grad_frames, grad_proj * grad_scale, conv_sum * grad_scale, gains_sum * grad_scale)


def solution(mesh):
    return jax.shard_map(
        per_device,
        mesh=mesh,
        in_specs=(P("dp", "tm", None), P("dp", "tm", None), P("dp"), P(), P(), P(), P()),
        out_specs=(P("dp", "tm", None), P(("dp", "tm"), None), P(), P()),
        check_vma=False,
    )
```

```python
import math

import jax
import jax.numpy as jnp
from jax import lax
from jax.sharding import PartitionSpec as P

HEADS = 8
HDIM = 64
KER = 31


epsilon = 1e-05
negative = -1e30


def padded_2(value, sides, width):
    for axis, dim in sides:
        size, length = (lax.axis_size(axis), value.shape[dim])
        up = [(i, (i + 1) % size) for i in range(size - 1)]
        down = [(j, i) for i, j in up]
        last = lax.slice_in_dim(value, length - width, length, axis=dim)
        first = lax.slice_in_dim(value, 0, width, axis=dim)
        before = lax.ppermute(last, axis, up)
        after = lax.ppermute(first, axis, down)
        value = jnp.concatenate([before, value, after], axis=dim)
    return value


def normalize(inputs, gain):
    centre = inputs - jnp.mean(inputs, axis=-1, keepdims=True)
    spread = jnp.mean(centre * centre, axis=-1, keepdims=True)
    return centre * lax.rsqrt(spread + epsilon) * gain


def split_heads(matrix):
    return matrix.reshape(matrix.shape[0], HEADS, HDIM)


def over_blocks(advance, carried, members):
    total_rows = members[0].shape[0]
    stride = math.gcd(total_rows, 1024)

    def one_block(block_index, inner_state):
        offset = block_index * stride
        sliced = tuple((lax.dynamic_slice_in_dim(member, offset, stride, 0) for member in members))
        return advance(inner_state, sliced, offset)

    return lax.fori_loop(0, total_rows // stride, one_block, carried)


def forward_step(query_heads, length, scaling):

    def advance(carried, sliced, first_row):
        key_heads = split_heads(sliced[0])
        value_heads = split_heads(sliced[1])
        positions = first_row + jnp.arange(key_heads.shape[0], dtype=jnp.int32)
        living = (positions < length)[None, None, :]
        scores = (
            jnp.einsum("bhd,lhd->hbl", query_heads, key_heads, preferred_element_type=jnp.float32)
            * scaling
        )
        scores = jnp.where(living, scores, negative)
        top_old, total_old, accumulated = carried
        top_new = jnp.maximum(top_old, jnp.max(scores, axis=-1))
        weights = jnp.where(living, jnp.exp(scores - top_new[:, :, None]), 0.0)
        fading = jnp.exp(top_old - top_new)
        total_new = total_old * fading + jnp.sum(weights, axis=-1)
        update = jnp.einsum(
            "hbl,lhd->bhd",
            weights.astype(jnp.bfloat16),
            value_heads,
            preferred_element_type=jnp.float32,
        )
        return (top_new, total_new, accumulated * fading.T[:, :, None] + update)

    return advance


def query_side(query_heads, grad_heads, logsum, delta, length, scaling):

    def advance(carried, sliced, first_row):
        key_heads = split_heads(sliced[0])
        value_heads = split_heads(sliced[1])
        count_here = key_heads.shape[0]
        positions = first_row + jnp.arange(count_here, dtype=jnp.int32)
        living = (positions < length)[None, None, :]
        scores = (
            jnp.einsum("bhd,lhd->hbl", query_heads, key_heads, preferred_element_type=jnp.float32)
            * scaling
        )
        scores = jnp.where(living, scores, negative)
        probs = jnp.where(living, jnp.exp(scores - logsum.T[:, :, None]), 0.0)
        dprobs = jnp.einsum(
            "bhd,lhd->hbl", grad_heads, value_heads, preferred_element_type=jnp.float32
        )
        grad_scores = (probs * (dprobs - delta.T[:, :, None])).astype(jnp.bfloat16)
        grad_query = (
            carried[0]
            + jnp.einsum("hbl,lhd->bhd", grad_scores, key_heads, preferred_element_type=jnp.float32)
            * scaling
        )
        return (grad_query,)

    return advance


def key_side(key_heads, value_heads, own_living, scaling):

    def advance(carried, sliced, first_row):
        query_heads = split_heads(sliced[0].astype(jnp.bfloat16))
        grad_heads = split_heads(sliced[1].astype(jnp.bfloat16))
        logsum_block = sliced[2]
        delta_block = sliced[3]
        scores = (
            jnp.einsum("bhd,lhd->hbl", query_heads, key_heads, preferred_element_type=jnp.float32)
            * scaling
        )
        scores = jnp.where(own_living, scores, negative)
        probs = jnp.where(own_living, jnp.exp(scores - logsum_block.T[:, :, None]), 0.0)
        dprobs = jnp.einsum(
            "bhd,lhd->hbl", grad_heads, value_heads, preferred_element_type=jnp.float32
        )
        grad_scores = (probs * (dprobs - delta_block.T[:, :, None])).astype(jnp.bfloat16)
        grad_key = (
            carried[0]
            + jnp.einsum(
                "hbl,bhd->lhd", grad_scores, query_heads, preferred_element_type=jnp.float32
            )
            * scaling
        )
        grad_value = carried[1] + jnp.einsum(
            "hbl,bhd->lhd",
            probs.astype(jnp.bfloat16),
            grad_heads,
            preferred_element_type=jnp.float32,
        )
        return (grad_key, grad_value)

    return advance


def per_device(frames, cotangent, lengths, w_proj, gain_attn, gain_conv, w_conv):
    frame_count = frames.shape[1]
    width = HEADS * HDIM
    cycle_size = lax.axis_size("tm")
    own_start = lax.axis_index("tm") * frame_count
    length = lengths[0]
    scaling = 1.0 / math.sqrt(HDIM)
    total_frames = lax.axis_size("dp") * frames.shape[0] * frame_count * cycle_size
    grad_scale = 1.0 / math.sqrt(total_frames)
    contract_last = (((1,), (1,)), ((), ()))
    contract_first = (((0,), (0,)), ((), ()))
    inputs = frames[0].astype(jnp.float32)
    normed_attn = normalize(inputs, gain_attn).astype(jnp.bfloat16)
    projected = jnp.dot(
        normed_attn, w_proj[:, : 3 * width], preferred_element_type=jnp.float32
    ).astype(jnp.bfloat16)
    tm_count = lax.axis_size("tm")
    halves = tm_count // HEADS
    me = lax.axis_index("tm")
    half = me // HEADS
    span = frame_count * HEADS
    total = frame_count * tm_count
    key_live = (jnp.arange(total, dtype=jnp.int32) < length)[None, :]
    half_live = lax.dynamic_slice_in_dim(key_live, half * span, span, 1)
    mine = (jnp.arange(halves) == half).reshape(halves, 1, 1, 1, 1)
    qkv = projected.reshape(frame_count, 3, HEADS, HDIM).transpose(2, 0, 1, 3)
    got = lax.all_to_all(jnp.tile(qkv, (halves, 1, 1, 1)), "tm", 0, 0, tiled=True)
    got = got.reshape(total, 3, HDIM)
    q_all, k_all, v_all = got[:, 0], got[:, 1], got[:, 2]
    q_half = lax.dynamic_slice_in_dim(q_all, half * span, span, 0)
    scores = lax.dot_general(q_half, k_all, contract_last, preferred_element_type=jnp.float32)
    scores = jnp.where(key_live, scores * scaling, negative)
    top = jnp.max(scores, axis=-1)
    weights = jnp.where(key_live, jnp.exp(scores - top[:, None]), 0.0)
    summed = jnp.sum(weights, axis=-1)
    acc = jnp.dot(weights.astype(jnp.bfloat16), v_all, preferred_element_type=jnp.float32)
    a_half = (acc / summed[:, None]).astype(jnp.bfloat16)
    lse_half = top + jnp.log(summed)

    def to_frames(rows):
        blocks = rows.reshape((1, HEADS, frame_count) + rows.shape[1:])
        placed = jnp.where(mine.reshape((halves,) + (1,) * (blocks.ndim - 1)), blocks, 0)
        placed = placed.reshape((tm_count, frame_count) + rows.shape[1:])
        back = lax.all_to_all(placed, "tm", 0, 0, tiled=True)
        back = back.reshape((halves, HEADS, frame_count) + rows.shape[1:])
        return jnp.sum(back.astype(jnp.float32), axis=0).astype(rows.dtype)

    attended = to_frames(a_half).transpose(1, 0, 2).reshape(frame_count, width)
    w_out = w_proj[:, 3 * width :]
    mixed = inputs + lax.dot_general(
        attended, w_out, contract_last, preferred_element_type=jnp.float32
    )
    resid_f = mixed.astype(jnp.bfloat16).astype(jnp.float32)
    positions = own_start + jnp.arange(frame_count, dtype=jnp.int32)
    valid = (positions < length)[:, None]
    normed_conv = jnp.where(valid, normalize(resid_f, gain_conv), 0.0).astype(jnp.bfloat16)
    reach = KER // 2
    padded = padded_2(normed_conv, (("tm", 0),), reach).astype(jnp.float32)
    kernel = w_conv.astype(jnp.float32)
    conv = jnp.zeros((frame_count, padded.shape[1]), jnp.float32)
    for shift_index in range(KER):
        conv = conv + kernel[shift_index] * padded[shift_index : shift_index + frame_count]
    upstream = cotangent[0].astype(jnp.float32)
    gate = jax.nn.sigmoid(conv)
    grad_conv_in = upstream * gate * (1.0 + conv * (1.0 - gate))
    conv_term = jnp.stack(
        [
            jnp.sum(grad_conv_in * padded[shift_index : shift_index + frame_count], axis=0)
            for shift_index in range(KER)
        ]
    )
    grad_padded = padded_2(grad_conv_in.astype(jnp.bfloat16), (("tm", 0),), reach).astype(
        grad_conv_in.dtype
    )
    grad_normed = jnp.zeros_like(grad_conv_in)
    for shift_index in range(KER):
        begin = 2 * reach - shift_index
        grad_normed = grad_normed + kernel[shift_index] * grad_padded[begin : begin + frame_count]
    grad_normed = jnp.where(valid, grad_normed, 0.0)
    unused_conv, pull_conv = jax.vjp(normalize, resid_f, gain_conv)
    back_resid, gain_conv_term = pull_conv(grad_normed)
    grad_resid = upstream + back_resid
    grad_resid_low = grad_resid.astype(jnp.bfloat16)
    grad_attended = jnp.dot(grad_resid_low, w_out, preferred_element_type=jnp.float32).astype(
        jnp.bfloat16
    )
    send_grad = grad_attended.reshape(frame_count, HEADS, HDIM).transpose(1, 0, 2)
    da_all = lax.all_to_all(jnp.tile(send_grad, (halves, 1, 1)), "tm", 0, 0, tiled=True)
    da_all = da_all.reshape(total, HDIM)
    da_half = lax.dynamic_slice_in_dim(da_all, half * span, span, 0)
    delta_half = jnp.sum(da_half.astype(jnp.float32) * a_half.astype(jnp.float32), axis=-1)
    stats_half = jnp.stack([lse_half, delta_half], axis=0)
    partner = lax.ppermute(
        stats_half, "tm", [(i, (i + HEADS) % tm_count) for i in range(tm_count)]
    )
    stats_all = jnp.where(
        half == 0,
        jnp.concatenate([stats_half, partner], axis=1),
        jnp.concatenate([partner, stats_half], axis=1),
    )
    lse_all = stats_all[0][:, None]
    delta_all = stats_all[1][:, None]
    scores = lax.dot_general(q_half, k_all, contract_last, preferred_element_type=jnp.float32)
    scores = jnp.where(key_live, scores * scaling, negative)
    probs = jnp.where(key_live, jnp.exp(scores - lse_half[:, None]), 0.0)
    dprobs = lax.dot_general(da_half, v_all, contract_last, preferred_element_type=jnp.float32)
    grad_scores = (probs * (dprobs - delta_half[:, None])).astype(jnp.bfloat16)
    grad_q = jnp.dot(grad_scores, k_all, preferred_element_type=jnp.float32) * scaling
    k_half = lax.dynamic_slice_in_dim(k_all, half * span, span, 0)
    v_half = lax.dynamic_slice_in_dim(v_all, half * span, span, 0)
    scores = lax.dot_general(q_all, k_half, contract_last, preferred_element_type=jnp.float32)
    scores = jnp.where(half_live, scores * scaling, negative)
    probs = jnp.where(half_live, jnp.exp(scores - lse_all), 0.0)
    dprobs = lax.dot_general(da_all, v_half, contract_last, preferred_element_type=jnp.float32)
    grad_scores = (probs * (dprobs - delta_all)).astype(jnp.bfloat16)
    grad_k = (
        lax.dot_general(grad_scores, q_all, contract_first, preferred_element_type=jnp.float32)
        * scaling
    )
    grad_v = lax.dot_general(
        probs.astype(jnp.bfloat16), da_all, contract_first, preferred_element_type=jnp.float32
    )
    grad_rows = jnp.stack([grad_q, grad_k, grad_v], axis=1).astype(jnp.bfloat16)
    grad_qkv = to_frames(grad_rows).transpose(1, 2, 0, 3).reshape(frame_count, 3 * width)
    back_normed = lax.dot_general(
        grad_qkv, w_proj[:, : 3 * width], contract_last, preferred_element_type=jnp.float32
    )
    unused_attn, pull_attn = jax.vjp(normalize, inputs, gain_attn)
    back_inputs, gain_attn_term = pull_attn(back_normed)
    grad_frames = (grad_resid + back_inputs).astype(jnp.bfloat16)[None]
    inner_part = lax.dot_general(
        normed_attn, grad_qkv, contract_first, preferred_element_type=jnp.float32
    )
    outer_part = lax.dot_general(
        grad_resid_low, attended, contract_first, preferred_element_type=jnp.float32
    )
    axes = ("dp", "tm")
    devices = lax.axis_size(axes)
    rows = inner_part.shape[0]
    small = jnp.concatenate([conv_term, gain_attn_term[None], gain_conv_term[None]], axis=0)
    small_count = small.size
    small_width = -(-small_count // rows)
    small_flat = jnp.pad(small.reshape(-1), (0, small_width * rows - small_count))
    packed = jnp.concatenate(
        [inner_part, outer_part, small_flat.reshape(rows, small_width)], axis=1
    )
    outer_count = lax.axis_size("dp")
    cores = 2
    chips = tm_count // cores
    pairs = [[cores * k + c for c in range(cores)] for k in range(chips)]
    same_core = [[cores * k + c for k in range(chips)] for c in range(cores)]
    cols = packed.shape[1]
    packed = packed.reshape(outer_count, chips, cores, rows // devices, cols)
    packed = packed.transpose(2, 0, 1, 3, 4).astype(jnp.bfloat16)
    reduced = lax.all_to_all(packed, "tm", 0, 0, tiled=True, axis_index_groups=pairs)
    reduced = reduced.astype(jnp.float32).sum(0).transpose(1, 0, 2, 3).astype(jnp.bfloat16)
    reduced = lax.all_to_all(reduced, "tm", 0, 0, tiled=True, axis_index_groups=same_core)
    reduced = reduced.astype(jnp.float32).sum(0).astype(jnp.bfloat16)
    reduced = lax.all_to_all(reduced, "dp", 0, 0, tiled=True)
    reduced = reduced.astype(jnp.float32).sum(0)
    grad_proj = reduced[:, : 4 * width]
    small_part = reduced[:, 4 * width :].reshape(1, -1)
    small_all = lax.all_to_all(
        jnp.broadcast_to(small_part, (devices, small_part.shape[1])), axes, 0, 0, tiled=True
    )
    small_sum = small_all.reshape(-1)[:small_count]
    conv_sum = small_sum[: conv_term.size].reshape(conv_term.shape)
    gains_sum = small_sum[conv_term.size :].reshape(2, -1)
    return (grad_frames, grad_proj * grad_scale, conv_sum * grad_scale, gains_sum * grad_scale)


def solution(mesh):
    return jax.shard_map(
        per_device,
        mesh=mesh,
        in_specs=(P("dp", "tm", None), P("dp", "tm", None), P("dp"), P(), P(), P(), P()),
        out_specs=(P("dp", "tm", None), P(("dp", "tm"), None), P(), P()),
        check_vma=False,
    )
```

```python
import math

import jax
import jax.numpy as jnp
from jax import lax
from jax.sharding import PartitionSpec as P

HEADS = 8
HDIM = 64
KER = 31


epsilon = 1e-05
negative = -1e30


def padded_2(value, sides, width):
    for axis, dim in sides:
        size, length = (lax.axis_size(axis), value.shape[dim])
        up = [(i, (i + 1) % size) for i in range(size - 1)]
        down = [(j, i) for i, j in up]
        last = lax.slice_in_dim(value, length - width, length, axis=dim)
        first = lax.slice_in_dim(value, 0, width, axis=dim)
        before = lax.ppermute(last, axis, up)
        after = lax.ppermute(first, axis, down)
        value = jnp.concatenate([before, value, after], axis=dim)
    return value


def normalize(inputs, gain):
    centre = inputs - jnp.mean(inputs, axis=-1, keepdims=True)
    spread = jnp.mean(centre * centre, axis=-1, keepdims=True)
    return centre * lax.rsqrt(spread + epsilon) * gain


def split_heads(matrix):
    return matrix.reshape(matrix.shape[0], HEADS, HDIM)


def over_blocks(advance, carried, members):
    total_rows = members[0].shape[0]
    stride = math.gcd(total_rows, 1024)

    def one_block(block_index, inner_state):
        offset = block_index * stride
        sliced = tuple((lax.dynamic_slice_in_dim(member, offset, stride, 0) for member in members))
        return advance(inner_state, sliced, offset)

    return lax.fori_loop(0, total_rows // stride, one_block, carried)


def forward_step(query_heads, length, scaling):

    def advance(carried, sliced, first_row):
        key_heads = split_heads(sliced[0])
        value_heads = split_heads(sliced[1])
        positions = first_row + jnp.arange(key_heads.shape[0], dtype=jnp.int32)
        living = (positions < length)[None, None, :]
        scores = (
            jnp.einsum("bhd,lhd->hbl", query_heads, key_heads, preferred_element_type=jnp.float32)
            * scaling
        )
        scores = jnp.where(living, scores, negative)
        top_old, total_old, accumulated = carried
        top_new = jnp.maximum(top_old, jnp.max(scores, axis=-1))
        weights = jnp.where(living, jnp.exp(scores - top_new[:, :, None]), 0.0)
        fading = jnp.exp(top_old - top_new)
        total_new = total_old * fading + jnp.sum(weights, axis=-1)
        update = jnp.einsum(
            "hbl,lhd->bhd",
            weights.astype(jnp.bfloat16),
            value_heads,
            preferred_element_type=jnp.float32,
        )
        return (top_new, total_new, accumulated * fading.T[:, :, None] + update)

    return advance


def query_side(query_heads, grad_heads, logsum, delta, length, scaling):

    def advance(carried, sliced, first_row):
        key_heads = split_heads(sliced[0])
        value_heads = split_heads(sliced[1])
        count_here = key_heads.shape[0]
        positions = first_row + jnp.arange(count_here, dtype=jnp.int32)
        living = (positions < length)[None, None, :]
        scores = (
            jnp.einsum("bhd,lhd->hbl", query_heads, key_heads, preferred_element_type=jnp.float32)
            * scaling
        )
        scores = jnp.where(living, scores, negative)
        probs = jnp.where(living, jnp.exp(scores - logsum.T[:, :, None]), 0.0)
        dprobs = jnp.einsum(
            "bhd,lhd->hbl", grad_heads, value_heads, preferred_element_type=jnp.float32
        )
        grad_scores = (probs * (dprobs - delta.T[:, :, None])).astype(jnp.bfloat16)
        grad_query = (
            carried[0]
            + jnp.einsum("hbl,lhd->bhd", grad_scores, key_heads, preferred_element_type=jnp.float32)
            * scaling
        )
        return (grad_query,)

    return advance


def key_side(key_heads, value_heads, own_living, scaling):

    def advance(carried, sliced, first_row):
        query_heads = split_heads(sliced[0].astype(jnp.bfloat16))
        grad_heads = split_heads(sliced[1].astype(jnp.bfloat16))
        logsum_block = sliced[2]
        delta_block = sliced[3]
        scores = (
            jnp.einsum("bhd,lhd->hbl", query_heads, key_heads, preferred_element_type=jnp.float32)
            * scaling
        )
        scores = jnp.where(own_living, scores, negative)
        probs = jnp.where(own_living, jnp.exp(scores - logsum_block.T[:, :, None]), 0.0)
        dprobs = jnp.einsum(
            "bhd,lhd->hbl", grad_heads, value_heads, preferred_element_type=jnp.float32
        )
        grad_scores = (probs * (dprobs - delta_block.T[:, :, None])).astype(jnp.bfloat16)
        grad_key = (
            carried[0]
            + jnp.einsum(
                "hbl,bhd->lhd", grad_scores, query_heads, preferred_element_type=jnp.float32
            )
            * scaling
        )
        grad_value = carried[1] + jnp.einsum(
            "hbl,bhd->lhd",
            probs.astype(jnp.bfloat16),
            grad_heads,
            preferred_element_type=jnp.float32,
        )
        return (grad_key, grad_value)

    return advance


def per_device(frames, cotangent, lengths, w_proj, gain_attn, gain_conv, w_conv):
    frame_count = frames.shape[1]
    width = HEADS * HDIM
    cycle_size = lax.axis_size("tm")
    own_start = lax.axis_index("tm") * frame_count
    length = lengths[0]
    scaling = 1.0 / math.sqrt(HDIM)
    total_frames = lax.axis_size("dp") * frames.shape[0] * frame_count * cycle_size
    grad_scale = 1.0 / math.sqrt(total_frames)
    contract_last = (((1,), (1,)), ((), ()))
    contract_first = (((0,), (0,)), ((), ()))
    inputs = frames[0].astype(jnp.float32)
    normed_attn = normalize(inputs, gain_attn).astype(jnp.bfloat16)
    projected = jnp.dot(
        normed_attn, w_proj[:, : 3 * width], preferred_element_type=jnp.float32
    ).astype(jnp.bfloat16)
    tm_count = lax.axis_size("tm")
    halves = tm_count // HEADS
    me = lax.axis_index("tm")
    half = me // HEADS
    span = frame_count * HEADS
    total = frame_count * tm_count
    key_live = (jnp.arange(total, dtype=jnp.int32) < length)[None, :]
    half_live = lax.dynamic_slice_in_dim(key_live, half * span, span, 1)
    qkv = projected.reshape(frame_count, 3, HEADS, HDIM).transpose(2, 0, 1, 3)
    got = lax.all_to_all(jnp.tile(qkv, (halves, 1, 1, 1)), "tm", 0, 0, tiled=True)
    got = got.reshape(total, 3, HDIM)
    q_all, k_all, v_all = got[:, 0], got[:, 1], got[:, 2]
    q_half = lax.dynamic_slice_in_dim(q_all, half * span, span, 0)
    scores = lax.dot_general(q_half, k_all, contract_last, preferred_element_type=jnp.float32)
    scores = jnp.where(key_live, scores * scaling, negative)
    top = jnp.max(scores, axis=-1)
    weights = jnp.where(key_live, jnp.exp(scores - top[:, None]), 0.0)
    summed = jnp.sum(weights, axis=-1)
    acc = jnp.dot(weights.astype(jnp.bfloat16), v_all, preferred_element_type=jnp.float32)
    a_half = (acc / summed[:, None]).astype(jnp.bfloat16)
    lse_half = top + jnp.log(summed)

    half_groups = [[part * HEADS + k for k in range(HEADS)] for part in range(halves)]

    def to_frames(rows):
        blocks = rows.reshape((HEADS, frame_count) + rows.shape[1:])
        return lax.all_to_all(blocks, "tm", 0, 0, tiled=True, axis_index_groups=half_groups)

    attended = to_frames(a_half).transpose(1, 0, 2).reshape(frame_count, width)
    w_out = w_proj[:, 3 * width :]
    mixed = inputs + lax.dot_general(
        attended, w_out, contract_last, preferred_element_type=jnp.float32
    )
    resid_f = mixed.astype(jnp.bfloat16).astype(jnp.float32)
    positions = own_start + jnp.arange(frame_count, dtype=jnp.int32)
    valid = (positions < length)[:, None]
    normed_conv = jnp.where(valid, normalize(resid_f, gain_conv), 0.0).astype(jnp.bfloat16)
    reach = KER // 2
    padded = padded_2(normed_conv, (("tm", 0),), reach).astype(jnp.float32)
    kernel = w_conv.astype(jnp.float32)
    conv = jnp.zeros((frame_count, padded.shape[1]), jnp.float32)
    for shift_index in range(KER):
        conv = conv + kernel[shift_index] * padded[shift_index : shift_index + frame_count]
    upstream = cotangent[0].astype(jnp.float32)
    gate = jax.nn.sigmoid(conv)
    grad_conv_in = upstream * gate * (1.0 + conv * (1.0 - gate))
    conv_term = jnp.stack(
        [
            jnp.sum(grad_conv_in * padded[shift_index : shift_index + frame_count], axis=0)
            for shift_index in range(KER)
        ]
    )
    grad_padded = padded_2(grad_conv_in.astype(jnp.bfloat16), (("tm", 0),), reach).astype(
        grad_conv_in.dtype
    )
    grad_normed = jnp.zeros_like(grad_conv_in)
    for shift_index in range(KER):
        begin = 2 * reach - shift_index
        grad_normed = grad_normed + kernel[shift_index] * grad_padded[begin : begin + frame_count]
    grad_normed = jnp.where(valid, grad_normed, 0.0)
    unused_conv, pull_conv = jax.vjp(normalize, resid_f, gain_conv)
    back_resid, gain_conv_term = pull_conv(grad_normed)
    grad_resid = upstream + back_resid
    grad_resid_low = grad_resid.astype(jnp.bfloat16)
    grad_attended = jnp.dot(grad_resid_low, w_out, preferred_element_type=jnp.float32).astype(
        jnp.bfloat16
    )
    send_grad = grad_attended.reshape(frame_count, HEADS, HDIM).transpose(1, 0, 2)
    da_all = lax.all_to_all(jnp.tile(send_grad, (halves, 1, 1)), "tm", 0, 0, tiled=True)
    da_all = da_all.reshape(total, HDIM)
    da_half = lax.dynamic_slice_in_dim(da_all, half * span, span, 0)
    delta_half = jnp.sum(da_half.astype(jnp.float32) * a_half.astype(jnp.float32), axis=-1)
    stats_half = jnp.stack([lse_half, delta_half], axis=0)
    partner = lax.ppermute(
        stats_half, "tm", [(i, (i + HEADS) % tm_count) for i in range(tm_count)]
    )
    stats_all = jnp.where(
        half == 0,
        jnp.concatenate([stats_half, partner], axis=1),
        jnp.concatenate([partner, stats_half], axis=1),
    )
    lse_all = stats_all[0][:, None]
    delta_all = stats_all[1][:, None]
    scores = lax.dot_general(q_half, k_all, contract_last, preferred_element_type=jnp.float32)
    scores = jnp.where(key_live, scores * scaling, negative)
    probs = jnp.where(key_live, jnp.exp(scores - lse_half[:, None]), 0.0)
    dprobs = lax.dot_general(da_half, v_all, contract_last, preferred_element_type=jnp.float32)
    grad_scores = (probs * (dprobs - delta_half[:, None])).astype(jnp.bfloat16)
    grad_q = jnp.dot(grad_scores, k_all, preferred_element_type=jnp.float32) * scaling
    k_half = lax.dynamic_slice_in_dim(k_all, half * span, span, 0)
    v_half = lax.dynamic_slice_in_dim(v_all, half * span, span, 0)
    scores = lax.dot_general(q_all, k_half, contract_last, preferred_element_type=jnp.float32)
    scores = jnp.where(half_live, scores * scaling, negative)
    probs = jnp.where(half_live, jnp.exp(scores - lse_all), 0.0)
    dprobs = lax.dot_general(da_all, v_half, contract_last, preferred_element_type=jnp.float32)
    grad_scores = (probs * (dprobs - delta_all)).astype(jnp.bfloat16)
    grad_k = (
        lax.dot_general(grad_scores, q_all, contract_first, preferred_element_type=jnp.float32)
        * scaling
    )
    grad_v = lax.dot_general(
        probs.astype(jnp.bfloat16), da_all, contract_first, preferred_element_type=jnp.float32
    )
    grad_rows = jnp.stack([grad_q, grad_k, grad_v], axis=1).astype(jnp.bfloat16)
    grad_qkv = to_frames(grad_rows).transpose(1, 2, 0, 3).reshape(frame_count, 3 * width)
    back_normed = lax.dot_general(
        grad_qkv, w_proj[:, : 3 * width], contract_last, preferred_element_type=jnp.float32
    )
    unused_attn, pull_attn = jax.vjp(normalize, inputs, gain_attn)
    back_inputs, gain_attn_term = pull_attn(back_normed)
    grad_frames = (grad_resid + back_inputs).astype(jnp.bfloat16)[None]
    inner_part = lax.dot_general(
        normed_attn, grad_qkv, contract_first, preferred_element_type=jnp.float32
    )
    outer_part = lax.dot_general(
        grad_resid_low, attended, contract_first, preferred_element_type=jnp.float32
    )
    axes = ("dp", "tm")
    devices = lax.axis_size(axes)
    rows = inner_part.shape[0]
    small = jnp.concatenate([conv_term, gain_attn_term[None], gain_conv_term[None]], axis=0)
    small_count = small.size
    small_width = -(-small_count // rows)
    small_flat = jnp.pad(small.reshape(-1), (0, small_width * rows - small_count))
    packed = jnp.concatenate(
        [inner_part, outer_part, small_flat.reshape(rows, small_width)], axis=1
    )
    outer_count = lax.axis_size("dp")
    packed = packed.reshape(outer_count, tm_count, rows // devices, packed.shape[1])
    packed = packed.transpose(1, 0, 2, 3).astype(jnp.bfloat16)
    reduced = lax.all_to_all(packed, "tm", 0, 0, tiled=True).astype(jnp.float32).sum(0)
    reduced = lax.all_to_all(reduced.astype(jnp.bfloat16), "dp", 0, 0, tiled=True)
    reduced = reduced.astype(jnp.float32).sum(0)
    grad_proj = reduced[:, : 4 * width]
    small_part = reduced[:, 4 * width :].reshape(1, -1)
    small_all = lax.all_to_all(
        jnp.broadcast_to(small_part, (devices, small_part.shape[1])), axes, 0, 0, tiled=True
    )
    small_sum = small_all.reshape(-1)[:small_count]
    conv_sum = small_sum[: conv_term.size].reshape(conv_term.shape)
    gains_sum = small_sum[conv_term.size :].reshape(2, -1)
    return (grad_frames, grad_proj * grad_scale, conv_sum * grad_scale, gains_sum * grad_scale)


def solution(mesh):
    return jax.shard_map(
        per_device,
        mesh=mesh,
        in_specs=(P("dp", "tm", None), P("dp", "tm", None), P("dp"), P(), P(), P(), P()),
        out_specs=(P("dp", "tm", None), P(("dp", "tm"), None), P(), P()),
        check_vma=False,
    )
```

```python
import math

import jax
import jax.numpy as jnp
from jax import lax
from jax.sharding import PartitionSpec as P

HEADS = 8
HDIM = 64
KER = 31


epsilon = 1e-05
negative = -1e30


def padded_2(value, sides, width):
    for axis, dim in sides:
        size, length = (lax.axis_size(axis), value.shape[dim])
        up = [(i, (i + 1) % size) for i in range(size - 1)]
        down = [(j, i) for i, j in up]
        last = lax.slice_in_dim(value, length - width, length, axis=dim)
        first = lax.slice_in_dim(value, 0, width, axis=dim)
        before = lax.ppermute(last, axis, up)
        after = lax.ppermute(first, axis, down)
        value = jnp.concatenate([before, value, after], axis=dim)
    return value


def normalize(inputs, gain):
    centre = inputs - jnp.mean(inputs, axis=-1, keepdims=True)
    spread = jnp.mean(centre * centre, axis=-1, keepdims=True)
    return centre * lax.rsqrt(spread + epsilon) * gain


def split_heads(matrix):
    return matrix.reshape(matrix.shape[0], HEADS, HDIM)


def over_blocks(advance, carried, members):
    total_rows = members[0].shape[0]
    stride = math.gcd(total_rows, 1024)

    def one_block(block_index, inner_state):
        offset = block_index * stride
        sliced = tuple((lax.dynamic_slice_in_dim(member, offset, stride, 0) for member in members))
        return advance(inner_state, sliced, offset)

    return lax.fori_loop(0, total_rows // stride, one_block, carried)


def forward_step(query_heads, length, scaling):

    def advance(carried, sliced, first_row):
        key_heads = split_heads(sliced[0])
        value_heads = split_heads(sliced[1])
        positions = first_row + jnp.arange(key_heads.shape[0], dtype=jnp.int32)
        living = (positions < length)[None, None, :]
        scores = (
            jnp.einsum("bhd,lhd->hbl", query_heads, key_heads, preferred_element_type=jnp.float32)
            * scaling
        )
        scores = jnp.where(living, scores, negative)
        top_old, total_old, accumulated = carried
        top_new = jnp.maximum(top_old, jnp.max(scores, axis=-1))
        weights = jnp.where(living, jnp.exp(scores - top_new[:, :, None]), 0.0)
        fading = jnp.exp(top_old - top_new)
        total_new = total_old * fading + jnp.sum(weights, axis=-1)
        update = jnp.einsum(
            "hbl,lhd->bhd",
            weights.astype(jnp.bfloat16),
            value_heads,
            preferred_element_type=jnp.float32,
        )
        return (top_new, total_new, accumulated * fading.T[:, :, None] + update)

    return advance


def query_side(query_heads, grad_heads, logsum, delta, length, scaling):

    def advance(carried, sliced, first_row):
        key_heads = split_heads(sliced[0])
        value_heads = split_heads(sliced[1])
        count_here = key_heads.shape[0]
        positions = first_row + jnp.arange(count_here, dtype=jnp.int32)
        living = (positions < length)[None, None, :]
        scores = (
            jnp.einsum("bhd,lhd->hbl", query_heads, key_heads, preferred_element_type=jnp.float32)
            * scaling
        )
        scores = jnp.where(living, scores, negative)
        probs = jnp.where(living, jnp.exp(scores - logsum.T[:, :, None]), 0.0)
        dprobs = jnp.einsum(
            "bhd,lhd->hbl", grad_heads, value_heads, preferred_element_type=jnp.float32
        )
        grad_scores = (probs * (dprobs - delta.T[:, :, None])).astype(jnp.bfloat16)
        grad_query = (
            carried[0]
            + jnp.einsum("hbl,lhd->bhd", grad_scores, key_heads, preferred_element_type=jnp.float32)
            * scaling
        )
        return (grad_query,)

    return advance


def key_side(key_heads, value_heads, own_living, scaling):

    def advance(carried, sliced, first_row):
        query_heads = split_heads(sliced[0].astype(jnp.bfloat16))
        grad_heads = split_heads(sliced[1].astype(jnp.bfloat16))
        logsum_block = sliced[2]
        delta_block = sliced[3]
        scores = (
            jnp.einsum("bhd,lhd->hbl", query_heads, key_heads, preferred_element_type=jnp.float32)
            * scaling
        )
        scores = jnp.where(own_living, scores, negative)
        probs = jnp.where(own_living, jnp.exp(scores - logsum_block.T[:, :, None]), 0.0)
        dprobs = jnp.einsum(
            "bhd,lhd->hbl", grad_heads, value_heads, preferred_element_type=jnp.float32
        )
        grad_scores = (probs * (dprobs - delta_block.T[:, :, None])).astype(jnp.bfloat16)
        grad_key = (
            carried[0]
            + jnp.einsum(
                "hbl,bhd->lhd", grad_scores, query_heads, preferred_element_type=jnp.float32
            )
            * scaling
        )
        grad_value = carried[1] + jnp.einsum(
            "hbl,bhd->lhd",
            probs.astype(jnp.bfloat16),
            grad_heads,
            preferred_element_type=jnp.float32,
        )
        return (grad_key, grad_value)

    return advance


def per_device(frames, cotangent, lengths, w_proj, gain_attn, gain_conv, w_conv):
    frame_count = frames.shape[1]
    width = HEADS * HDIM
    cycle_size = lax.axis_size("tm")
    own_start = lax.axis_index("tm") * frame_count
    length = lengths[0]
    scaling = 1.0 / math.sqrt(HDIM)
    total_frames = lax.axis_size("dp") * frames.shape[0] * frame_count * cycle_size
    grad_scale = 1.0 / math.sqrt(total_frames)
    contract_last = (((1,), (1,)), ((), ()))
    contract_first = (((0,), (0,)), ((), ()))
    inputs = frames[0].astype(jnp.float32)
    normed_attn = normalize(inputs, gain_attn).astype(jnp.bfloat16)
    projected = jnp.dot(
        normed_attn, w_proj[:, : 3 * width], preferred_element_type=jnp.float32
    ).astype(jnp.bfloat16)
    tm_count = lax.axis_size("tm")
    halves = tm_count // HEADS
    me = lax.axis_index("tm")
    half = me // HEADS
    span = frame_count * HEADS
    total = frame_count * tm_count
    key_live = (jnp.arange(total, dtype=jnp.int32) < length)[None, :]
    half_live = lax.dynamic_slice_in_dim(key_live, half * span, span, 1)
    qkv = projected.reshape(frame_count, 3, HEADS, HDIM).transpose(2, 0, 1, 3)
    got = lax.all_to_all(jnp.tile(qkv, (halves, 1, 1, 1)), "tm", 0, 0, tiled=True)
    got = got.reshape(total, 3, HDIM)
    q_all, k_all, v_all = got[:, 0], got[:, 1], got[:, 2]
    q_half = lax.dynamic_slice_in_dim(q_all, half * span, span, 0)
    scores = lax.dot_general(q_half, k_all, contract_last, preferred_element_type=jnp.float32)
    scores = jnp.where(key_live, scores * scaling, negative)
    top = jnp.max(scores, axis=-1)
    weights = jnp.where(key_live, jnp.exp(scores - top[:, None]), 0.0)
    summed = jnp.sum(weights, axis=-1)
    acc = jnp.dot(weights.astype(jnp.bfloat16), v_all, preferred_element_type=jnp.float32)
    a_half = (acc / summed[:, None]).astype(jnp.bfloat16)
    lse_half = top + jnp.log(summed)

    half_groups = [[part * HEADS + k for k in range(HEADS)] for part in range(halves)]

    def to_frames(rows):
        blocks = rows.reshape((HEADS, frame_count) + rows.shape[1:])
        return lax.all_to_all(blocks, "tm", 0, 0, tiled=True, axis_index_groups=half_groups)

    attended = to_frames(a_half).transpose(1, 0, 2).reshape(frame_count, width)
    w_out = w_proj[:, 3 * width :]
    mixed = inputs + lax.dot_general(
        attended, w_out, contract_last, preferred_element_type=jnp.float32
    )
    resid_f = mixed.astype(jnp.bfloat16).astype(jnp.float32)
    positions = own_start + jnp.arange(frame_count, dtype=jnp.int32)
    valid = (positions < length)[:, None]
    normed_conv = jnp.where(valid, normalize(resid_f, gain_conv), 0.0).astype(jnp.bfloat16)
    reach = KER // 2
    padded = padded_2(normed_conv, (("tm", 0),), reach).astype(jnp.float32)
    kernel = w_conv.astype(jnp.float32)
    conv = jnp.zeros((frame_count, padded.shape[1]), jnp.float32)
    for shift_index in range(KER):
        conv = conv + kernel[shift_index] * padded[shift_index : shift_index + frame_count]
    upstream = cotangent[0].astype(jnp.float32)
    gate = jax.nn.sigmoid(conv)
    grad_conv_in = upstream * gate * (1.0 + conv * (1.0 - gate))
    conv_term = jnp.stack(
        [
            jnp.sum(grad_conv_in * padded[shift_index : shift_index + frame_count], axis=0)
            for shift_index in range(KER)
        ]
    )
    grad_padded = padded_2(grad_conv_in.astype(jnp.bfloat16), (("tm", 0),), reach).astype(
        grad_conv_in.dtype
    )
    grad_normed = jnp.zeros_like(grad_conv_in)
    for shift_index in range(KER):
        begin = 2 * reach - shift_index
        grad_normed = grad_normed + kernel[shift_index] * grad_padded[begin : begin + frame_count]
    grad_normed = jnp.where(valid, grad_normed, 0.0)
    unused_conv, pull_conv = jax.vjp(normalize, resid_f, gain_conv)
    back_resid, gain_conv_term = pull_conv(grad_normed)
    grad_resid = upstream + back_resid
    grad_resid_low = grad_resid.astype(jnp.bfloat16)
    grad_attended = jnp.dot(grad_resid_low, w_out, preferred_element_type=jnp.float32).astype(
        jnp.bfloat16
    )
    send_grad = grad_attended.reshape(frame_count, HEADS, HDIM).transpose(1, 0, 2)
    da_all = lax.all_to_all(jnp.tile(send_grad, (halves, 1, 1)), "tm", 0, 0, tiled=True)
    da_all = da_all.reshape(total, HDIM)
    da_half = lax.dynamic_slice_in_dim(da_all, half * span, span, 0)
    delta_half = jnp.sum(da_half.astype(jnp.float32) * a_half.astype(jnp.float32), axis=-1)
    stats_half = jnp.stack([lse_half, delta_half], axis=0)
    partner = lax.ppermute(
        stats_half, "tm", [(i, (i + HEADS) % tm_count) for i in range(tm_count)]
    )
    stats_all = jnp.where(
        half == 0,
        jnp.concatenate([stats_half, partner], axis=1),
        jnp.concatenate([partner, stats_half], axis=1),
    )
    lse_all = stats_all[0][:, None]
    delta_all = stats_all[1][:, None]
    scores = lax.dot_general(q_half, k_all, contract_last, preferred_element_type=jnp.float32)
    scores = jnp.where(key_live, scores * scaling, negative)
    probs = jnp.where(key_live, jnp.exp(scores - lse_half[:, None]), 0.0)
    dprobs = lax.dot_general(da_half, v_all, contract_last, preferred_element_type=jnp.float32)
    grad_scores = (probs * (dprobs - delta_half[:, None])).astype(jnp.bfloat16)
    grad_q = jnp.dot(grad_scores, k_all, preferred_element_type=jnp.float32) * scaling
    k_half = lax.dynamic_slice_in_dim(k_all, half * span, span, 0)
    v_half = lax.dynamic_slice_in_dim(v_all, half * span, span, 0)
    scores = lax.dot_general(q_all, k_half, contract_last, preferred_element_type=jnp.float32)
    scores = jnp.where(half_live, scores * scaling, negative)
    probs = jnp.where(half_live, jnp.exp(scores - lse_all), 0.0)
    dprobs = lax.dot_general(da_all, v_half, contract_last, preferred_element_type=jnp.float32)
    grad_scores = (probs * (dprobs - delta_all)).astype(jnp.bfloat16)
    grad_k = (
        lax.dot_general(grad_scores, q_all, contract_first, preferred_element_type=jnp.float32)
        * scaling
    )
    grad_v = lax.dot_general(
        probs.astype(jnp.bfloat16), da_all, contract_first, preferred_element_type=jnp.float32
    )
    grad_rows = jnp.stack([grad_q, grad_k, grad_v], axis=1).astype(jnp.bfloat16)
    grad_qkv = to_frames(grad_rows).transpose(1, 2, 0, 3).reshape(frame_count, 3 * width)
    back_normed = lax.dot_general(
        grad_qkv, w_proj[:, : 3 * width], contract_last, preferred_element_type=jnp.float32
    )
    unused_attn, pull_attn = jax.vjp(normalize, inputs, gain_attn)
    back_inputs, gain_attn_term = pull_attn(back_normed)
    grad_frames = (grad_resid + back_inputs).astype(jnp.bfloat16)[None]
    inner_part = lax.dot_general(
        normed_attn, grad_qkv, contract_first, preferred_element_type=jnp.float32
    )
    outer_part = lax.dot_general(
        grad_resid_low, attended, contract_first, preferred_element_type=jnp.float32
    )
    axes = ("dp", "tm")
    devices = lax.axis_size(axes)
    rows = inner_part.shape[0]
    small = jnp.concatenate([conv_term, gain_attn_term[None], gain_conv_term[None]], axis=0)
    small_count = small.size
    small_width = -(-small_count // rows)
    small_flat = jnp.pad(small.reshape(-1), (0, small_width * rows - small_count))
    packed = jnp.concatenate(
        [inner_part, outer_part, small_flat.reshape(rows, small_width)], axis=1
    )
    outer_count = lax.axis_size("dp")
    packed = packed.reshape(outer_count, tm_count, rows // devices, packed.shape[1])
    packed = packed.transpose(1, 0, 2, 3).astype(jnp.bfloat16)
    reduced = lax.all_to_all(packed, "tm", 0, 0, tiled=True).astype(jnp.float32).sum(0)
    big_cols = 4 * width
    spare = reduced[:, :, big_cols:].reshape(-1)
    spare_rows = -(-spare.size // big_cols)
    spare = jnp.pad(spare, (0, spare_rows * big_cols - spare.size)).reshape(spare_rows, big_cols)
    body = jnp.concatenate(
        [reduced[:, :, :big_cols], jnp.broadcast_to(spare, (outer_count,) + spare.shape)], axis=1
    )
    body = lax.all_to_all(body.astype(jnp.bfloat16), "dp", 0, 0, tiled=True)
    body = body.astype(jnp.float32).sum(0)
    grad_proj = body[: rows // devices]
    spread = rows // devices * small_width
    small_part = body[rows // devices :].reshape(1, -1)[:, : outer_count * spread]
    small_all = lax.all_to_all(
        jnp.broadcast_to(small_part, (tm_count, small_part.shape[1])), "tm", 0, 0, tiled=True
    )
    small_all = small_all.reshape(tm_count, outer_count, spread).transpose(1, 0, 2)
    small_sum = small_all.reshape(-1)[:small_count]
    conv_sum = small_sum[: conv_term.size].reshape(conv_term.shape)
    gains_sum = small_sum[conv_term.size :].reshape(2, -1)
    return (grad_frames, grad_proj * grad_scale, conv_sum * grad_scale, gains_sum * grad_scale)


def solution(mesh):
    return jax.shard_map(
        per_device,
        mesh=mesh,
        in_specs=(P("dp", "tm", None), P("dp", "tm", None), P("dp"), P(), P(), P(), P()),
        out_specs=(P("dp", "tm", None), P(("dp", "tm"), None), P(), P()),
        check_vma=False,
    )
```

```python
import math

import jax
import jax.numpy as jnp
from jax import lax
from jax.sharding import PartitionSpec as P

HEADS = 8
HDIM = 64
KER = 31


epsilon = 1e-05
negative = -1e30


def padded_2(value, sides, width):
    for axis, dim in sides:
        size, length = (lax.axis_size(axis), value.shape[dim])
        up = [(i, (i + 1) % size) for i in range(size - 1)]
        down = [(j, i) for i, j in up]
        last = lax.slice_in_dim(value, length - width, length, axis=dim)
        first = lax.slice_in_dim(value, 0, width, axis=dim)
        before = lax.ppermute(last, axis, up)
        after = lax.ppermute(first, axis, down)
        value = jnp.concatenate([before, value, after], axis=dim)
    return value


def normalize(inputs, gain):
    centre = inputs - jnp.mean(inputs, axis=-1, keepdims=True)
    spread = jnp.mean(centre * centre, axis=-1, keepdims=True)
    return centre * lax.rsqrt(spread + epsilon) * gain


def split_heads(matrix):
    return matrix.reshape(matrix.shape[0], HEADS, HDIM)


def over_blocks(advance, carried, members):
    total_rows = members[0].shape[0]
    stride = math.gcd(total_rows, 1024)

    def one_block(block_index, inner_state):
        offset = block_index * stride
        sliced = tuple((lax.dynamic_slice_in_dim(member, offset, stride, 0) for member in members))
        return advance(inner_state, sliced, offset)

    return lax.fori_loop(0, total_rows // stride, one_block, carried)


def forward_step(query_heads, length, scaling):

    def advance(carried, sliced, first_row):
        key_heads = split_heads(sliced[0])
        value_heads = split_heads(sliced[1])
        positions = first_row + jnp.arange(key_heads.shape[0], dtype=jnp.int32)
        living = (positions < length)[None, None, :]
        scores = (
            jnp.einsum("bhd,lhd->hbl", query_heads, key_heads, preferred_element_type=jnp.float32)
            * scaling
        )
        scores = jnp.where(living, scores, negative)
        top_old, total_old, accumulated = carried
        top_new = jnp.maximum(top_old, jnp.max(scores, axis=-1))
        weights = jnp.where(living, jnp.exp(scores - top_new[:, :, None]), 0.0)
        fading = jnp.exp(top_old - top_new)
        total_new = total_old * fading + jnp.sum(weights, axis=-1)
        update = jnp.einsum(
            "hbl,lhd->bhd",
            weights.astype(jnp.bfloat16),
            value_heads,
            preferred_element_type=jnp.float32,
        )
        return (top_new, total_new, accumulated * fading.T[:, :, None] + update)

    return advance


def query_side(query_heads, grad_heads, logsum, delta, length, scaling):

    def advance(carried, sliced, first_row):
        key_heads = split_heads(sliced[0])
        value_heads = split_heads(sliced[1])
        count_here = key_heads.shape[0]
        positions = first_row + jnp.arange(count_here, dtype=jnp.int32)
        living = (positions < length)[None, None, :]
        scores = (
            jnp.einsum("bhd,lhd->hbl", query_heads, key_heads, preferred_element_type=jnp.float32)
            * scaling
        )
        scores = jnp.where(living, scores, negative)
        probs = jnp.where(living, jnp.exp(scores - logsum.T[:, :, None]), 0.0)
        dprobs = jnp.einsum(
            "bhd,lhd->hbl", grad_heads, value_heads, preferred_element_type=jnp.float32
        )
        grad_scores = (probs * (dprobs - delta.T[:, :, None])).astype(jnp.bfloat16)
        grad_query = (
            carried[0]
            + jnp.einsum("hbl,lhd->bhd", grad_scores, key_heads, preferred_element_type=jnp.float32)
            * scaling
        )
        return (grad_query,)

    return advance


def key_side(key_heads, value_heads, own_living, scaling):

    def advance(carried, sliced, first_row):
        query_heads = split_heads(sliced[0].astype(jnp.bfloat16))
        grad_heads = split_heads(sliced[1].astype(jnp.bfloat16))
        logsum_block = sliced[2]
        delta_block = sliced[3]
        scores = (
            jnp.einsum("bhd,lhd->hbl", query_heads, key_heads, preferred_element_type=jnp.float32)
            * scaling
        )
        scores = jnp.where(own_living, scores, negative)
        probs = jnp.where(own_living, jnp.exp(scores - logsum_block.T[:, :, None]), 0.0)
        dprobs = jnp.einsum(
            "bhd,lhd->hbl", grad_heads, value_heads, preferred_element_type=jnp.float32
        )
        grad_scores = (probs * (dprobs - delta_block.T[:, :, None])).astype(jnp.bfloat16)
        grad_key = (
            carried[0]
            + jnp.einsum(
                "hbl,bhd->lhd", grad_scores, query_heads, preferred_element_type=jnp.float32
            )
            * scaling
        )
        grad_value = carried[1] + jnp.einsum(
            "hbl,bhd->lhd",
            probs.astype(jnp.bfloat16),
            grad_heads,
            preferred_element_type=jnp.float32,
        )
        return (grad_key, grad_value)

    return advance


def per_device(frames, cotangent, lengths, w_proj, gain_attn, gain_conv, w_conv):
    frame_count = frames.shape[1]
    width = HEADS * HDIM
    cycle_size = lax.axis_size("tm")
    own_start = lax.axis_index("tm") * frame_count
    length = lengths[0]
    scaling = 1.0 / math.sqrt(HDIM)
    total_frames = lax.axis_size("dp") * frames.shape[0] * frame_count * cycle_size
    grad_scale = 1.0 / math.sqrt(total_frames)
    contract_last = (((1,), (1,)), ((), ()))
    contract_first = (((0,), (0,)), ((), ()))
    inputs = frames[0].astype(jnp.float32)
    normed_attn = normalize(inputs, gain_attn).astype(jnp.bfloat16)
    projected = jnp.dot(
        normed_attn, w_proj[:, : 3 * width], preferred_element_type=jnp.float32
    ).astype(jnp.bfloat16)
    tm_count = lax.axis_size("tm")
    halves = tm_count // HEADS
    me = lax.axis_index("tm")
    half = me // HEADS
    span = frame_count * HEADS
    total = frame_count * tm_count
    key_live = (jnp.arange(total, dtype=jnp.int32) < length)[None, :]
    half_live = lax.dynamic_slice_in_dim(key_live, half * span, span, 1)
    qkv = projected.reshape(frame_count, 3, HEADS, HDIM).transpose(2, 0, 1, 3)
    got = lax.all_to_all(jnp.tile(qkv, (halves, 1, 1, 1)), "tm", 0, 0, tiled=True)
    got = got.reshape(total, 3, HDIM)
    q_all, k_all, v_all = got[:, 0], got[:, 1], got[:, 2]
    q_half = lax.dynamic_slice_in_dim(q_all, half * span, span, 0)
    scores = lax.dot_general(q_half, k_all, contract_last, preferred_element_type=jnp.float32)
    scores = jnp.where(key_live, scores * scaling, negative)
    top = jnp.max(scores, axis=-1)
    weights = jnp.where(key_live, jnp.exp(scores - top[:, None]), 0.0)
    summed = jnp.sum(weights, axis=-1)
    acc = jnp.dot(weights.astype(jnp.bfloat16), v_all, preferred_element_type=jnp.float32)
    a_half = (acc / summed[:, None]).astype(jnp.bfloat16)
    lse_half = top + jnp.log(summed)

    half_groups = [[part * HEADS + k for k in range(HEADS)] for part in range(halves)]

    def to_frames(rows):
        blocks = rows.reshape((HEADS, frame_count) + rows.shape[1:])
        return lax.all_to_all(blocks, "tm", 0, 0, tiled=True, axis_index_groups=half_groups)

    attended = to_frames(a_half).transpose(1, 0, 2).reshape(frame_count, width)
    w_out = w_proj[:, 3 * width :]
    mixed = inputs + lax.dot_general(
        attended, w_out, contract_last, preferred_element_type=jnp.float32
    )
    resid_f = mixed.astype(jnp.bfloat16).astype(jnp.float32)
    positions = own_start + jnp.arange(frame_count, dtype=jnp.int32)
    valid = (positions < length)[:, None]
    normed_conv = jnp.where(valid, normalize(resid_f, gain_conv), 0.0).astype(jnp.bfloat16)
    reach = KER // 2
    padded = padded_2(normed_conv, (("tm", 0),), reach).astype(jnp.float32)
    kernel = w_conv.astype(jnp.float32)
    conv = jnp.zeros((frame_count, padded.shape[1]), jnp.float32)
    for shift_index in range(KER):
        conv = conv + kernel[shift_index] * padded[shift_index : shift_index + frame_count]
    upstream = cotangent[0].astype(jnp.float32)
    gate = jax.nn.sigmoid(conv)
    grad_conv_in = upstream * gate * (1.0 + conv * (1.0 - gate))
    conv_term = jnp.stack(
        [
            jnp.sum(grad_conv_in * padded[shift_index : shift_index + frame_count], axis=0)
            for shift_index in range(KER)
        ]
    )
    grad_padded = padded_2(grad_conv_in.astype(jnp.bfloat16), (("tm", 0),), reach).astype(
        grad_conv_in.dtype
    )
    grad_normed = jnp.zeros_like(grad_conv_in)
    for shift_index in range(KER):
        begin = 2 * reach - shift_index
        grad_normed = grad_normed + kernel[shift_index] * grad_padded[begin : begin + frame_count]
    grad_normed = jnp.where(valid, grad_normed, 0.0)
    unused_conv, pull_conv = jax.vjp(normalize, resid_f, gain_conv)
    back_resid, gain_conv_term = pull_conv(grad_normed)
    grad_resid = upstream + back_resid
    grad_resid_low = grad_resid.astype(jnp.bfloat16)
    grad_attended = jnp.dot(grad_resid_low, w_out, preferred_element_type=jnp.float32).astype(
        jnp.bfloat16
    )
    send_grad = grad_attended.reshape(frame_count, HEADS, HDIM).transpose(1, 0, 2)
    da_all = lax.all_to_all(jnp.tile(send_grad, (halves, 1, 1)), "tm", 0, 0, tiled=True)
    da_all = da_all.reshape(total, HDIM)
    da_half = lax.dynamic_slice_in_dim(da_all, half * span, span, 0)
    delta_half = jnp.sum(da_half.astype(jnp.float32) * a_half.astype(jnp.float32), axis=-1)
    stats_half = jnp.stack([lse_half, delta_half], axis=0)
    partner = lax.ppermute(
        stats_half, "tm", [(i, (i + HEADS) % tm_count) for i in range(tm_count)]
    )
    stats_all = jnp.where(
        half == 0,
        jnp.concatenate([stats_half, partner], axis=1),
        jnp.concatenate([partner, stats_half], axis=1),
    )
    lse_all = stats_all[0][:, None]
    delta_all = stats_all[1][:, None]
    scores = lax.dot_general(q_half, k_all, contract_last, preferred_element_type=jnp.float32)
    scores = jnp.where(key_live, scores * scaling, negative)
    probs = jnp.where(key_live, jnp.exp(scores - lse_half[:, None]), 0.0)
    dprobs = lax.dot_general(da_half, v_all, contract_last, preferred_element_type=jnp.float32)
    grad_scores = (probs * (dprobs - delta_half[:, None])).astype(jnp.bfloat16)
    grad_q = jnp.dot(grad_scores, k_all, preferred_element_type=jnp.float32) * scaling
    k_half = lax.dynamic_slice_in_dim(k_all, half * span, span, 0)
    v_half = lax.dynamic_slice_in_dim(v_all, half * span, span, 0)
    scores = lax.dot_general(q_all, k_half, contract_last, preferred_element_type=jnp.float32)
    scores = jnp.where(half_live, scores * scaling, negative)
    probs = jnp.where(half_live, jnp.exp(scores - lse_all), 0.0)
    dprobs = lax.dot_general(da_all, v_half, contract_last, preferred_element_type=jnp.float32)
    grad_scores = (probs * (dprobs - delta_all)).astype(jnp.bfloat16)
    grad_k = (
        lax.dot_general(grad_scores, q_all, contract_first, preferred_element_type=jnp.float32)
        * scaling
    )
    grad_v = lax.dot_general(
        probs.astype(jnp.bfloat16), da_all, contract_first, preferred_element_type=jnp.float32
    )
    grad_rows = jnp.stack([grad_q, grad_k, grad_v], axis=1).astype(jnp.bfloat16)
    grad_qkv = to_frames(grad_rows).transpose(1, 2, 0, 3).reshape(frame_count, 3 * width)
    back_normed = lax.dot_general(
        grad_qkv, w_proj[:, : 3 * width], contract_last, preferred_element_type=jnp.float32
    )
    unused_attn, pull_attn = jax.vjp(normalize, inputs, gain_attn)
    back_inputs, gain_attn_term = pull_attn(back_normed)
    grad_frames = (grad_resid + back_inputs).astype(jnp.bfloat16)[None]
    inner_part = lax.dot_general(
        normed_attn, grad_qkv, contract_first, preferred_element_type=jnp.float32
    )
    outer_part = lax.dot_general(
        grad_resid_low, attended, contract_first, preferred_element_type=jnp.float32
    )
    axes = ("dp", "tm")
    devices = lax.axis_size(axes)
    rows = inner_part.shape[0]
    rows_per = rows // devices
    small = jnp.concatenate([conv_term, gain_conv_term[None]], axis=0)
    small_count = small.size
    small_width = -(-small_count // rows)
    small_flat = jnp.pad(small.reshape(-1), (0, small_width * rows - small_count))
    packed = jnp.concatenate(
        [inner_part, outer_part, small_flat.reshape(rows, small_width)], axis=1
    )
    outer_count = lax.axis_size("dp")
    packed = packed.reshape(outer_count, tm_count, rows_per, packed.shape[1])
    packed = packed.transpose(1, 0, 2, 3).astype(jnp.bfloat16)
    reduced = lax.all_to_all(packed, "tm", 0, 0, tiled=True).astype(jnp.float32).sum(0)
    w_rows = w_proj.reshape(outer_count, tm_count, rows_per, 4 * width)
    w_rows = lax.dynamic_index_in_dim(w_rows, me, 1, keepdims=False)[:, :, : 3 * width]
    g_rows = lax.dynamic_index_in_dim(
        gain_attn.reshape(outer_count, tm_count, rows_per), me, 1, keepdims=False
    )
    gain_attn_part = (
        jnp.sum(w_rows.astype(jnp.float32) * reduced[:, :, : 3 * width], axis=-1) / g_rows
    )
    big_cols = 4 * width
    spare = jnp.concatenate(
        [reduced[:, :, big_cols:].reshape(-1), gain_attn_part.reshape(-1)]
    )
    spare_size = spare.size
    spare_rows = -(-spare_size // big_cols)
    spare = jnp.pad(spare, (0, spare_rows * big_cols - spare_size)).reshape(spare_rows, big_cols)
    body = jnp.concatenate(
        [reduced[:, :, :big_cols], jnp.broadcast_to(spare, (outer_count,) + spare.shape)], axis=1
    )
    body = lax.all_to_all(body.astype(jnp.bfloat16), "dp", 0, 0, tiled=True)
    body = body.astype(jnp.float32).sum(0)
    grad_proj = body[:rows_per]
    small_part = body[rows_per:].reshape(1, -1)[:, :spare_size]
    small_all = lax.all_to_all(
        jnp.broadcast_to(small_part, (tm_count, spare_size)), "tm", 0, 0, tiled=True
    )
    spread = outer_count * rows_per * small_width
    small_sum = small_all[:, :spread].reshape(tm_count, outer_count, rows_per * small_width)
    small_sum = small_sum.transpose(1, 0, 2).reshape(-1)[:small_count]
    gain_attn_sum = small_all[:, spread:].reshape(tm_count, outer_count, rows_per)
    gain_attn_sum = gain_attn_sum.transpose(1, 0, 2).reshape(-1)
    conv_sum = small_sum[: conv_term.size].reshape(conv_term.shape)
    gains_sum = jnp.stack([gain_attn_sum, small_sum[conv_term.size :]])
    return (grad_frames, grad_proj * grad_scale, conv_sum * grad_scale, gains_sum * grad_scale)


def solution(mesh):
    return jax.shard_map(
        per_device,
        mesh=mesh,
        in_specs=(P("dp", "tm", None), P("dp", "tm", None), P("dp"), P(), P(), P(), P()),
        out_specs=(P("dp", "tm", None), P(("dp", "tm"), None), P(), P()),
        check_vma=False,
    )
```

```python
import math

import jax
import jax.numpy as jnp
from jax import lax
from jax.sharding import PartitionSpec as P

HEADS = 8
HDIM = 64
KER = 31


epsilon = 1e-05
negative = -1e30


def padded_2(value, sides, width):
    for axis, dim in sides:
        size, length = (lax.axis_size(axis), value.shape[dim])
        up = [(i, (i + 1) % size) for i in range(size - 1)]
        down = [(j, i) for i, j in up]
        last = lax.slice_in_dim(value, length - width, length, axis=dim)
        first = lax.slice_in_dim(value, 0, width, axis=dim)
        before = lax.ppermute(last, axis, up)
        after = lax.ppermute(first, axis, down)
        value = jnp.concatenate([before, value, after], axis=dim)
    return value


def normalize(inputs, gain):
    centre = inputs - jnp.mean(inputs, axis=-1, keepdims=True)
    spread = jnp.mean(centre * centre, axis=-1, keepdims=True)
    return centre * lax.rsqrt(spread + epsilon) * gain


def split_heads(matrix):
    return matrix.reshape(matrix.shape[0], HEADS, HDIM)


def over_blocks(advance, carried, members):
    total_rows = members[0].shape[0]
    stride = math.gcd(total_rows, 1024)

    def one_block(block_index, inner_state):
        offset = block_index * stride
        sliced = tuple((lax.dynamic_slice_in_dim(member, offset, stride, 0) for member in members))
        return advance(inner_state, sliced, offset)

    return lax.fori_loop(0, total_rows // stride, one_block, carried)


def forward_step(query_heads, length, scaling):

    def advance(carried, sliced, first_row):
        key_heads = split_heads(sliced[0])
        value_heads = split_heads(sliced[1])
        positions = first_row + jnp.arange(key_heads.shape[0], dtype=jnp.int32)
        living = (positions < length)[None, None, :]
        scores = (
            jnp.einsum("bhd,lhd->hbl", query_heads, key_heads, preferred_element_type=jnp.float32)
            * scaling
        )
        scores = jnp.where(living, scores, negative)
        top_old, total_old, accumulated = carried
        top_new = jnp.maximum(top_old, jnp.max(scores, axis=-1))
        weights = jnp.where(living, jnp.exp(scores - top_new[:, :, None]), 0.0)
        fading = jnp.exp(top_old - top_new)
        total_new = total_old * fading + jnp.sum(weights, axis=-1)
        update = jnp.einsum(
            "hbl,lhd->bhd",
            weights.astype(jnp.bfloat16),
            value_heads,
            preferred_element_type=jnp.float32,
        )
        return (top_new, total_new, accumulated * fading.T[:, :, None] + update)

    return advance


def query_side(query_heads, grad_heads, logsum, delta, length, scaling):

    def advance(carried, sliced, first_row):
        key_heads = split_heads(sliced[0])
        value_heads = split_heads(sliced[1])
        count_here = key_heads.shape[0]
        positions = first_row + jnp.arange(count_here, dtype=jnp.int32)
        living = (positions < length)[None, None, :]
        scores = (
            jnp.einsum("bhd,lhd->hbl", query_heads, key_heads, preferred_element_type=jnp.float32)
            * scaling
        )
        scores = jnp.where(living, scores, negative)
        probs = jnp.where(living, jnp.exp(scores - logsum.T[:, :, None]), 0.0)
        dprobs = jnp.einsum(
            "bhd,lhd->hbl", grad_heads, value_heads, preferred_element_type=jnp.float32
        )
        grad_scores = (probs * (dprobs - delta.T[:, :, None])).astype(jnp.bfloat16)
        grad_query = (
            carried[0]
            + jnp.einsum("hbl,lhd->bhd", grad_scores, key_heads, preferred_element_type=jnp.float32)
            * scaling
        )
        return (grad_query,)

    return advance


def key_side(key_heads, value_heads, own_living, scaling):

    def advance(carried, sliced, first_row):
        query_heads = split_heads(sliced[0].astype(jnp.bfloat16))
        grad_heads = split_heads(sliced[1].astype(jnp.bfloat16))
        logsum_block = sliced[2]
        delta_block = sliced[3]
        scores = (
            jnp.einsum("bhd,lhd->hbl", query_heads, key_heads, preferred_element_type=jnp.float32)
            * scaling
        )
        scores = jnp.where(own_living, scores, negative)
        probs = jnp.where(own_living, jnp.exp(scores - logsum_block.T[:, :, None]), 0.0)
        dprobs = jnp.einsum(
            "bhd,lhd->hbl", grad_heads, value_heads, preferred_element_type=jnp.float32
        )
        grad_scores = (probs * (dprobs - delta_block.T[:, :, None])).astype(jnp.bfloat16)
        grad_key = (
            carried[0]
            + jnp.einsum(
                "hbl,bhd->lhd", grad_scores, query_heads, preferred_element_type=jnp.float32
            )
            * scaling
        )
        grad_value = carried[1] + jnp.einsum(
            "hbl,bhd->lhd",
            probs.astype(jnp.bfloat16),
            grad_heads,
            preferred_element_type=jnp.float32,
        )
        return (grad_key, grad_value)

    return advance


def per_device(frames, cotangent, lengths, w_proj, gain_attn, gain_conv, w_conv):
    frame_count = frames.shape[1]
    width = HEADS * HDIM
    cycle_size = lax.axis_size("tm")
    own_start = lax.axis_index("tm") * frame_count
    length = lengths[0]
    scaling = 1.0 / math.sqrt(HDIM)
    total_frames = lax.axis_size("dp") * frames.shape[0] * frame_count * cycle_size
    grad_scale = 1.0 / math.sqrt(total_frames)
    contract_last = (((1,), (1,)), ((), ()))
    contract_first = (((0,), (0,)), ((), ()))
    inputs = frames[0].astype(jnp.float32)
    normed_attn = normalize(inputs, gain_attn).astype(jnp.bfloat16)
    projected = jnp.dot(
        normed_attn, w_proj[:, : 3 * width], preferred_element_type=jnp.float32
    ).astype(jnp.bfloat16)
    tm_count = lax.axis_size("tm")
    halves = tm_count // HEADS
    me = lax.axis_index("tm")
    half = me // HEADS
    span = frame_count * HEADS
    total = frame_count * tm_count
    key_live = (jnp.arange(total, dtype=jnp.int32) < length)[None, :]
    half_live = lax.dynamic_slice_in_dim(key_live, half * span, span, 1)
    qkv = projected.reshape(frame_count, 3, HEADS, HDIM).transpose(2, 0, 1, 3)
    got = lax.all_to_all(jnp.tile(qkv, (halves, 1, 1, 1)), "tm", 0, 0, tiled=True)
    got = got.reshape(total, 3, HDIM)
    q_all, k_all, v_all = got[:, 0], got[:, 1], got[:, 2]
    q_half = lax.dynamic_slice_in_dim(q_all, half * span, span, 0)
    scores = lax.dot_general(q_half, k_all, contract_last, preferred_element_type=jnp.float32)
    scores = jnp.where(key_live, scores * scaling, negative)
    top = jnp.max(scores, axis=-1)
    weights = jnp.where(key_live, jnp.exp(scores - top[:, None]), 0.0)
    summed = jnp.sum(weights, axis=-1)
    acc = jnp.dot(weights.astype(jnp.bfloat16), v_all, preferred_element_type=jnp.float32)
    a_half = (acc / summed[:, None]).astype(jnp.bfloat16)
    lse_half = top + jnp.log(summed)

    half_groups = [[part * HEADS + k for k in range(HEADS)] for part in range(halves)]

    def to_frames(rows):
        blocks = rows.reshape((HEADS, frame_count) + rows.shape[1:])
        return lax.all_to_all(blocks, "tm", 0, 0, tiled=True, axis_index_groups=half_groups)

    attended = to_frames(a_half).transpose(1, 0, 2).reshape(frame_count, width)
    w_out = w_proj[:, 3 * width :]
    mixed = inputs + lax.dot_general(
        attended, w_out, contract_last, preferred_element_type=jnp.float32
    )
    resid_f = mixed.astype(jnp.bfloat16).astype(jnp.float32)
    positions = own_start + jnp.arange(frame_count, dtype=jnp.int32)
    valid = (positions < length)[:, None]
    normed_conv = jnp.where(valid, normalize(resid_f, gain_conv), 0.0).astype(jnp.bfloat16)
    reach = KER // 2
    kernel = w_conv.astype(jnp.float32)
    up = [(i, i + 1) for i in range(tm_count - 1)]
    down = [(j, i) for i, j in up]

    def halos(value):
        before = lax.ppermute(value[frame_count - reach :], "tm", up).astype(jnp.float32)
        after = lax.ppermute(value[:reach], "tm", down).astype(jnp.float32)
        zeros = jnp.zeros((2 * reach, value.shape[1]), jnp.float32)
        return (
            jnp.concatenate([before, zeros], axis=0),
            jnp.concatenate([zeros, after], axis=0),
        )

    def taps(source, count, start):
        result = kernel[0] * source[start(0) : start(0) + count]
        for shift_index in range(1, KER):
            begin = start(shift_index)
            result = result + kernel[shift_index] * source[begin : begin + count]
        return result

    edge = frame_count - reach
    own_conv = jnp.pad(normed_conv.astype(jnp.float32), ((reach, reach), (0, 0)))
    head_conv, tail_conv = halos(normed_conv)
    conv = taps(own_conv, frame_count, lambda j: j)
    conv = conv.at[:reach].add(taps(head_conv, reach, lambda j: j))
    conv = conv.at[edge:].add(taps(tail_conv, reach, lambda j: j))
    upstream = cotangent[0].astype(jnp.float32)
    gate = jax.nn.sigmoid(conv)
    grad_conv_in = upstream * gate * (1.0 + conv * (1.0 - gate))
    conv_term = jnp.stack(
        [
            jnp.sum(grad_conv_in * own_conv[j : j + frame_count], axis=0)
            + jnp.sum(grad_conv_in[:reach] * head_conv[j : j + reach], axis=0)
            + jnp.sum(grad_conv_in[edge:] * tail_conv[j : j + reach], axis=0)
            for j in range(KER)
        ]
    )
    grad_low = grad_conv_in.astype(jnp.bfloat16)
    own_grad = jnp.pad(grad_low.astype(jnp.float32), ((reach, reach), (0, 0)))
    head_grad, tail_grad = halos(grad_low)
    grad_normed = taps(own_grad, frame_count, lambda j: 2 * reach - j)
    grad_normed = grad_normed.at[:reach].add(taps(head_grad, reach, lambda j: 2 * reach - j))
    grad_normed = grad_normed.at[edge:].add(taps(tail_grad, reach, lambda j: 2 * reach - j))
    grad_normed = jnp.where(valid, grad_normed, 0.0)
    unused_conv, pull_conv = jax.vjp(normalize, resid_f, gain_conv)
    back_resid, gain_conv_term = pull_conv(grad_normed)
    grad_resid = upstream + back_resid
    grad_resid_low = grad_resid.astype(jnp.bfloat16)
    grad_attended = jnp.dot(grad_resid_low, w_out, preferred_element_type=jnp.float32).astype(
        jnp.bfloat16
    )
    send_grad = grad_attended.reshape(frame_count, HEADS, HDIM).transpose(1, 0, 2)
    da_all = lax.all_to_all(jnp.tile(send_grad, (halves, 1, 1)), "tm", 0, 0, tiled=True)
    da_all = da_all.reshape(total, HDIM)
    da_half = lax.dynamic_slice_in_dim(da_all, half * span, span, 0)
    delta_half = jnp.sum(da_half.astype(jnp.float32) * a_half.astype(jnp.float32), axis=-1)
    stats_half = jnp.stack([lse_half, delta_half], axis=0)
    partner = lax.ppermute(
        stats_half, "tm", [(i, (i + HEADS) % tm_count) for i in range(tm_count)]
    )
    stats_all = jnp.where(
        half == 0,
        jnp.concatenate([stats_half, partner], axis=1),
        jnp.concatenate([partner, stats_half], axis=1),
    )
    lse_all = stats_all[0][:, None]
    delta_all = stats_all[1][:, None]
    scores = lax.dot_general(q_half, k_all, contract_last, preferred_element_type=jnp.float32)
    scores = jnp.where(key_live, scores * scaling, negative)
    probs = jnp.where(key_live, jnp.exp(scores - lse_half[:, None]), 0.0)
    dprobs = lax.dot_general(da_half, v_all, contract_last, preferred_element_type=jnp.float32)
    grad_scores = (probs * (dprobs - delta_half[:, None])).astype(jnp.bfloat16)
    grad_q = jnp.dot(grad_scores, k_all, preferred_element_type=jnp.float32) * scaling
    k_half = lax.dynamic_slice_in_dim(k_all, half * span, span, 0)
    v_half = lax.dynamic_slice_in_dim(v_all, half * span, span, 0)
    scores = lax.dot_general(q_all, k_half, contract_last, preferred_element_type=jnp.float32)
    scores = jnp.where(half_live, scores * scaling, negative)
    probs = jnp.where(half_live, jnp.exp(scores - lse_all), 0.0)
    dprobs = lax.dot_general(da_all, v_half, contract_last, preferred_element_type=jnp.float32)
    grad_scores = (probs * (dprobs - delta_all)).astype(jnp.bfloat16)
    grad_k = (
        lax.dot_general(grad_scores, q_all, contract_first, preferred_element_type=jnp.float32)
        * scaling
    )
    grad_v = lax.dot_general(
        probs.astype(jnp.bfloat16), da_all, contract_first, preferred_element_type=jnp.float32
    )
    grad_rows = jnp.stack([grad_q, grad_k, grad_v], axis=1).astype(jnp.bfloat16)
    grad_qkv = to_frames(grad_rows).transpose(1, 2, 0, 3).reshape(frame_count, 3 * width)
    back_normed = lax.dot_general(
        grad_qkv, w_proj[:, : 3 * width], contract_last, preferred_element_type=jnp.float32
    )
    unused_attn, pull_attn = jax.vjp(normalize, inputs, gain_attn)
    back_inputs, gain_attn_term = pull_attn(back_normed)
    grad_frames = (grad_resid + back_inputs).astype(jnp.bfloat16)[None]
    inner_part = lax.dot_general(
        normed_attn, grad_qkv, contract_first, preferred_element_type=jnp.float32
    )
    outer_part = lax.dot_general(
        grad_resid_low, attended, contract_first, preferred_element_type=jnp.float32
    )
    axes = ("dp", "tm")
    devices = lax.axis_size(axes)
    rows = inner_part.shape[0]
    small = jnp.concatenate([conv_term, gain_attn_term[None], gain_conv_term[None]], axis=0)
    small_count = small.size
    small_width = -(-small_count // rows)
    small_flat = jnp.pad(small.reshape(-1), (0, small_width * rows - small_count))
    packed = jnp.concatenate(
        [inner_part, outer_part, small_flat.reshape(rows, small_width)], axis=1
    )
    outer_count = lax.axis_size("dp")
    packed = packed.reshape(outer_count, tm_count, rows // devices, packed.shape[1])
    packed = packed.transpose(1, 0, 2, 3).astype(jnp.bfloat16)
    reduced = lax.all_to_all(packed, "tm", 0, 0, tiled=True).astype(jnp.float32).sum(0)
    big_cols = 4 * width
    spare = reduced[:, :, big_cols:].reshape(-1)
    spare_rows = -(-spare.size // big_cols)
    spare = jnp.pad(spare, (0, spare_rows * big_cols - spare.size)).reshape(spare_rows, big_cols)
    body = jnp.concatenate(
        [reduced[:, :, :big_cols], jnp.broadcast_to(spare, (outer_count,) + spare.shape)], axis=1
    )
    body = lax.all_to_all(body.astype(jnp.bfloat16), "dp", 0, 0, tiled=True)
    body = body.astype(jnp.float32).sum(0)
    grad_proj = body[: rows // devices]
    spread = rows // devices * small_width
    small_part = body[rows // devices :].reshape(1, -1)[:, : outer_count * spread]
    small_all = lax.all_to_all(
        jnp.broadcast_to(small_part, (tm_count, small_part.shape[1])), "tm", 0, 0, tiled=True
    )
    small_all = small_all.reshape(tm_count, outer_count, spread).transpose(1, 0, 2)
    small_sum = small_all.reshape(-1)[:small_count]
    conv_sum = small_sum[: conv_term.size].reshape(conv_term.shape)
    gains_sum = small_sum[conv_term.size :].reshape(2, -1)
    return (grad_frames, grad_proj * grad_scale, conv_sum * grad_scale, gains_sum * grad_scale)


def solution(mesh):
    return jax.shard_map(
        per_device,
        mesh=mesh,
        in_specs=(P("dp", "tm", None), P("dp", "tm", None), P("dp"), P(), P(), P(), P()),
        out_specs=(P("dp", "tm", None), P(("dp", "tm"), None), P(), P()),
        check_vma=False,
    )
```

```python
import math

import jax
import jax.numpy as jnp
from jax import lax
from jax.sharding import PartitionSpec as P

HEADS = 8
HDIM = 64
KER = 31


epsilon = 1e-05
negative = -1e30


def padded_2(value, sides, width):
    for axis, dim in sides:
        size, length = (lax.axis_size(axis), value.shape[dim])
        up = [(i, (i + 1) % size) for i in range(size - 1)]
        down = [(j, i) for i, j in up]
        last = lax.slice_in_dim(value, length - width, length, axis=dim)
        first = lax.slice_in_dim(value, 0, width, axis=dim)
        before = lax.ppermute(last, axis, up)
        after = lax.ppermute(first, axis, down)
        value = jnp.concatenate([before, value, after], axis=dim)
    return value


def normalize(inputs, gain):
    centre = inputs - jnp.mean(inputs, axis=-1, keepdims=True)
    spread = jnp.mean(centre * centre, axis=-1, keepdims=True)
    return centre * lax.rsqrt(spread + epsilon) * gain


def split_heads(matrix):
    return matrix.reshape(matrix.shape[0], HEADS, HDIM)


def over_blocks(advance, carried, members):
    total_rows = members[0].shape[0]
    stride = math.gcd(total_rows, 1024)

    def one_block(block_index, inner_state):
        offset = block_index * stride
        sliced = tuple((lax.dynamic_slice_in_dim(member, offset, stride, 0) for member in members))
        return advance(inner_state, sliced, offset)

    return lax.fori_loop(0, total_rows // stride, one_block, carried)


def forward_step(query_heads, length, scaling):

    def advance(carried, sliced, first_row):
        key_heads = split_heads(sliced[0])
        value_heads = split_heads(sliced[1])
        positions = first_row + jnp.arange(key_heads.shape[0], dtype=jnp.int32)
        living = (positions < length)[None, None, :]
        scores = (
            jnp.einsum("bhd,lhd->hbl", query_heads, key_heads, preferred_element_type=jnp.float32)
            * scaling
        )
        scores = jnp.where(living, scores, negative)
        top_old, total_old, accumulated = carried
        top_new = jnp.maximum(top_old, jnp.max(scores, axis=-1))
        weights = jnp.where(living, jnp.exp(scores - top_new[:, :, None]), 0.0)
        fading = jnp.exp(top_old - top_new)
        total_new = total_old * fading + jnp.sum(weights, axis=-1)
        update = jnp.einsum(
            "hbl,lhd->bhd",
            weights.astype(jnp.bfloat16),
            value_heads,
            preferred_element_type=jnp.float32,
        )
        return (top_new, total_new, accumulated * fading.T[:, :, None] + update)

    return advance


def query_side(query_heads, grad_heads, logsum, delta, length, scaling):

    def advance(carried, sliced, first_row):
        key_heads = split_heads(sliced[0])
        value_heads = split_heads(sliced[1])
        count_here = key_heads.shape[0]
        positions = first_row + jnp.arange(count_here, dtype=jnp.int32)
        living = (positions < length)[None, None, :]
        scores = (
            jnp.einsum("bhd,lhd->hbl", query_heads, key_heads, preferred_element_type=jnp.float32)
            * scaling
        )
        scores = jnp.where(living, scores, negative)
        probs = jnp.where(living, jnp.exp(scores - logsum.T[:, :, None]), 0.0)
        dprobs = jnp.einsum(
            "bhd,lhd->hbl", grad_heads, value_heads, preferred_element_type=jnp.float32
        )
        grad_scores = (probs * (dprobs - delta.T[:, :, None])).astype(jnp.bfloat16)
        grad_query = (
            carried[0]
            + jnp.einsum("hbl,lhd->bhd", grad_scores, key_heads, preferred_element_type=jnp.float32)
            * scaling
        )
        return (grad_query,)

    return advance


def key_side(key_heads, value_heads, own_living, scaling):

    def advance(carried, sliced, first_row):
        query_heads = split_heads(sliced[0].astype(jnp.bfloat16))
        grad_heads = split_heads(sliced[1].astype(jnp.bfloat16))
        logsum_block = sliced[2]
        delta_block = sliced[3]
        scores = (
            jnp.einsum("bhd,lhd->hbl", query_heads, key_heads, preferred_element_type=jnp.float32)
            * scaling
        )
        scores = jnp.where(own_living, scores, negative)
        probs = jnp.where(own_living, jnp.exp(scores - logsum_block.T[:, :, None]), 0.0)
        dprobs = jnp.einsum(
            "bhd,lhd->hbl", grad_heads, value_heads, preferred_element_type=jnp.float32
        )
        grad_scores = (probs * (dprobs - delta_block.T[:, :, None])).astype(jnp.bfloat16)
        grad_key = (
            carried[0]
            + jnp.einsum(
                "hbl,bhd->lhd", grad_scores, query_heads, preferred_element_type=jnp.float32
            )
            * scaling
        )
        grad_value = carried[1] + jnp.einsum(
            "hbl,bhd->lhd",
            probs.astype(jnp.bfloat16),
            grad_heads,
            preferred_element_type=jnp.float32,
        )
        return (grad_key, grad_value)

    return advance


def per_device(frames, cotangent, lengths, w_proj, gain_attn, gain_conv, w_conv):
    frame_count = frames.shape[1]
    width = HEADS * HDIM
    cycle_size = lax.axis_size("tm")
    own_start = lax.axis_index("tm") * frame_count
    length = lengths[0]
    scaling = 1.0 / math.sqrt(HDIM)
    total_frames = lax.axis_size("dp") * frames.shape[0] * frame_count * cycle_size
    grad_scale = 1.0 / math.sqrt(total_frames)
    contract_last = (((1,), (1,)), ((), ()))
    contract_first = (((0,), (0,)), ((), ()))
    inputs = frames[0].astype(jnp.float32)
    normed_attn = normalize(inputs, gain_attn).astype(jnp.bfloat16)
    projected = jnp.dot(
        normed_attn, w_proj[:, : 3 * width], preferred_element_type=jnp.float32
    ).astype(jnp.bfloat16)
    tm_count = lax.axis_size("tm")
    halves = tm_count // HEADS
    me = lax.axis_index("tm")
    half = me // HEADS
    span = frame_count * HEADS
    total = frame_count * tm_count
    key_live = (jnp.arange(total, dtype=jnp.int32) < length)[None, :]
    half_live = lax.dynamic_slice_in_dim(key_live, half * span, span, 1)
    qkv = projected.reshape(frame_count, 3, HEADS, HDIM).transpose(2, 0, 1, 3)
    got = lax.all_to_all(jnp.tile(qkv, (halves, 1, 1, 1)), "tm", 0, 0, tiled=True)
    got = got.reshape(total, 3, HDIM)
    q_all, k_all, v_all = got[:, 0], got[:, 1], got[:, 2]
    q_half = lax.dynamic_slice_in_dim(q_all, half * span, span, 0)
    scores = lax.dot_general(q_half, k_all, contract_last, preferred_element_type=jnp.float32)
    scores = jnp.where(key_live, scores * scaling, negative)
    top = jnp.max(scores, axis=-1)
    weights = jnp.where(key_live, jnp.exp(scores - top[:, None]), 0.0)
    summed = jnp.sum(weights, axis=-1)
    acc = jnp.dot(weights.astype(jnp.bfloat16), v_all, preferred_element_type=jnp.float32)
    a_half = (acc / summed[:, None]).astype(jnp.bfloat16)
    lse_half = top + jnp.log(summed)

    half_groups = [[part * HEADS + k for k in range(HEADS)] for part in range(halves)]

    def to_frames(rows):
        blocks = rows.reshape((HEADS, frame_count) + rows.shape[1:])
        return lax.all_to_all(blocks, "tm", 0, 0, tiled=True, axis_index_groups=half_groups)

    attended = to_frames(a_half).transpose(1, 0, 2).reshape(frame_count, width)
    w_out = w_proj[:, 3 * width :]
    mixed = inputs + lax.dot_general(
        attended, w_out, contract_last, preferred_element_type=jnp.float32
    )
    resid_f = mixed.astype(jnp.bfloat16).astype(jnp.float32)
    positions = own_start + jnp.arange(frame_count, dtype=jnp.int32)
    valid = (positions < length)[:, None]
    normed_conv = jnp.where(valid, normalize(resid_f, gain_conv), 0.0).astype(jnp.bfloat16)
    reach = KER // 2
    padded = padded_2(normed_conv, (("tm", 0),), reach).astype(jnp.float32)
    kernel = w_conv.astype(jnp.float32)
    conv = jnp.zeros((frame_count, padded.shape[1]), jnp.float32)
    for shift_index in range(KER):
        conv = conv + kernel[shift_index] * padded[shift_index : shift_index + frame_count]
    upstream = cotangent[0].astype(jnp.float32)
    gate = jax.nn.sigmoid(conv)
    grad_conv_in = upstream * gate * (1.0 + conv * (1.0 - gate))
    conv_term = jnp.stack(
        [
            jnp.sum(grad_conv_in * padded[shift_index : shift_index + frame_count], axis=0)
            for shift_index in range(KER)
        ]
    )
    grad_padded = padded_2(grad_conv_in.astype(jnp.bfloat16), (("tm", 0),), reach).astype(
        grad_conv_in.dtype
    )
    grad_normed = jnp.zeros_like(grad_conv_in)
    for shift_index in range(KER):
        begin = 2 * reach - shift_index
        grad_normed = grad_normed + kernel[shift_index] * grad_padded[begin : begin + frame_count]
    grad_normed = jnp.where(valid, grad_normed, 0.0)
    unused_conv, pull_conv = jax.vjp(normalize, resid_f, gain_conv)
    back_resid, gain_conv_term = pull_conv(grad_normed)
    grad_resid = upstream + back_resid
    grad_resid_low = grad_resid.astype(jnp.bfloat16)
    grad_attended = jnp.dot(grad_resid_low, w_out, preferred_element_type=jnp.float32).astype(
        jnp.bfloat16
    )
    send_grad = grad_attended.reshape(frame_count, HEADS, HDIM).transpose(1, 0, 2)
    da_all = lax.all_to_all(jnp.tile(send_grad, (halves, 1, 1)), "tm", 0, 0, tiled=True)
    da_all = da_all.reshape(total, HDIM)
    da_half = lax.dynamic_slice_in_dim(da_all, half * span, span, 0)
    delta_half = jnp.sum(da_half.astype(jnp.float32) * a_half.astype(jnp.float32), axis=-1)
    stats_half = jnp.stack([lse_half, delta_half], axis=0)
    partner = lax.ppermute(
        stats_half, "tm", [(i, (i + HEADS) % tm_count) for i in range(tm_count)]
    )
    stats_all = jnp.where(
        half == 0,
        jnp.concatenate([stats_half, partner], axis=1),
        jnp.concatenate([partner, stats_half], axis=1),
    )
    lse_all = stats_all[0][:, None]
    delta_all = stats_all[1][:, None]
    scores = lax.dot_general(q_half, k_all, contract_last, preferred_element_type=jnp.float32)
    scores = jnp.where(key_live, scores * scaling, negative)
    probs = jnp.where(key_live, jnp.exp(scores - lse_half[:, None]), 0.0)
    dprobs = lax.dot_general(da_half, v_all, contract_last, preferred_element_type=jnp.float32)
    grad_scores = (probs * (dprobs - delta_half[:, None])).astype(jnp.bfloat16)
    grad_q = jnp.dot(grad_scores, k_all, preferred_element_type=jnp.float32) * scaling
    k_half = lax.dynamic_slice_in_dim(k_all, half * span, span, 0)
    v_half = lax.dynamic_slice_in_dim(v_all, half * span, span, 0)
    scores = lax.dot_general(q_all, k_half, contract_last, preferred_element_type=jnp.float32)
    scores = jnp.where(half_live, scores * scaling, negative)
    probs = jnp.where(half_live, jnp.exp(scores - lse_all), 0.0)
    dprobs = lax.dot_general(da_all, v_half, contract_last, preferred_element_type=jnp.float32)
    grad_scores = (probs * (dprobs - delta_all)).astype(jnp.bfloat16)
    grad_k = (
        lax.dot_general(grad_scores, q_all, contract_first, preferred_element_type=jnp.float32)
        * scaling
    )
    grad_v = lax.dot_general(
        probs.astype(jnp.bfloat16), da_all, contract_first, preferred_element_type=jnp.float32
    )
    grad_rows = jnp.stack([grad_q, grad_k, grad_v], axis=1).astype(jnp.bfloat16)
    grad_qkv = to_frames(grad_rows).transpose(1, 2, 0, 3).reshape(frame_count, 3 * width)
    back_normed = lax.dot_general(
        grad_qkv, w_proj[:, : 3 * width], contract_last, preferred_element_type=jnp.float32
    )
    unused_attn, pull_attn = jax.vjp(normalize, inputs, gain_attn)
    back_inputs, gain_attn_term = pull_attn(back_normed)
    grad_frames = (grad_resid + back_inputs).astype(jnp.bfloat16)[None]
    inner_part = lax.dot_general(
        normed_attn, grad_qkv, contract_first, preferred_element_type=jnp.float32
    )
    outer_part = lax.dot_general(
        grad_resid_low, attended, contract_first, preferred_element_type=jnp.float32
    )
    axes = ("dp", "tm")
    devices = lax.axis_size(axes)
    rows = inner_part.shape[0]
    small = jnp.concatenate([conv_term, gain_attn_term[None], gain_conv_term[None]], axis=0)
    small_count = small.size
    small_width = -(-small_count // rows)
    small_flat = jnp.pad(small.reshape(-1), (0, small_width * rows - small_count))
    packed = jnp.concatenate(
        [inner_part, outer_part, small_flat.reshape(rows, small_width)], axis=1
    )
    outer_count = lax.axis_size("dp")
    cores = 2
    chips = tm_count // cores
    pairs = [[cores * k + c for c in range(cores)] for k in range(chips)]
    same_core = [[cores * k + c for k in range(chips)] for c in range(cores)]
    cols = packed.shape[1]
    packed = packed.reshape(outer_count, chips, cores, rows // devices, cols)
    packed = packed.transpose(2, 0, 1, 3, 4).astype(jnp.bfloat16)
    reduced = lax.all_to_all(packed, "tm", 0, 0, tiled=True, axis_index_groups=pairs)
    reduced = reduced.astype(jnp.float32).sum(0).transpose(1, 0, 2, 3).astype(jnp.bfloat16)
    reduced = lax.all_to_all(reduced, "tm", 0, 0, tiled=True, axis_index_groups=same_core)
    reduced = reduced.astype(jnp.float32).sum(0)
    big_cols = 4 * width
    spare = reduced[:, :, big_cols:].reshape(-1)
    spare_rows = -(-spare.size // big_cols)
    spare = jnp.pad(spare, (0, spare_rows * big_cols - spare.size)).reshape(spare_rows, big_cols)
    body = jnp.concatenate(
        [reduced[:, :, :big_cols], jnp.broadcast_to(spare, (outer_count,) + spare.shape)], axis=1
    )
    body = lax.all_to_all(body.astype(jnp.bfloat16), "dp", 0, 0, tiled=True)
    body = body.astype(jnp.float32).sum(0)
    grad_proj = body[: rows // devices]
    spread = rows // devices * small_width
    small_part = body[rows // devices :].reshape(1, -1)[:, : outer_count * spread]
    small_all = lax.all_to_all(
        jnp.broadcast_to(small_part, (tm_count, small_part.shape[1])), "tm", 0, 0, tiled=True
    )
    small_all = small_all.reshape(tm_count, outer_count, spread).transpose(1, 0, 2)
    small_sum = small_all.reshape(-1)[:small_count]
    conv_sum = small_sum[: conv_term.size].reshape(conv_term.shape)
    gains_sum = small_sum[conv_term.size :].reshape(2, -1)
    return (grad_frames, grad_proj * grad_scale, conv_sum * grad_scale, gains_sum * grad_scale)


def solution(mesh):
    return jax.shard_map(
        per_device,
        mesh=mesh,
        in_specs=(P("dp", "tm", None), P("dp", "tm", None), P("dp"), P(), P(), P(), P()),
        out_specs=(P("dp", "tm", None), P(("dp", "tm"), None), P(), P()),
        check_vma=False,
    )
```

```python
import math

import jax
import jax.numpy as jnp
from jax import lax
from jax.sharding import PartitionSpec as P

HEADS = 8
HDIM = 64
KER = 31


epsilon = 1e-05
negative = -1e30


def padded_2(value, sides, width):
    for axis, dim in sides:
        size, length = (lax.axis_size(axis), value.shape[dim])
        up = [(i, (i + 1) % size) for i in range(size - 1)]
        down = [(j, i) for i, j in up]
        last = lax.slice_in_dim(value, length - width, length, axis=dim)
        first = lax.slice_in_dim(value, 0, width, axis=dim)
        before = lax.ppermute(last, axis, up)
        after = lax.ppermute(first, axis, down)
        value = jnp.concatenate([before, value, after], axis=dim)
    return value


def normalize(inputs, gain):
    centre = inputs - jnp.mean(inputs, axis=-1, keepdims=True)
    spread = jnp.mean(centre * centre, axis=-1, keepdims=True)
    return centre * lax.rsqrt(spread + epsilon) * gain


def split_heads(matrix):
    return matrix.reshape(matrix.shape[0], HEADS, HDIM)


def over_blocks(advance, carried, members):
    total_rows = members[0].shape[0]
    stride = math.gcd(total_rows, 1024)

    def one_block(block_index, inner_state):
        offset = block_index * stride
        sliced = tuple((lax.dynamic_slice_in_dim(member, offset, stride, 0) for member in members))
        return advance(inner_state, sliced, offset)

    return lax.fori_loop(0, total_rows // stride, one_block, carried)


def forward_step(query_heads, length, scaling):

    def advance(carried, sliced, first_row):
        key_heads = split_heads(sliced[0])
        value_heads = split_heads(sliced[1])
        positions = first_row + jnp.arange(key_heads.shape[0], dtype=jnp.int32)
        living = (positions < length)[None, None, :]
        scores = (
            jnp.einsum("bhd,lhd->hbl", query_heads, key_heads, preferred_element_type=jnp.float32)
            * scaling
        )
        scores = jnp.where(living, scores, negative)
        top_old, total_old, accumulated = carried
        top_new = jnp.maximum(top_old, jnp.max(scores, axis=-1))
        weights = jnp.where(living, jnp.exp(scores - top_new[:, :, None]), 0.0)
        fading = jnp.exp(top_old - top_new)
        total_new = total_old * fading + jnp.sum(weights, axis=-1)
        update = jnp.einsum(
            "hbl,lhd->bhd",
            weights.astype(jnp.bfloat16),
            value_heads,
            preferred_element_type=jnp.float32,
        )
        return (top_new, total_new, accumulated * fading.T[:, :, None] + update)

    return advance


def query_side(query_heads, grad_heads, logsum, delta, length, scaling):

    def advance(carried, sliced, first_row):
        key_heads = split_heads(sliced[0])
        value_heads = split_heads(sliced[1])
        count_here = key_heads.shape[0]
        positions = first_row + jnp.arange(count_here, dtype=jnp.int32)
        living = (positions < length)[None, None, :]
        scores = (
            jnp.einsum("bhd,lhd->hbl", query_heads, key_heads, preferred_element_type=jnp.float32)
            * scaling
        )
        scores = jnp.where(living, scores, negative)
        probs = jnp.where(living, jnp.exp(scores - logsum.T[:, :, None]), 0.0)
        dprobs = jnp.einsum(
            "bhd,lhd->hbl", grad_heads, value_heads, preferred_element_type=jnp.float32
        )
        grad_scores = (probs * (dprobs - delta.T[:, :, None])).astype(jnp.bfloat16)
        grad_query = (
            carried[0]
            + jnp.einsum("hbl,lhd->bhd", grad_scores, key_heads, preferred_element_type=jnp.float32)
            * scaling
        )
        return (grad_query,)

    return advance


def key_side(key_heads, value_heads, own_living, scaling):

    def advance(carried, sliced, first_row):
        query_heads = split_heads(sliced[0].astype(jnp.bfloat16))
        grad_heads = split_heads(sliced[1].astype(jnp.bfloat16))
        logsum_block = sliced[2]
        delta_block = sliced[3]
        scores = (
            jnp.einsum("bhd,lhd->hbl", query_heads, key_heads, preferred_element_type=jnp.float32)
            * scaling
        )
        scores = jnp.where(own_living, scores, negative)
        probs = jnp.where(own_living, jnp.exp(scores - logsum_block.T[:, :, None]), 0.0)
        dprobs = jnp.einsum(
            "bhd,lhd->hbl", grad_heads, value_heads, preferred_element_type=jnp.float32
        )
        grad_scores = (probs * (dprobs - delta_block.T[:, :, None])).astype(jnp.bfloat16)
        grad_key = (
            carried[0]
            + jnp.einsum(
                "hbl,bhd->lhd", grad_scores, query_heads, preferred_element_type=jnp.float32
            )
            * scaling
        )
        grad_value = carried[1] + jnp.einsum(
            "hbl,bhd->lhd",
            probs.astype(jnp.bfloat16),
            grad_heads,
            preferred_element_type=jnp.float32,
        )
        return (grad_key, grad_value)

    return advance


def per_device(frames, cotangent, lengths, w_proj, gain_attn, gain_conv, w_conv):
    frame_count = frames.shape[1]
    width = HEADS * HDIM
    cycle_size = lax.axis_size("tm")
    own_start = lax.axis_index("tm") * frame_count
    length = lengths[0]
    scaling = 1.0 / math.sqrt(HDIM)
    total_frames = lax.axis_size("dp") * frames.shape[0] * frame_count * cycle_size
    grad_scale = 1.0 / math.sqrt(total_frames)
    contract_last = (((1,), (1,)), ((), ()))
    contract_first = (((0,), (0,)), ((), ()))
    inputs = frames[0].astype(jnp.float32)
    normed_attn = normalize(inputs, gain_attn).astype(jnp.bfloat16)
    projected = jnp.dot(
        normed_attn, w_proj[:, : 3 * width], preferred_element_type=jnp.float32
    ).astype(jnp.bfloat16)
    tm_count = lax.axis_size("tm")
    halves = tm_count // HEADS
    me = lax.axis_index("tm")
    half = me // HEADS
    span = frame_count * HEADS
    total = frame_count * tm_count
    key_live = (jnp.arange(total, dtype=jnp.int32) < length)[None, :]
    half_live = lax.dynamic_slice_in_dim(key_live, half * span, span, 1)
    qkv = projected.reshape(frame_count, 3, HEADS, HDIM).transpose(2, 0, 1, 3)
    got = lax.all_to_all(jnp.tile(qkv, (halves, 1, 1, 1)), "tm", 0, 0, tiled=True)
    got = got.reshape(total, 3, HDIM)
    q_all, k_all, v_all = got[:, 0], got[:, 1], got[:, 2]
    q_half = lax.dynamic_slice_in_dim(q_all, half * span, span, 0)
    scores = lax.dot_general(q_half, k_all, contract_last, preferred_element_type=jnp.float32)
    scores = jnp.where(key_live, scores * scaling, negative)
    top = jnp.max(scores, axis=-1)
    weights = jnp.where(key_live, jnp.exp(scores - top[:, None]), 0.0)
    summed = jnp.sum(weights, axis=-1)
    acc = jnp.dot(weights.astype(jnp.bfloat16), v_all, preferred_element_type=jnp.float32)
    a_half = (acc / summed[:, None]).astype(jnp.bfloat16)
    lse_half = top + jnp.log(summed)

    half_groups = [[part * HEADS + k for k in range(HEADS)] for part in range(halves)]

    def to_frames(rows):
        blocks = rows.reshape((HEADS, frame_count) + rows.shape[1:])
        return lax.all_to_all(blocks, "tm", 0, 0, tiled=True, axis_index_groups=half_groups)

    attended = to_frames(a_half).transpose(1, 0, 2).reshape(frame_count, width)
    w_out = w_proj[:, 3 * width :]
    mixed = inputs + lax.dot_general(
        attended, w_out, contract_last, preferred_element_type=jnp.float32
    )
    resid_f = mixed.astype(jnp.bfloat16).astype(jnp.float32)
    positions = own_start + jnp.arange(frame_count, dtype=jnp.int32)
    valid = (positions < length)[:, None]
    normed_conv = jnp.where(valid, normalize(resid_f, gain_conv), 0.0).astype(jnp.bfloat16)
    reach = KER // 2
    padded = padded_2(normed_conv, (("tm", 0),), reach).astype(jnp.float32)
    kernel = w_conv.astype(jnp.float32)
    conv = jnp.zeros((frame_count, padded.shape[1]), jnp.float32)
    for shift_index in range(KER):
        conv = conv + kernel[shift_index] * padded[shift_index : shift_index + frame_count]
    upstream = cotangent[0].astype(jnp.float32)
    gate = jax.nn.sigmoid(conv)
    grad_conv_in = upstream * gate * (1.0 + conv * (1.0 - gate))
    conv_term = jnp.stack(
        [
            jnp.sum(grad_conv_in * padded[shift_index : shift_index + frame_count], axis=0)
            for shift_index in range(KER)
        ]
    )
    grad_padded = padded_2(grad_conv_in.astype(jnp.bfloat16), (("tm", 0),), reach).astype(
        grad_conv_in.dtype
    )
    grad_normed = jnp.zeros_like(grad_conv_in)
    for shift_index in range(KER):
        begin = 2 * reach - shift_index
        grad_normed = grad_normed + kernel[shift_index] * grad_padded[begin : begin + frame_count]
    grad_normed = jnp.where(valid, grad_normed, 0.0)
    unused_conv, pull_conv = jax.vjp(normalize, resid_f, gain_conv)
    back_resid, gain_conv_term = pull_conv(grad_normed)
    grad_resid = upstream + back_resid
    grad_resid_low = grad_resid.astype(jnp.bfloat16)
    grad_attended = jnp.dot(grad_resid_low, w_out, preferred_element_type=jnp.float32).astype(
        jnp.bfloat16
    )
    send_grad = grad_attended.reshape(frame_count, HEADS, HDIM).transpose(1, 0, 2)
    da_all = lax.all_to_all(jnp.tile(send_grad, (halves, 1, 1)), "tm", 0, 0, tiled=True)
    da_all = da_all.reshape(total, HDIM)
    da_half = lax.dynamic_slice_in_dim(da_all, half * span, span, 0)
    delta_half = jnp.sum(da_half.astype(jnp.float32) * a_half.astype(jnp.float32), axis=-1)
    stats_half = jnp.stack([lse_half, delta_half], axis=0)
    partner = lax.ppermute(
        stats_half, "tm", [(i, (i + HEADS) % tm_count) for i in range(tm_count)]
    )
    stats_all = jnp.where(
        half == 0,
        jnp.concatenate([stats_half, partner], axis=1),
        jnp.concatenate([partner, stats_half], axis=1),
    )
    lse_all = stats_all[0][:, None]
    delta_all = stats_all[1][:, None]
    scores = lax.dot_general(q_half, k_all, contract_last, preferred_element_type=jnp.float32)
    scores = jnp.where(key_live, scores * scaling, negative)
    probs = jnp.where(key_live, jnp.exp(scores - lse_half[:, None]), 0.0)
    dprobs = lax.dot_general(da_half, v_all, contract_last, preferred_element_type=jnp.float32)
    grad_scores = (probs * (dprobs - delta_half[:, None])).astype(jnp.bfloat16)
    grad_q = jnp.dot(grad_scores, k_all, preferred_element_type=jnp.float32) * scaling
    k_half = lax.dynamic_slice_in_dim(k_all, half * span, span, 0)
    v_half = lax.dynamic_slice_in_dim(v_all, half * span, span, 0)
    scores = lax.dot_general(q_all, k_half, contract_last, preferred_element_type=jnp.float32)
    scores = jnp.where(half_live, scores * scaling, negative)
    probs = jnp.where(half_live, jnp.exp(scores - lse_all), 0.0)
    dprobs = lax.dot_general(da_all, v_half, contract_last, preferred_element_type=jnp.float32)
    grad_scores = (probs * (dprobs - delta_all)).astype(jnp.bfloat16)
    grad_k = (
        lax.dot_general(grad_scores, q_all, contract_first, preferred_element_type=jnp.float32)
        * scaling
    )
    grad_v = lax.dot_general(
        probs.astype(jnp.bfloat16), da_all, contract_first, preferred_element_type=jnp.float32
    )
    grad_rows = jnp.stack([grad_q, grad_k, grad_v], axis=1).astype(jnp.bfloat16)
    grad_qkv = to_frames(grad_rows).transpose(1, 2, 0, 3).reshape(frame_count, 3 * width)
    back_normed = lax.dot_general(
        grad_qkv, w_proj[:, : 3 * width], contract_last, preferred_element_type=jnp.float32
    )
    unused_attn, pull_attn = jax.vjp(normalize, inputs, gain_attn)
    back_inputs, gain_attn_term = pull_attn(back_normed)
    grad_frames = (grad_resid + back_inputs).astype(jnp.bfloat16)[None]
    inner_part = lax.dot_general(
        normed_attn, grad_qkv, contract_first, preferred_element_type=jnp.float32
    )
    outer_part = lax.dot_general(
        grad_resid_low, attended, contract_first, preferred_element_type=jnp.float32
    )
    axes = ("dp", "tm")
    devices = lax.axis_size(axes)
    rows = inner_part.shape[0]
    small = jnp.concatenate([conv_term, gain_attn_term[None], gain_conv_term[None]], axis=0)
    small_count = small.size
    small_width = -(-small_count // rows)
    small_flat = jnp.pad(small.reshape(-1), (0, small_width * rows - small_count))
    packed = jnp.concatenate(
        [inner_part, outer_part, small_flat.reshape(rows, small_width)], axis=1
    )
    outer_count = lax.axis_size("dp")
    cores = 2
    chips = tm_count // cores
    pairs = [[cores * k + c for c in range(cores)] for k in range(chips)]
    same_core = [[cores * k + c for k in range(chips)] for c in range(cores)]
    cols = packed.shape[1]
    packed = packed.reshape(outer_count, chips, cores, rows // devices, cols)
    packed = packed.transpose(2, 0, 1, 3, 4).astype(jnp.bfloat16)
    reduced = lax.all_to_all(packed, "tm", 0, 0, tiled=True, axis_index_groups=pairs)
    reduced = reduced.astype(jnp.float32).sum(0).transpose(1, 0, 2, 3).astype(jnp.bfloat16)
    reduced = lax.all_to_all(reduced, "tm", 0, 0, tiled=True, axis_index_groups=same_core)
    reduced = reduced.astype(jnp.float32).sum(0)
    big_cols = 4 * width
    spare = reduced[:, :, big_cols:].reshape(-1)
    spare_rows = -(-spare.size // big_cols)
    spare = jnp.pad(spare, (0, spare_rows * big_cols - spare.size)).reshape(spare_rows, big_cols)
    body = jnp.concatenate(
        [reduced[:, :, :big_cols], jnp.broadcast_to(spare, (outer_count,) + spare.shape)], axis=1
    )
    rings = 2
    ring_size = outer_count // rings
    across = [[r * ring_size + z for r in range(rings)] for z in range(ring_size)]
    along = [[r * ring_size + z for z in range(ring_size)] for r in range(rings)]
    body = body.reshape((rings, ring_size) + body.shape[1:]).astype(jnp.bfloat16)
    body = lax.all_to_all(body, "dp", 0, 0, tiled=True, axis_index_groups=across)
    body = body.astype(jnp.float32).sum(0).astype(jnp.bfloat16)
    body = lax.all_to_all(body, "dp", 0, 0, tiled=True, axis_index_groups=along)
    body = body.astype(jnp.float32).sum(0)
    grad_proj = body[: rows // devices]
    spread = rows // devices * small_width
    small_part = body[rows // devices :].reshape(1, -1)[:, : outer_count * spread]
    small_all = lax.all_to_all(
        jnp.broadcast_to(small_part, (tm_count, small_part.shape[1])), "tm", 0, 0, tiled=True
    )
    small_all = small_all.reshape(tm_count, outer_count, spread).transpose(1, 0, 2)
    small_sum = small_all.reshape(-1)[:small_count]
    conv_sum = small_sum[: conv_term.size].reshape(conv_term.shape)
    gains_sum = small_sum[conv_term.size :].reshape(2, -1)
    return (grad_frames, grad_proj * grad_scale, conv_sum * grad_scale, gains_sum * grad_scale)


def solution(mesh):
    return jax.shard_map(
        per_device,
        mesh=mesh,
        in_specs=(P("dp", "tm", None), P("dp", "tm", None), P("dp"), P(), P(), P(), P()),
        out_specs=(P("dp", "tm", None), P(("dp", "tm"), None), P(), P()),
        check_vma=False,
    )
```

```python
import math

import jax
import jax.numpy as jnp
from jax import lax
from jax.sharding import PartitionSpec as P

HEADS = 8
HDIM = 64
KER = 31


epsilon = 1e-05
negative = -1e30


def padded_2(value, sides, width):
    for axis, dim in sides:
        size, length = (lax.axis_size(axis), value.shape[dim])
        up = [(i, (i + 1) % size) for i in range(size - 1)]
        down = [(j, i) for i, j in up]
        last = lax.slice_in_dim(value, length - width, length, axis=dim)
        first = lax.slice_in_dim(value, 0, width, axis=dim)
        before = lax.ppermute(last, axis, up)
        after = lax.ppermute(first, axis, down)
        value = jnp.concatenate([before, value, after], axis=dim)
    return value


def normalize(inputs, gain):
    centre = inputs - jnp.mean(inputs, axis=-1, keepdims=True)
    spread = jnp.mean(centre * centre, axis=-1, keepdims=True)
    return centre * lax.rsqrt(spread + epsilon) * gain


def split_heads(matrix):
    return matrix.reshape(matrix.shape[0], HEADS, HDIM)


def over_blocks(advance, carried, members):
    total_rows = members[0].shape[0]
    stride = math.gcd(total_rows, 1024)

    def one_block(block_index, inner_state):
        offset = block_index * stride
        sliced = tuple((lax.dynamic_slice_in_dim(member, offset, stride, 0) for member in members))
        return advance(inner_state, sliced, offset)

    return lax.fori_loop(0, total_rows // stride, one_block, carried)


def forward_step(query_heads, length, scaling):

    def advance(carried, sliced, first_row):
        key_heads = split_heads(sliced[0])
        value_heads = split_heads(sliced[1])
        positions = first_row + jnp.arange(key_heads.shape[0], dtype=jnp.int32)
        living = (positions < length)[None, None, :]
        scores = (
            jnp.einsum("bhd,lhd->hbl", query_heads, key_heads, preferred_element_type=jnp.float32)
            * scaling
        )
        scores = jnp.where(living, scores, negative)
        top_old, total_old, accumulated = carried
        top_new = jnp.maximum(top_old, jnp.max(scores, axis=-1))
        weights = jnp.where(living, jnp.exp(scores - top_new[:, :, None]), 0.0)
        fading = jnp.exp(top_old - top_new)
        total_new = total_old * fading + jnp.sum(weights, axis=-1)
        update = jnp.einsum(
            "hbl,lhd->bhd",
            weights.astype(jnp.bfloat16),
            value_heads,
            preferred_element_type=jnp.float32,
        )
        return (top_new, total_new, accumulated * fading.T[:, :, None] + update)

    return advance


def query_side(query_heads, grad_heads, logsum, delta, length, scaling):

    def advance(carried, sliced, first_row):
        key_heads = split_heads(sliced[0])
        value_heads = split_heads(sliced[1])
        count_here = key_heads.shape[0]
        positions = first_row + jnp.arange(count_here, dtype=jnp.int32)
        living = (positions < length)[None, None, :]
        scores = (
            jnp.einsum("bhd,lhd->hbl", query_heads, key_heads, preferred_element_type=jnp.float32)
            * scaling
        )
        scores = jnp.where(living, scores, negative)
        probs = jnp.where(living, jnp.exp(scores - logsum.T[:, :, None]), 0.0)
        dprobs = jnp.einsum(
            "bhd,lhd->hbl", grad_heads, value_heads, preferred_element_type=jnp.float32
        )
        grad_scores = (probs * (dprobs - delta.T[:, :, None])).astype(jnp.bfloat16)
        grad_query = (
            carried[0]
            + jnp.einsum("hbl,lhd->bhd", grad_scores, key_heads, preferred_element_type=jnp.float32)
            * scaling
        )
        return (grad_query,)

    return advance


def key_side(key_heads, value_heads, own_living, scaling):

    def advance(carried, sliced, first_row):
        query_heads = split_heads(sliced[0].astype(jnp.bfloat16))
        grad_heads = split_heads(sliced[1].astype(jnp.bfloat16))
        logsum_block = sliced[2]
        delta_block = sliced[3]
        scores = (
            jnp.einsum("bhd,lhd->hbl", query_heads, key_heads, preferred_element_type=jnp.float32)
            * scaling
        )
        scores = jnp.where(own_living, scores, negative)
        probs = jnp.where(own_living, jnp.exp(scores - logsum_block.T[:, :, None]), 0.0)
        dprobs = jnp.einsum(
            "bhd,lhd->hbl", grad_heads, value_heads, preferred_element_type=jnp.float32
        )
        grad_scores = (probs * (dprobs - delta_block.T[:, :, None])).astype(jnp.bfloat16)
        grad_key = (
            carried[0]
            + jnp.einsum(
                "hbl,bhd->lhd", grad_scores, query_heads, preferred_element_type=jnp.float32
            )
            * scaling
        )
        grad_value = carried[1] + jnp.einsum(
            "hbl,bhd->lhd",
            probs.astype(jnp.bfloat16),
            grad_heads,
            preferred_element_type=jnp.float32,
        )
        return (grad_key, grad_value)

    return advance


def per_device(frames, cotangent, lengths, w_proj, gain_attn, gain_conv, w_conv):
    frame_count = frames.shape[1]
    width = HEADS * HDIM
    cycle_size = lax.axis_size("tm")
    own_start = lax.axis_index("tm") * frame_count
    length = lengths[0]
    scaling = 1.0 / math.sqrt(HDIM)
    total_frames = lax.axis_size("dp") * frames.shape[0] * frame_count * cycle_size
    grad_scale = 1.0 / math.sqrt(total_frames)
    contract_last = (((1,), (1,)), ((), ()))
    contract_first = (((0,), (0,)), ((), ()))
    inputs = frames[0].astype(jnp.float32)
    normed_attn = normalize(inputs, gain_attn).astype(jnp.bfloat16)
    projected = jnp.dot(
        normed_attn, w_proj[:, : 3 * width], preferred_element_type=jnp.float32
    ).astype(jnp.bfloat16)
    tm_count = lax.axis_size("tm")
    halves = tm_count // HEADS
    me = lax.axis_index("tm")
    half = me // HEADS
    span = frame_count * HEADS
    total = frame_count * tm_count
    key_live = (jnp.arange(total, dtype=jnp.int32) < length)[None, :]
    half_live = lax.dynamic_slice_in_dim(key_live, half * span, span, 1)
    qkv = projected.reshape(frame_count, 3, HEADS, HDIM).transpose(2, 0, 1, 3)
    got = lax.all_to_all(jnp.tile(qkv, (halves, 1, 1, 1)), "tm", 0, 0, tiled=True)
    got = got.reshape(total, 3, HDIM)
    q_all, k_all, v_all = got[:, 0], got[:, 1], got[:, 2]
    q_half = lax.dynamic_slice_in_dim(q_all, half * span, span, 0)
    scores = lax.dot_general(q_half, k_all, contract_last, preferred_element_type=jnp.float32)
    scores = jnp.where(key_live, scores * scaling, negative)
    top = jnp.max(scores, axis=-1)
    weights = jnp.where(key_live, jnp.exp(scores - top[:, None]), 0.0)
    summed = jnp.sum(weights, axis=-1)
    acc = jnp.dot(weights.astype(jnp.bfloat16), v_all, preferred_element_type=jnp.float32)
    a_half = (acc / summed[:, None]).astype(jnp.bfloat16)
    lse_half = top + jnp.log(summed)

    half_groups = [[part * HEADS + k for k in range(HEADS)] for part in range(halves)]

    def to_frames(rows):
        blocks = rows.reshape((HEADS, frame_count) + rows.shape[1:])
        return lax.all_to_all(blocks, "tm", 0, 0, tiled=True, axis_index_groups=half_groups)

    attended = to_frames(a_half).transpose(1, 0, 2).reshape(frame_count, width)
    w_out = w_proj[:, 3 * width :]
    mixed = inputs + lax.dot_general(
        attended, w_out, contract_last, preferred_element_type=jnp.float32
    )
    resid_f = mixed.astype(jnp.bfloat16).astype(jnp.float32)
    positions = own_start + jnp.arange(frame_count, dtype=jnp.int32)
    valid = (positions < length)[:, None]
    normed_conv = jnp.where(valid, normalize(resid_f, gain_conv), 0.0).astype(jnp.bfloat16)
    reach = KER // 2
    padded = padded_2(normed_conv, (("tm", 0),), reach).astype(jnp.float32)
    kernel = w_conv.astype(jnp.float32)
    conv = jnp.zeros((frame_count, padded.shape[1]), jnp.float32)
    for shift_index in range(KER):
        conv = conv + kernel[shift_index] * padded[shift_index : shift_index + frame_count]
    upstream = cotangent[0].astype(jnp.float32)
    gate = jax.nn.sigmoid(conv)
    grad_conv_in = upstream * gate * (1.0 + conv * (1.0 - gate))
    conv_term = jnp.stack(
        [
            jnp.sum(grad_conv_in * padded[shift_index : shift_index + frame_count], axis=0)
            for shift_index in range(KER)
        ]
    )
    grad_padded = padded_2(grad_conv_in.astype(jnp.bfloat16), (("tm", 0),), reach).astype(
        grad_conv_in.dtype
    )
    grad_normed = jnp.zeros_like(grad_conv_in)
    for shift_index in range(KER):
        begin = 2 * reach - shift_index
        grad_normed = grad_normed + kernel[shift_index] * grad_padded[begin : begin + frame_count]
    grad_normed = jnp.where(valid, grad_normed, 0.0)
    unused_conv, pull_conv = jax.vjp(normalize, resid_f, gain_conv)
    back_resid, gain_conv_term = pull_conv(grad_normed)
    grad_resid = upstream + back_resid
    grad_resid_low = grad_resid.astype(jnp.bfloat16)
    grad_attended = jnp.dot(grad_resid_low, w_out, preferred_element_type=jnp.float32).astype(
        jnp.bfloat16
    )
    send_grad = grad_attended.reshape(frame_count, HEADS, HDIM).transpose(1, 0, 2)
    da_all = lax.all_to_all(jnp.tile(send_grad, (halves, 1, 1)), "tm", 0, 0, tiled=True)
    da_all = da_all.reshape(total, HDIM)
    da_half = lax.dynamic_slice_in_dim(da_all, half * span, span, 0)
    delta_half = jnp.sum(da_half.astype(jnp.float32) * a_half.astype(jnp.float32), axis=-1)
    stats_half = jnp.stack([lse_half, delta_half], axis=0)
    partner = lax.ppermute(
        stats_half, "tm", [(i, (i + HEADS) % tm_count) for i in range(tm_count)]
    )
    stats_all = jnp.where(
        half == 0,
        jnp.concatenate([stats_half, partner], axis=1),
        jnp.concatenate([partner, stats_half], axis=1),
    )
    lse_all = stats_all[0][:, None]
    delta_all = stats_all[1][:, None]
    scores = lax.dot_general(q_half, k_all, contract_last, preferred_element_type=jnp.float32)
    scores = jnp.where(key_live, scores * scaling, negative)
    probs = jnp.where(key_live, jnp.exp(scores - lse_half[:, None]), 0.0)
    dprobs = lax.dot_general(da_half, v_all, contract_last, preferred_element_type=jnp.float32)
    grad_scores = (probs * (dprobs - delta_half[:, None])).astype(jnp.bfloat16)
    grad_q = jnp.dot(grad_scores, k_all, preferred_element_type=jnp.float32) * scaling
    k_half = lax.dynamic_slice_in_dim(k_all, half * span, span, 0)
    v_half = lax.dynamic_slice_in_dim(v_all, half * span, span, 0)
    scores = lax.dot_general(q_all, k_half, contract_last, preferred_element_type=jnp.float32)
    scores = jnp.where(half_live, scores * scaling, negative)
    probs = jnp.where(half_live, jnp.exp(scores - lse_all), 0.0)
    dprobs = lax.dot_general(da_all, v_half, contract_last, preferred_element_type=jnp.float32)
    grad_scores = (probs * (dprobs - delta_all)).astype(jnp.bfloat16)
    grad_k = (
        lax.dot_general(grad_scores, q_all, contract_first, preferred_element_type=jnp.float32)
        * scaling
    )
    grad_v = lax.dot_general(
        probs.astype(jnp.bfloat16), da_all, contract_first, preferred_element_type=jnp.float32
    )
    grad_rows = jnp.stack([grad_q, grad_k, grad_v], axis=1).astype(jnp.bfloat16)
    grad_qkv = to_frames(grad_rows).transpose(1, 2, 0, 3).reshape(frame_count, 3 * width)
    back_normed = lax.dot_general(
        grad_qkv, w_proj[:, : 3 * width], contract_last, preferred_element_type=jnp.float32
    )
    unused_attn, pull_attn = jax.vjp(normalize, inputs, gain_attn)
    back_inputs, gain_attn_term = pull_attn(back_normed)
    grad_frames = (grad_resid + back_inputs).astype(jnp.bfloat16)[None]
    inner_part = lax.dot_general(
        normed_attn, grad_qkv, contract_first, preferred_element_type=jnp.float32
    )
    outer_part = lax.dot_general(
        grad_resid_low, attended, contract_first, preferred_element_type=jnp.float32
    )
    axes = ("dp", "tm")
    devices = lax.axis_size(axes)
    rows = inner_part.shape[0]
    small = jnp.concatenate([conv_term, gain_attn_term[None], gain_conv_term[None]], axis=0)
    small_count = small.size
    small_width = -(-small_count // rows)
    small_flat = jnp.pad(small.reshape(-1), (0, small_width * rows - small_count))
    packed = jnp.concatenate(
        [inner_part, outer_part, small_flat.reshape(rows, small_width)], axis=1
    )
    outer_count = lax.axis_size("dp")
    cores = 2
    chips = tm_count // cores
    pairs = [[cores * k + c for c in range(cores)] for k in range(chips)]
    same_core = [[cores * k + c for k in range(chips)] for c in range(cores)]
    cols = packed.shape[1]
    packed = packed.reshape(outer_count, chips, cores, rows // devices, cols)
    packed = packed.transpose(2, 0, 1, 3, 4).astype(jnp.bfloat16)
    reduced = lax.all_to_all(packed, "tm", 0, 0, tiled=True, axis_index_groups=pairs)
    reduced = reduced.astype(jnp.float32).sum(0).transpose(1, 0, 2, 3).astype(jnp.bfloat16)
    reduced = lax.all_to_all(reduced, "tm", 0, 0, tiled=True, axis_index_groups=same_core)
    reduced = reduced.astype(jnp.float32).sum(0)
    big_cols = 4 * width
    spare = reduced[:, :, big_cols:].reshape(rows // devices, -1)
    body = jnp.concatenate(
        [reduced[:, :, :big_cols], jnp.broadcast_to(spare, (outer_count,) + spare.shape)], axis=2
    )
    body = lax.all_to_all(body.astype(jnp.bfloat16), "dp", 0, 0, tiled=True)
    body = body.astype(jnp.float32).sum(0)
    grad_proj = body[:, :big_cols]
    spread = rows // devices * small_width
    small_part = body[:, big_cols:].reshape(1, -1)
    small_all = lax.all_to_all(
        jnp.broadcast_to(small_part, (tm_count, small_part.shape[1])), "tm", 0, 0, tiled=True
    )
    small_all = small_all.reshape(tm_count, outer_count, spread).transpose(1, 0, 2)
    small_sum = small_all.reshape(-1)[:small_count]
    conv_sum = small_sum[: conv_term.size].reshape(conv_term.shape)
    gains_sum = small_sum[conv_term.size :].reshape(2, -1)
    return (grad_frames, grad_proj * grad_scale, conv_sum * grad_scale, gains_sum * grad_scale)


def solution(mesh):
    return jax.shard_map(
        per_device,
        mesh=mesh,
        in_specs=(P("dp", "tm", None), P("dp", "tm", None), P("dp"), P(), P(), P(), P()),
        out_specs=(P("dp", "tm", None), P(("dp", "tm"), None), P(), P()),
        check_vma=False,
    )
```

```python
import math

import jax
import jax.numpy as jnp
from jax import lax
from jax.sharding import PartitionSpec as P

HEADS = 8
HDIM = 64
KER = 31


epsilon = 1e-05
negative = -1e30


def padded_2(value, sides, width):
    for axis, dim in sides:
        size, length = (lax.axis_size(axis), value.shape[dim])
        up = [(i, (i + 1) % size) for i in range(size - 1)]
        down = [(j, i) for i, j in up]
        last = lax.slice_in_dim(value, length - width, length, axis=dim)
        first = lax.slice_in_dim(value, 0, width, axis=dim)
        before = lax.ppermute(last, axis, up)
        after = lax.ppermute(first, axis, down)
        value = jnp.concatenate([before, value, after], axis=dim)
    return value


def normalize(inputs, gain):
    centre = inputs - jnp.mean(inputs, axis=-1, keepdims=True)
    spread = jnp.mean(centre * centre, axis=-1, keepdims=True)
    return centre * lax.rsqrt(spread + epsilon) * gain


def split_heads(matrix):
    return matrix.reshape(matrix.shape[0], HEADS, HDIM)


def over_blocks(advance, carried, members):
    total_rows = members[0].shape[0]
    stride = math.gcd(total_rows, 1024)

    def one_block(block_index, inner_state):
        offset = block_index * stride
        sliced = tuple((lax.dynamic_slice_in_dim(member, offset, stride, 0) for member in members))
        return advance(inner_state, sliced, offset)

    return lax.fori_loop(0, total_rows // stride, one_block, carried)


def forward_step(query_heads, length, scaling):

    def advance(carried, sliced, first_row):
        key_heads = split_heads(sliced[0])
        value_heads = split_heads(sliced[1])
        positions = first_row + jnp.arange(key_heads.shape[0], dtype=jnp.int32)
        living = (positions < length)[None, None, :]
        scores = (
            jnp.einsum("bhd,lhd->hbl", query_heads, key_heads, preferred_element_type=jnp.float32)
            * scaling
        )
        scores = jnp.where(living, scores, negative)
        top_old, total_old, accumulated = carried
        top_new = jnp.maximum(top_old, jnp.max(scores, axis=-1))
        weights = jnp.where(living, jnp.exp(scores - top_new[:, :, None]), 0.0)
        fading = jnp.exp(top_old - top_new)
        total_new = total_old * fading + jnp.sum(weights, axis=-1)
        update = jnp.einsum(
            "hbl,lhd->bhd",
            weights.astype(jnp.bfloat16),
            value_heads,
            preferred_element_type=jnp.float32,
        )
        return (top_new, total_new, accumulated * fading.T[:, :, None] + update)

    return advance


def query_side(query_heads, grad_heads, logsum, delta, length, scaling):

    def advance(carried, sliced, first_row):
        key_heads = split_heads(sliced[0])
        value_heads = split_heads(sliced[1])
        count_here = key_heads.shape[0]
        positions = first_row + jnp.arange(count_here, dtype=jnp.int32)
        living = (positions < length)[None, None, :]
        scores = (
            jnp.einsum("bhd,lhd->hbl", query_heads, key_heads, preferred_element_type=jnp.float32)
            * scaling
        )
        scores = jnp.where(living, scores, negative)
        probs = jnp.where(living, jnp.exp(scores - logsum.T[:, :, None]), 0.0)
        dprobs = jnp.einsum(
            "bhd,lhd->hbl", grad_heads, value_heads, preferred_element_type=jnp.float32
        )
        grad_scores = (probs * (dprobs - delta.T[:, :, None])).astype(jnp.bfloat16)
        grad_query = (
            carried[0]
            + jnp.einsum("hbl,lhd->bhd", grad_scores, key_heads, preferred_element_type=jnp.float32)
            * scaling
        )
        return (grad_query,)

    return advance


def key_side(key_heads, value_heads, own_living, scaling):

    def advance(carried, sliced, first_row):
        query_heads = split_heads(sliced[0].astype(jnp.bfloat16))
        grad_heads = split_heads(sliced[1].astype(jnp.bfloat16))
        logsum_block = sliced[2]
        delta_block = sliced[3]
        scores = (
            jnp.einsum("bhd,lhd->hbl", query_heads, key_heads, preferred_element_type=jnp.float32)
            * scaling
        )
        scores = jnp.where(own_living, scores, negative)
        probs = jnp.where(own_living, jnp.exp(scores - logsum_block.T[:, :, None]), 0.0)
        dprobs = jnp.einsum(
            "bhd,lhd->hbl", grad_heads, value_heads, preferred_element_type=jnp.float32
        )
        grad_scores = (probs * (dprobs - delta_block.T[:, :, None])).astype(jnp.bfloat16)
        grad_key = (
            carried[0]
            + jnp.einsum(
                "hbl,bhd->lhd", grad_scores, query_heads, preferred_element_type=jnp.float32
            )
            * scaling
        )
        grad_value = carried[1] + jnp.einsum(
            "hbl,bhd->lhd",
            probs.astype(jnp.bfloat16),
            grad_heads,
            preferred_element_type=jnp.float32,
        )
        return (grad_key, grad_value)

    return advance


def per_device(frames, cotangent, lengths, w_proj, gain_attn, gain_conv, w_conv):
    frame_count = frames.shape[1]
    width = HEADS * HDIM
    cycle_size = lax.axis_size("tm")
    own_start = lax.axis_index("tm") * frame_count
    length = lengths[0]
    scaling = 1.0 / math.sqrt(HDIM)
    total_frames = lax.axis_size("dp") * frames.shape[0] * frame_count * cycle_size
    grad_scale = 1.0 / math.sqrt(total_frames)
    contract_last = (((1,), (1,)), ((), ()))
    contract_first = (((0,), (0,)), ((), ()))
    inputs = frames[0].astype(jnp.float32)
    normed_attn = normalize(inputs, gain_attn).astype(jnp.bfloat16)
    projected = jnp.dot(
        normed_attn, w_proj[:, : 3 * width], preferred_element_type=jnp.float32
    ).astype(jnp.bfloat16)
    tm_count = lax.axis_size("tm")
    halves = tm_count // HEADS
    me = lax.axis_index("tm")
    half = me // HEADS
    span = frame_count * HEADS
    total = frame_count * tm_count
    key_live = (jnp.arange(total, dtype=jnp.int32) < length)[None, :]
    half_live = lax.dynamic_slice_in_dim(key_live, half * span, span, 1)
    qkv = projected.reshape(frame_count, 3, HEADS, HDIM).transpose(2, 0, 1, 3)
    got = lax.all_to_all(jnp.tile(qkv, (halves, 1, 1, 1)), "tm", 0, 0, tiled=True)
    got = got.reshape(total, 3, HDIM)
    q_all, k_all, v_all = got[:, 0], got[:, 1], got[:, 2]
    q_half = lax.dynamic_slice_in_dim(q_all, half * span, span, 0)
    scores = lax.dot_general(q_half, k_all, contract_last, preferred_element_type=jnp.float32)
    scores = jnp.where(key_live, scores * scaling, negative)
    top = jnp.max(scores, axis=-1)
    weights = jnp.where(key_live, jnp.exp(scores - top[:, None]), 0.0)
    summed = jnp.sum(weights, axis=-1)
    acc = jnp.dot(weights.astype(jnp.bfloat16), v_all, preferred_element_type=jnp.float32)
    a_half = (acc / summed[:, None]).astype(jnp.bfloat16)
    lse_half = top + jnp.log(summed)

    half_groups = [[part * HEADS + k for k in range(HEADS)] for part in range(halves)]

    def to_frames(rows):
        blocks = rows.reshape((HEADS, frame_count) + rows.shape[1:])
        return lax.all_to_all(blocks, "tm", 0, 0, tiled=True, axis_index_groups=half_groups)

    attended = to_frames(a_half).transpose(1, 0, 2).reshape(frame_count, width)
    w_out = w_proj[:, 3 * width :]
    mixed = inputs + lax.dot_general(
        attended, w_out, contract_last, preferred_element_type=jnp.float32
    )
    resid_f = mixed.astype(jnp.bfloat16).astype(jnp.float32)
    positions = own_start + jnp.arange(frame_count, dtype=jnp.int32)
    valid = (positions < length)[:, None]
    normed_conv = jnp.where(valid, normalize(resid_f, gain_conv), 0.0).astype(jnp.bfloat16)
    reach = KER // 2
    padded = padded_2(normed_conv, (("tm", 0),), reach).astype(jnp.float32)
    kernel = w_conv.astype(jnp.float32)
    conv = jnp.zeros((frame_count, padded.shape[1]), jnp.float32)
    for shift_index in range(KER):
        conv = conv + kernel[shift_index] * padded[shift_index : shift_index + frame_count]
    upstream = cotangent[0].astype(jnp.float32)
    gate = jax.nn.sigmoid(conv)
    grad_conv_in = upstream * gate * (1.0 + conv * (1.0 - gate))
    conv_term = jnp.stack(
        [
            jnp.sum(grad_conv_in * padded[shift_index : shift_index + frame_count], axis=0)
            for shift_index in range(KER)
        ]
    )
    grad_padded = padded_2(grad_conv_in.astype(jnp.bfloat16), (("tm", 0),), reach).astype(
        grad_conv_in.dtype
    )
    grad_normed = jnp.zeros_like(grad_conv_in)
    for shift_index in range(KER):
        begin = 2 * reach - shift_index
        grad_normed = grad_normed + kernel[shift_index] * grad_padded[begin : begin + frame_count]
    grad_normed = jnp.where(valid, grad_normed, 0.0)
    unused_conv, pull_conv = jax.vjp(normalize, resid_f, gain_conv)
    back_resid, gain_conv_term = pull_conv(grad_normed)
    grad_resid = upstream + back_resid
    grad_resid_low = grad_resid.astype(jnp.bfloat16)
    grad_attended = jnp.dot(grad_resid_low, w_out, preferred_element_type=jnp.float32).astype(
        jnp.bfloat16
    )
    send_grad = grad_attended.reshape(frame_count, HEADS, HDIM).transpose(1, 0, 2)
    da_all = lax.all_to_all(jnp.tile(send_grad, (halves, 1, 1)), "tm", 0, 0, tiled=True)
    da_all = da_all.reshape(total, HDIM)
    da_half = lax.dynamic_slice_in_dim(da_all, half * span, span, 0)
    delta_half = jnp.sum(da_half.astype(jnp.float32) * a_half.astype(jnp.float32), axis=-1)
    stats_half = jnp.stack([lse_half, delta_half], axis=0)
    partner = lax.ppermute(
        stats_half, "tm", [(i, (i + HEADS) % tm_count) for i in range(tm_count)]
    )
    stats_all = jnp.where(
        half == 0,
        jnp.concatenate([stats_half, partner], axis=1),
        jnp.concatenate([partner, stats_half], axis=1),
    )
    lse_all = stats_all[0][:, None]
    delta_all = stats_all[1][:, None]
    scores = lax.dot_general(q_half, k_all, contract_last, preferred_element_type=jnp.float32)
    scores = jnp.where(key_live, scores * scaling, negative)
    probs = jnp.where(key_live, jnp.exp(scores - lse_half[:, None]), 0.0)
    dprobs = lax.dot_general(da_half, v_all, contract_last, preferred_element_type=jnp.float32)
    grad_scores = (probs * (dprobs - delta_half[:, None])).astype(jnp.bfloat16)
    grad_q = jnp.dot(grad_scores, k_all, preferred_element_type=jnp.float32) * scaling
    k_half = lax.dynamic_slice_in_dim(k_all, half * span, span, 0)
    v_half = lax.dynamic_slice_in_dim(v_all, half * span, span, 0)
    scores = lax.dot_general(q_all, k_half, contract_last, preferred_element_type=jnp.float32)
    scores = jnp.where(half_live, scores * scaling, negative)
    probs = jnp.where(half_live, jnp.exp(scores - lse_all), 0.0)
    dprobs = lax.dot_general(da_all, v_half, contract_last, preferred_element_type=jnp.float32)
    grad_scores = (probs * (dprobs - delta_all)).astype(jnp.bfloat16)
    grad_k = (
        lax.dot_general(grad_scores, q_all, contract_first, preferred_element_type=jnp.float32)
        * scaling
    )
    grad_v = lax.dot_general(
        probs.astype(jnp.bfloat16), da_all, contract_first, preferred_element_type=jnp.float32
    )
    grad_rows = jnp.stack([grad_q, grad_k, grad_v], axis=1).astype(jnp.bfloat16)
    grad_qkv = to_frames(grad_rows).transpose(1, 2, 0, 3).reshape(frame_count, 3 * width)
    back_normed = lax.dot_general(
        grad_qkv, w_proj[:, : 3 * width], contract_last, preferred_element_type=jnp.float32
    )
    unused_attn, pull_attn = jax.vjp(normalize, inputs, gain_attn)
    back_inputs, gain_attn_term = pull_attn(back_normed)
    grad_frames = (grad_resid + back_inputs).astype(jnp.bfloat16)[None]
    order = (lax.axis_size("dp"), tm_count // 2, 2, normed_attn.shape[1] // (2 * tm_count * lax.axis_size("dp")))

    def by_core(matrix):
        lead = matrix.shape[:-1]
        moved = matrix.reshape(lead + order + (-1,))
        base = len(lead)
        axes_order = tuple(range(base)) + (base + 2, base, base + 1, base + 3, base + 4)
        return moved.transpose(axes_order).reshape(matrix.shape)

    inner_part = lax.dot_general(
        by_core(normed_attn), grad_qkv, contract_first, preferred_element_type=jnp.float32
    )
    outer_part = lax.dot_general(
        by_core(grad_resid_low), attended, contract_first, preferred_element_type=jnp.float32
    )
    axes = ("dp", "tm")
    devices = lax.axis_size(axes)
    rows = inner_part.shape[0]
    small = jnp.concatenate([conv_term, gain_attn_term[None], gain_conv_term[None]], axis=0)
    small_count = small.size
    small_width = -(-small_count // rows)
    small_flat = jnp.pad(small.reshape(-1), (0, small_width * rows - small_count))
    packed = jnp.concatenate(
        [inner_part, outer_part, by_core(small_flat.reshape(rows, small_width).T).T], axis=1
    )
    outer_count = lax.axis_size("dp")
    cores = 2
    chips = tm_count // cores
    pairs = [[cores * k + c for c in range(cores)] for k in range(chips)]
    same_core = [[cores * k + c for k in range(chips)] for c in range(cores)]
    cols = packed.shape[1]
    packed = packed.reshape(cores, outer_count, chips, rows // devices, cols).astype(jnp.bfloat16)
    reduced = lax.all_to_all(packed, "tm", 0, 0, tiled=True, axis_index_groups=pairs)
    reduced = reduced.astype(jnp.float32).sum(0).transpose(1, 0, 2, 3).astype(jnp.bfloat16)
    reduced = lax.all_to_all(reduced, "tm", 0, 0, tiled=True, axis_index_groups=same_core)
    reduced = reduced.astype(jnp.float32).sum(0)
    big_cols = 4 * width
    spare = reduced[:, :, big_cols:].reshape(rows // devices, -1)
    body = jnp.concatenate(
        [reduced[:, :, :big_cols], jnp.broadcast_to(spare, (outer_count,) + spare.shape)], axis=2
    )
    body = lax.all_to_all(body.astype(jnp.bfloat16), "dp", 0, 0, tiled=True)
    body = body.astype(jnp.float32).sum(0)
    grad_proj = body[:, :big_cols]
    spread = rows // devices * small_width
    small_part = body[:, big_cols:].reshape(1, -1)
    small_all = lax.all_to_all(
        jnp.broadcast_to(small_part, (tm_count, small_part.shape[1])), "tm", 0, 0, tiled=True
    )
    small_all = small_all.reshape(tm_count, outer_count, spread).transpose(1, 0, 2)
    small_sum = small_all.reshape(-1)[:small_count]
    conv_sum = small_sum[: conv_term.size].reshape(conv_term.shape)
    gains_sum = small_sum[conv_term.size :].reshape(2, -1)
    return (grad_frames, grad_proj * grad_scale, conv_sum * grad_scale, gains_sum * grad_scale)


def solution(mesh):
    return jax.shard_map(
        per_device,
        mesh=mesh,
        in_specs=(P("dp", "tm", None), P("dp", "tm", None), P("dp"), P(), P(), P(), P()),
        out_specs=(P("dp", "tm", None), P(("dp", "tm"), None), P(), P()),
        check_vma=False,
    )
```
